32 devices in a mesh: chan: 16 (over z, y, core), tm: 2 (over x).
Axes of the slice: x: 2, y: 2, z: 4, core: 2. Of those that a mesh axis runs over, the one named last changes fastest.
Arguments:
- record: bfloat16 [2, 256, 1536], P('tm', 'chan'), may hold values from -6 to 6
- pairs: int32 [32, 256], P('chan'), may hold values from 0 to 255, as said below
- stretch_index: int32 [4, 1024], replicated, may hold values from 0 to 1023, as said below
Outputs:
- coherence: float32 [2, 4, 32, 256], P('tm', None, 'chan')
The draws below stay inside these ranges and needn't reach their ends.
Inputs may be any that keep to these rules, and one draw needn't show every extreme that they name: `pairs`: row j lists the receivers of the virtual source at channel 8 j. With channel blocks of 16 channels, B = 16 of them, and b the block of channel 8 j: the first 128 receivers lie in blocks b - 1 to b + 1, and the others, across the fold of the fibre, in blocks B - 2 - b to B - b. `stretch_index`: row s is a stretch of the lag axis about lag index 512, rounded down and clipped to the lag range; row 0 reads every lag itself.
All inputs are finite; a program needn't handle non-finite values.
Results may differ from the reference program's by a relative error of at most 0.00074.
Values may be sent and summed in bfloat16 or wider, within the bound.
No kernel may reach another device: no remote copies, remote signals or barrier semaphores. Data moves between devices by JAX's collectives and lax.ppermute only.
A program may use at most 64 MiB of HBM per device.

```python
import math
import jax
import jax.numpy as jnp
from jax import lax

C_DEV = 16
NT = 1536
LAGS = 1024
RECV = 256
NSTRETCH = 4
NF = 768
CHANNELS = 256
SOURCES = 32
MINUTES = 2


def draw_pairs(key, part):
    blocks = CHANNELS // C_DEV
    source_block = jnp.arange(SOURCES, dtype=jnp.int32) * 8 // C_DEV
    near_low = jnp.maximum(source_block - 1, 0) * C_DEV
    near_high = jnp.minimum(source_block + 2, blocks) * C_DEV
    far_low = jnp.maximum(blocks - 2 - source_block, 0) * C_DEV
    far_high = jnp.minimum(blocks + 1 - source_block, blocks) * C_DEV
    near_key, far_key = jax.random.split(jax.random.fold_in(key, 11))
    half_recv = RECV // 2
    near_draw = jax.random.randint(near_key, (SOURCES, half_recv), 0, 1 << 30)
    far_draw = jax.random.randint(far_key, (SOURCES, RECV - half_recv), 0, 1 << 30)
    near_ids = near_low[:, None] + near_draw % (near_high - near_low)[:, None]
    far_ids = far_low[:, None] + far_draw % (far_high - far_low)[:, None]
    listed = jnp.concatenate([near_ids, far_ids], axis=1).astype(jnp.int32)
    listed = listed.at[0, 0].set(0)
    listed = listed.at[0, half_recv].set(CHANNELS - 1)
    return listed


def draw_stretch_index(key, part):
    size_key, sign_key = jax.random.split(jax.random.fold_in(key, 23))
    magnitude = jax.random.randint(size_key, (NSTRETCH,), LAGS // 8, LAGS // 4 + 1)
    sign_bit = jax.random.randint(sign_key, (NSTRETCH,), 0, 2)
    stretch_step = magnitude * (2 * sign_bit - 1)
    stretch_step = stretch_step.at[0].set(0)
    lag_offset = jnp.arange(LAGS, dtype=jnp.int32) - LAGS // 2
    stretched = LAGS // 2 + lag_offset[None, :] * (LAGS + stretch_step[:, None]) // LAGS
    return jnp.clip(stretched, 0, LAGS - 1).astype(jnp.int32)


def block_scale(stream_key, shape, cuts, low, high):
    def one(axis_at, blocks):
        heights = jax.random.uniform(jax.random.fold_in(jax.random.fold_in(stream_key, 6), axis_at), (blocks,), jnp.float32, low / len(cuts), high / len(cuts))
        return jnp.repeat(jnp.exp(heights), shape[axis_at] // blocks).reshape((-1,) + (1,) * (len(shape) - axis_at - 1))

    loudness = one(*cuts[0])
    for cut in cuts[1:]:
        loudness = loudness * one(*cut)
    return loudness


def normal_values(own_key, extent, deviation, reach, cuts=(), held_as=jnp.bfloat16):
    factor_of = block_scale(own_key, extent, cuts, -0.22, 0.18) if cuts else 1.0
    entries = jax.random.normal(own_key, extent, jnp.float32) * deviation * factor_of
    return jnp.minimum(jnp.maximum(entries, -reach), reach).astype(held_as)


def setup_inputs(seed: int = 0) -> dict:
    arg_keys = jax.random.split(jax.random.key(seed), 4)
    record = normal_values(arg_keys[0], (MINUTES, CHANNELS, NT), 1.0, 6.0, ((0, 2), (1, 16)))
    pairs = draw_pairs(jax.random.fold_in(arg_keys[3], 71), 0)
    stretch_index = draw_stretch_index(jax.random.fold_in(arg_keys[3], 71), 0)
    return {"record": record, "pairs": pairs, "stretch_index": stretch_index}


epsilon = 1e-05

def forward_table(first_bin, bin_count):
    sample_index = jnp.arange(NT, dtype=jnp.int32)[:, None]
    bin_index = (first_bin + jnp.arange(bin_count, dtype=jnp.int32))[None, :]
    phase_angle = (sample_index * bin_index % NT).astype(jnp.float32) * (2.0 * math.pi / NT)
    return jnp.concatenate([jnp.cos(phase_angle), -jnp.sin(phase_angle)], axis=1).astype(jnp.bfloat16)

def inverse_table():
    bin_index = jnp.arange(NF, dtype=jnp.int32)[:, None]
    lag_offset = jnp.arange(LAGS, dtype=jnp.int32)[None, :] - LAGS // 2
    phase_angle = (bin_index * lag_offset % NT).astype(jnp.float32) * (2.0 * math.pi / NT)
    bin_weight = jnp.where(bin_index == 0, 1.0, 2.0).astype(jnp.float32)
    return jnp.concatenate([bin_weight * jnp.cos(phase_angle), -bin_weight * jnp.sin(phase_angle)], axis=0).astype(jnp.bfloat16)

def whiten(spectrum):
    power = lax.optimization_barrier(jnp.mean(spectrum * spectrum, axis=-1, keepdims=True))
    return (spectrum / jnp.sqrt(power + epsilon)).astype(jnp.bfloat16)

def cross_spectrum(source_row, receivers):
    half_width = receivers.shape[-1] // 2
    source_vals = source_row.astype(jnp.float32)
    receiver_vals = receivers.astype(jnp.float32)
    src_re = source_vals[..., :half_width]
    src_im = source_vals[..., half_width:]
    rec_re = receiver_vals[..., :half_width]
    rec_im = receiver_vals[..., half_width:]
    real_part = src_re * rec_re + src_im * rec_im
    imag_part = src_re * rec_im - src_im * rec_re
    return jnp.concatenate([real_part, imag_part], axis=-1).astype(jnp.bfloat16)

def curves(current, stacked, stretch_index):
    current_power = lax.optimization_barrier(jnp.mean(current * current, axis=-1))
    columns = []
    for stretch in range(stretch_index.shape[0]):
        shifted = jnp.take(stacked, stretch_index[stretch], axis=1, mode='clip')
        numerator = lax.optimization_barrier(jnp.mean(current * shifted[None], axis=-1))
        shifted_power = lax.optimization_barrier(jnp.mean(shifted * shifted, axis=-1))[None]
        columns.append(numerator / jnp.sqrt((current_power + epsilon) * (shifted_power + epsilon)))
    return jnp.stack(columns, axis=1)

def reference(record, pairs, stretch_index):
    forward = forward_table(0, NF).astype(jnp.float32)
    spectrum = jnp.dot(record.reshape(-1, NT).astype(jnp.float32), forward, precision=lax.Precision.HIGHEST)
    whitened = whiten(spectrum).reshape(MINUTES, CHANNELS, 2 * NF)
    inverse = inverse_table().astype(jnp.float32)

    def per_source(inputs):
        source_id, receiver_ids = inputs
        source_rows = whitened[:, source_id * 8]
        receivers = jnp.take(whitened, receiver_ids, axis=1)
        crossed = cross_spectrum(source_rows[:, None, :], receivers)
        correlation = jnp.dot(crossed.reshape(-1, 2 * NF).astype(jnp.float32), inverse, precision=lax.Precision.HIGHEST)
        correlation = correlation.reshape(MINUTES, RECV, LAGS)
        stacked = lax.optimization_barrier(jnp.sum(correlation, axis=0))
        return curves(correlation, stacked, stretch_index)
    source_ids = jnp.arange(SOURCES, dtype=jnp.int32)
    results = lax.map(per_source, (source_ids, pairs))
    return jnp.transpose(results, (1, 2, 0, 3))
```

```python
import math

import jax
import jax.numpy as jnp
from jax import lax
from jax.sharding import PartitionSpec as P

NT = 1536
LAGS = 1024
NF = 768

epsilon = 1e-05


def unit_angles(numerators, period):
    phase = (numerators % period).astype(jnp.float32) * (2.0 * math.pi / period)
    return jnp.cos(phase), jnp.sin(phase)


def forward_table():
    coarse = NT // 64
    bins = jnp.arange(NF, dtype=jnp.int32)[None, :]
    cos_a, sin_a = unit_angles(jnp.arange(coarse, dtype=jnp.int32)[:, None] * bins, coarse)
    cos_c, sin_c = unit_angles(jnp.arange(64, dtype=jnp.int32)[:, None] * bins, NT)
    cos_t = cos_a[:, None, :] * cos_c[None] - sin_a[:, None, :] * sin_c[None]
    sin_t = sin_a[:, None, :] * cos_c[None] + cos_a[:, None, :] * sin_c[None]
    table = jnp.concatenate([cos_t, -sin_t], axis=-1).astype(jnp.bfloat16)
    return table.reshape(NT, 2 * NF)


def inverse_table():
    coarse = NT // 64
    groups = LAGS // 64
    bins = jnp.arange(NF, dtype=jnp.int32)[:, None]
    cos_a, sin_a = unit_angles(bins * (jnp.arange(groups, dtype=jnp.int32)[None, :] - groups // 2), coarse)
    cos_c, sin_c = unit_angles(bins * jnp.arange(64, dtype=jnp.int32)[None, :], NT)
    cos_t = cos_a[:, :, None] * cos_c[:, None, :] - sin_a[:, :, None] * sin_c[:, None, :]
    sin_t = sin_a[:, :, None] * cos_c[:, None, :] + cos_a[:, :, None] * sin_c[:, None, :]
    weight = jnp.where(bins == 0, 1.0, 2.0).astype(jnp.float32)[:, :, None]
    table = jnp.concatenate([weight * cos_t, -weight * sin_t], axis=0).astype(jnp.bfloat16)
    return table.reshape(2 * NF, LAGS)


def whiten(spectrum):
    power = jnp.mean(spectrum * spectrum, axis=-1, keepdims=True)
    return (spectrum / jnp.sqrt(power + epsilon)).astype(jnp.bfloat16)


def cross_spectrum(source_row, receivers):
    half_width = receivers.shape[-1] // 2
    source_vals = source_row.astype(jnp.float32)
    receiver_vals = receivers.astype(jnp.float32)
    src_re = source_vals[..., :half_width]
    src_im = source_vals[..., half_width:]
    rec_re = receiver_vals[..., :half_width]
    rec_im = receiver_vals[..., half_width:]
    real_part = src_re * rec_re + src_im * rec_im
    imag_part = src_re * rec_im - src_im * rec_re
    return jnp.concatenate([real_part, imag_part], axis=-1).astype(jnp.bfloat16)


def body(record, pairs, stretch_index):
    block_rows = record.shape[1]
    minutes = lax.axis_size("tm")
    blocks = lax.axis_size("chan")
    parts = [record]
    for shift in range(1, minutes):
        parts.append(
            lax.ppermute(record, "tm", [(i, (i + shift) % minutes) for i in range(minutes)])
        )
    own_block = jnp.concatenate(parts, axis=0)
    below = lax.ppermute(own_block, "chan", [(s, s + 1) for s in range(blocks - 1)])
    above = lax.ppermute(own_block, "chan", [(s, s - 1) for s in range(1, blocks)])
    far_low = lax.ppermute(own_block, "chan", [(s, blocks - 2 - s) for s in range(blocks - 1)])
    far_mid = lax.ppermute(own_block, "chan", [(s, blocks - 1 - s) for s in range(blocks)])
    far_high = lax.ppermute(own_block, "chan", [(s, blocks - s) for s in range(1, blocks)])
    candidates = jnp.concatenate([below, own_block, above, far_low, far_mid, far_high], axis=1)
    slot_rows = candidates.shape[1]
    spectrum = jnp.dot(
        candidates.reshape(minutes * slot_rows, NT), forward_table(),
        preferred_element_type=jnp.float32,
    )
    whitened = whiten(spectrum).reshape(minutes, slot_rows, 2 * NF)

    position = lax.axis_index("chan")
    column_index = jnp.arange(pairs.shape[1], dtype=jnp.int32)[None, :]
    is_near = column_index < pairs.shape[1] // 2
    near_slot = pairs - (position - 1) * block_rows
    far_slot = pairs - (blocks - 2 - position) * block_rows + 3 * block_rows
    slot_index = jnp.where(is_near, near_slot, far_slot)
    source_count, recv_count = slot_index.shape
    sources = whitened[:, block_rows:2 * block_rows:8]
    receivers = jnp.take(whitened, slot_index.reshape(-1), axis=1, mode="clip")
    receivers = receivers.reshape(minutes, source_count, recv_count, 2 * NF)
    crossed = cross_spectrum(sources[:, :, None, :], receivers)
    pair_count = source_count * recv_count
    crossed = crossed.reshape(minutes, pair_count, 2 * NF)
    correlation = jnp.einsum(
        "mpk,kl->mlp", crossed, inverse_table(), preferred_element_type=jnp.float32
    )
    current = correlation[0]
    stacked = jnp.sum(correlation, axis=0)
    current_power = jnp.mean(current * current, axis=0)
    stretch_count = stretch_index.shape[0]
    shifted = jnp.take(stacked, stretch_index.reshape(-1), axis=0, mode="clip")
    shifted = shifted.reshape(stretch_count, LAGS, pair_count)
    numerator = jnp.mean(current[None] * shifted, axis=1)
    shifted_power = jnp.mean(shifted * shifted, axis=1)
    result = numerator / jnp.sqrt((current_power[None] + epsilon) * (shifted_power + epsilon))
    return result.reshape(1, stretch_count, source_count, recv_count)


def solution(mesh):
    return jax.shard_map(
        body,
        mesh=mesh,
        in_specs=(P("tm", "chan", None), P("chan", None), P()),
        out_specs=P("tm", None, "chan", None),
        check_vma=False,
    )
```

```python
import math

import jax
import jax.numpy as jnp
from jax import lax
from jax.sharding import PartitionSpec as P

NT = 1536
LAGS = 1024
NF = 768

epsilon = 1e-05


def unit_angles(numerators, period):
    phase = (numerators % period).astype(jnp.float32) * (2.0 * math.pi / period)
    return jnp.cos(phase), jnp.sin(phase)


def forward_table():
    coarse = NT // 64
    bins = jnp.arange(NF, dtype=jnp.int32)[None, :]
    cos_a, sin_a = unit_angles(jnp.arange(coarse, dtype=jnp.int32)[:, None] * bins, coarse)
    cos_c, sin_c = unit_angles(jnp.arange(64, dtype=jnp.int32)[:, None] * bins, NT)
    cos_t = cos_a[:, None, :] * cos_c[None] - sin_a[:, None, :] * sin_c[None]
    sin_t = sin_a[:, None, :] * cos_c[None] + cos_a[:, None, :] * sin_c[None]
    table = jnp.concatenate([cos_t, -sin_t], axis=-1).astype(jnp.bfloat16)
    return table.reshape(NT, 2 * NF)


def inverse_table():
    coarse = NT // 64
    groups = LAGS // 64
    bins = jnp.arange(NF, dtype=jnp.int32)[:, None]
    cos_a, sin_a = unit_angles(bins * (jnp.arange(groups, dtype=jnp.int32)[None, :] - groups // 2), coarse)
    cos_c, sin_c = unit_angles(bins * jnp.arange(64, dtype=jnp.int32)[None, :], NT)
    cos_t = cos_a[:, :, None] * cos_c[:, None, :] - sin_a[:, :, None] * sin_c[:, None, :]
    sin_t = sin_a[:, :, None] * cos_c[:, None, :] + cos_a[:, :, None] * sin_c[:, None, :]
    weight = jnp.where(bins == 0, 1.0, 2.0).astype(jnp.float32)[:, :, None]
    table = jnp.concatenate([weight * cos_t, -weight * sin_t], axis=0).astype(jnp.bfloat16)
    return table.reshape(2 * NF, LAGS)


def whiten(spectrum):
    power = jnp.mean(spectrum * spectrum, axis=-1, keepdims=True)
    return (spectrum / jnp.sqrt(power + epsilon)).astype(jnp.bfloat16)


def cross_spectrum(source_row, receivers):
    half_width = receivers.shape[-1] // 2
    source_vals = source_row.astype(jnp.float32)
    receiver_vals = receivers.astype(jnp.float32)
    src_re = source_vals[..., :half_width]
    src_im = source_vals[..., half_width:]
    rec_re = receiver_vals[..., :half_width]
    rec_im = receiver_vals[..., half_width:]
    real_part = src_re * rec_re + src_im * rec_im
    imag_part = src_re * rec_im - src_im * rec_re
    return jnp.concatenate([real_part, imag_part], axis=-1).astype(jnp.bfloat16)


def body(record, pairs, stretch_index):
    block_rows = record.shape[1]
    minutes = lax.axis_size("tm")
    blocks = lax.axis_size("chan")
    parts = [record]
    for shift in range(1, minutes):
        parts.append(
            lax.ppermute(record, "tm", [(i, (i + shift) % minutes) for i in range(minutes)])
        )
    own_block = jnp.concatenate(parts, axis=0)
    below = lax.ppermute(own_block, "chan", [(s, s + 1) for s in range(blocks - 1)])
    above = lax.ppermute(own_block, "chan", [(s, s - 1) for s in range(1, blocks)])
    far_low = lax.ppermute(own_block, "chan", [(s, blocks - 2 - s) for s in range(blocks - 1)])
    far_mid = lax.ppermute(own_block, "chan", [(s, blocks - 1 - s) for s in range(blocks)])
    far_high = lax.ppermute(own_block, "chan", [(s, blocks - s) for s in range(1, blocks)])
    candidates = jnp.concatenate([below, own_block, above, far_low, far_mid, far_high], axis=1)
    slot_rows = candidates.shape[1]
    spectrum = jnp.dot(
        candidates.reshape(minutes * slot_rows, NT), forward_table(),
        preferred_element_type=jnp.float32,
    )
    whitened = whiten(spectrum).reshape(minutes, slot_rows, 2 * NF)

    position = lax.axis_index("chan")
    column_index = jnp.arange(pairs.shape[1], dtype=jnp.int32)[None, :]
    is_near = column_index < pairs.shape[1] // 2
    near_slot = pairs - (position - 1) * block_rows
    far_slot = pairs - (blocks - 2 - position) * block_rows + 3 * block_rows
    slot_index = jnp.where(is_near, near_slot, far_slot)
    source_count, recv_count = slot_index.shape
    pair_count = source_count * recv_count
    sources = whitened[:, block_rows:2 * block_rows:8]
    selector = (
        slot_index.reshape(pair_count, 1) == jnp.arange(slot_rows, dtype=jnp.int32)[None, :]
    ).astype(jnp.bfloat16)
    receivers = jnp.einsum(
        "pq,mqk->mpk", selector, whitened, preferred_element_type=jnp.float32
    )
    receivers = receivers.reshape(minutes, source_count, recv_count, 2 * NF)
    crossed = cross_spectrum(sources[:, :, None, :], receivers)
    crossed = crossed.reshape(minutes, pair_count, 2 * NF)
    correlation = jnp.einsum(
        "mpk,kl->mpl", crossed, inverse_table(), preferred_element_type=jnp.float32
    )
    current = correlation[0]
    stacked = jnp.sum(correlation, axis=0)
    current_power = jnp.mean(current * current, axis=-1)
    stretch_count = stretch_index.shape[0]
    picks = (
        jnp.arange(LAGS, dtype=jnp.int32)[:, None, None] == stretch_index[None, 1:, :]
    ).astype(jnp.bfloat16).reshape(LAGS, (stretch_count - 1) * LAGS)
    stacked_high = stacked.astype(jnp.bfloat16)
    stacked_low = (stacked - stacked_high.astype(jnp.float32)).astype(jnp.bfloat16)
    moved = jnp.dot(
        jnp.concatenate([stacked_high, stacked_low], axis=0), picks,
        preferred_element_type=jnp.float32,
    )
    moved = (moved[:pair_count] + moved[pair_count:]).reshape(pair_count, stretch_count - 1, LAGS)
    shifted = jnp.concatenate([stacked[:, None, :], moved], axis=1)
    numerator = jnp.mean(current[:, None, :] * shifted, axis=-1)
    shifted_power = jnp.mean(shifted * shifted, axis=-1)
    result = numerator / jnp.sqrt((current_power[:, None] + epsilon) * (shifted_power + epsilon))
    result = result.T
    return result.reshape(1, stretch_count, source_count, recv_count)


def solution(mesh):
    return jax.shard_map(
        body,
        mesh=mesh,
        in_specs=(P("tm", "chan", None), P("chan", None), P()),
        out_specs=P("tm", None, "chan", None),
        check_vma=False,
    )
```

```python
import functools
import math

import jax
import jax.numpy as jnp
from jax import lax
from jax.sharding import PartitionSpec as P

NT = 1536
LAGS = 1024
NF = 768

epsilon = 1e-05


def unit_angles(numerators, period):
    phase = (numerators % period).astype(jnp.float32) * (2.0 * math.pi / period)
    return jnp.cos(phase), jnp.sin(phase)


def forward_table():
    coarse = NT // 128
    bins = jnp.arange(NF, dtype=jnp.int32)[None, :]
    cos_a, sin_a = unit_angles(jnp.arange(coarse, dtype=jnp.int32)[:, None] * bins, coarse)
    cos_c, sin_c = unit_angles(jnp.arange(128, dtype=jnp.int32)[:, None] * bins, NT)
    cos_t = cos_a[:, None, :] * cos_c[None] - sin_a[:, None, :] * sin_c[None]
    sin_t = sin_a[:, None, :] * cos_c[None] + cos_a[:, None, :] * sin_c[None]
    table = jnp.concatenate([cos_t, -sin_t], axis=-1).astype(jnp.bfloat16)
    return table.reshape(NT, 2 * NF)


def inverse_table():
    coarse = NT // 128
    groups = LAGS // 128
    bins = jnp.arange(NF, dtype=jnp.int32)[:, None]
    cos_a, sin_a = unit_angles(bins * (jnp.arange(groups, dtype=jnp.int32)[None, :] - groups // 2), coarse)
    cos_c, sin_c = unit_angles(bins * jnp.arange(128, dtype=jnp.int32)[None, :], NT)
    cos_t = cos_a[:, :, None] * cos_c[:, None, :] - sin_a[:, :, None] * sin_c[:, None, :]
    sin_t = sin_a[:, :, None] * cos_c[:, None, :] + cos_a[:, :, None] * sin_c[:, None, :]
    weight = jnp.where(bins == 0, 1.0, 2.0).astype(jnp.float32)[:, :, None]
    table = jnp.concatenate([weight * cos_t, -weight * sin_t], axis=0).astype(jnp.bfloat16)
    return table.reshape(2 * NF, LAGS)


def whiten(spectrum):
    power = jnp.mean(spectrum * spectrum, axis=-1, keepdims=True)
    return (spectrum / jnp.sqrt(power + epsilon)).astype(jnp.bfloat16)


def cross_spectrum(source_row, receivers):
    half_width = receivers.shape[-1] // 2
    source_vals = source_row.astype(jnp.float32)
    receiver_vals = receivers.astype(jnp.float32)
    src_re = source_vals[..., :half_width]
    src_im = source_vals[..., half_width:]
    rec_re = receiver_vals[..., :half_width]
    rec_im = receiver_vals[..., half_width:]
    real_part = src_re * rec_re + src_im * rec_im
    imag_part = src_re * rec_im - src_im * rec_re
    return jnp.concatenate([real_part, imag_part], axis=-1).astype(jnp.bfloat16)


def body(axis_order, record, pairs, stretch_index):
    block_rows = record.shape[1]
    minutes = lax.axis_size("tm")
    blocks = lax.axis_size("chan")

    def linear(t, b):
        return t * blocks + b if axis_order[0] == "tm" else b * minutes + t

    slot_maps = (
        lambda b: b + 1,
        lambda b: b,
        lambda b: b - 1,
        lambda b: blocks - 2 - b,
        lambda b: blocks - 1 - b,
        lambda b: blocks - b,
    )
    minute_rows = []
    for shift in range(minutes):
        slots = []
        for slot, target in enumerate(slot_maps):
            if shift == 0 and slot == 1:
                slots.append(record)
                continue
            route = [
                (linear(t, b), linear((t + shift) % minutes, target(b)))
                for t in range(minutes)
                for b in range(blocks)
                if 0 <= target(b) < blocks
            ]
            slots.append(lax.ppermute(record, axis_order, route))
        minute_rows.append(jnp.concatenate(slots, axis=1))
    candidates = jnp.concatenate(minute_rows, axis=0)
    slot_rows = candidates.shape[1]
    spectrum = jnp.dot(
        candidates.reshape(minutes * slot_rows, NT), forward_table(),
        preferred_element_type=jnp.float32,
    )
    whitened = whiten(spectrum).reshape(minutes, slot_rows, 2 * NF)

    position = lax.axis_index("chan")
    column_index = jnp.arange(pairs.shape[1], dtype=jnp.int32)[None, :]
    is_near = column_index < pairs.shape[1] // 2
    near_slot = pairs - (position - 1) * block_rows
    far_slot = pairs - (blocks - 2 - position) * block_rows + 3 * block_rows
    slot_index = jnp.where(is_near, near_slot, far_slot)
    source_count, recv_count = slot_index.shape
    pair_count = source_count * recv_count
    sources = whitened[:, block_rows:2 * block_rows:8]
    selector = (
        slot_index.reshape(pair_count, 1) == jnp.arange(slot_rows, dtype=jnp.int32)[None, :]
    ).astype(jnp.bfloat16)
    receivers = jnp.einsum(
        "pq,mqk->mpk", selector, whitened, preferred_element_type=jnp.float32
    )
    receivers = receivers.reshape(minutes, source_count, recv_count, 2 * NF)
    crossed = cross_spectrum(sources[:, :, None, :], receivers)
    crossed = crossed.reshape(minutes, pair_count, 2 * NF)
    correlation = jnp.einsum(
        "mpk,kl->mpl", crossed, inverse_table(), preferred_element_type=jnp.float32
    )
    current = correlation[0]
    stacked = jnp.sum(correlation, axis=0)
    current_power = jnp.mean(current * current, axis=-1)
    stretch_count = stretch_index.shape[0]
    picks = (
        jnp.arange(LAGS, dtype=jnp.int32)[:, None, None] == stretch_index[None, 1:, :]
    ).astype(jnp.bfloat16).reshape(LAGS, (stretch_count - 1) * LAGS)
    stacked_round = lax.reduce_precision(stacked, exponent_bits=8, mantissa_bits=7)
    stacked_high = stacked_round.astype(jnp.bfloat16)
    stacked_low = (stacked - stacked_round).astype(jnp.bfloat16)
    moved = jnp.dot(
        jnp.concatenate([stacked_high, stacked_low], axis=0), picks,
        preferred_element_type=jnp.float32,
    )
    moved = (moved[:pair_count] + moved[pair_count:]).reshape(pair_count, stretch_count - 1, LAGS)
    shifted = jnp.concatenate([stacked[:, None, :], moved], axis=1)
    numerator = jnp.mean(current[:, None, :] * shifted, axis=-1)
    shifted_power = jnp.mean(shifted * shifted, axis=-1)
    result = numerator / jnp.sqrt((current_power[:, None] + epsilon) * (shifted_power + epsilon))
    result = result.T
    return result.reshape(1, stretch_count, source_count, recv_count)


def solution(mesh):
    axis_order = tuple(name for name in mesh.axis_names if name in ("tm", "chan"))
    return jax.shard_map(
        functools.partial(body, axis_order),
        mesh=mesh,
        in_specs=(P("tm", "chan", None), P("chan", None), P()),
        out_specs=P("tm", None, "chan", None),
        check_vma=False,
    )
```

```python
import functools
import math

import jax
import jax.numpy as jnp
from jax import lax
from jax.sharding import PartitionSpec as P

NT = 1536
LAGS = 1024
NF = 768

epsilon = 1e-05
GATHER_BYTES = 4 << 20


def unit_angles(numerators, period):
    phase = (numerators % period).astype(jnp.float32) * (2.0 * math.pi / period)
    return jnp.cos(phase), jnp.sin(phase)


def forward_table():
    coarse = NT // 128
    bins = jnp.arange(NF, dtype=jnp.int32)[None, :]
    cos_a, sin_a = unit_angles(jnp.arange(coarse, dtype=jnp.int32)[:, None] * bins, coarse)
    cos_c, sin_c = unit_angles(jnp.arange(128, dtype=jnp.int32)[:, None] * bins, NT)
    cos_t = cos_a[:, None, :] * cos_c[None] - sin_a[:, None, :] * sin_c[None]
    sin_t = sin_a[:, None, :] * cos_c[None] + cos_a[:, None, :] * sin_c[None]
    table = jnp.concatenate([cos_t, -sin_t], axis=-1).astype(jnp.bfloat16)
    return table.reshape(NT, 2 * NF)


def inverse_table():
    coarse = NT // 128
    groups = LAGS // 128
    bins = jnp.arange(NF, dtype=jnp.int32)[:, None]
    cos_a, sin_a = unit_angles(bins * (jnp.arange(groups, dtype=jnp.int32)[None, :] - groups // 2), coarse)
    cos_c, sin_c = unit_angles(bins * jnp.arange(128, dtype=jnp.int32)[None, :], NT)
    cos_t = cos_a[:, :, None] * cos_c[:, None, :] - sin_a[:, :, None] * sin_c[:, None, :]
    sin_t = sin_a[:, :, None] * cos_c[:, None, :] + cos_a[:, :, None] * sin_c[:, None, :]
    weight = jnp.where(bins == 0, 1.0, 2.0).astype(jnp.float32)[:, :, None]
    table = jnp.concatenate([weight * cos_t, -weight * sin_t], axis=0).astype(jnp.bfloat16)
    return table.reshape(2 * NF, LAGS)


def whiten(spectrum):
    power = jnp.mean(spectrum * spectrum, axis=-1, keepdims=True)
    return (spectrum / jnp.sqrt(power + epsilon)).astype(jnp.bfloat16)


def cross_spectrum(source_row, receivers):
    half_width = receivers.shape[-1] // 2
    source_vals = source_row.astype(jnp.float32)
    receiver_vals = receivers.astype(jnp.float32)
    src_re = source_vals[..., :half_width]
    src_im = source_vals[..., half_width:]
    rec_re = receiver_vals[..., :half_width]
    rec_im = receiver_vals[..., half_width:]
    real_part = src_re * rec_re + src_im * rec_im
    imag_part = src_re * rec_im - src_im * rec_re
    return jnp.concatenate([real_part, imag_part], axis=-1).astype(jnp.bfloat16)


def body(axis_order, record, pairs, stretch_index):
    block_rows = record.shape[1]
    minutes = lax.axis_size("tm")
    blocks = lax.axis_size("chan")


    position = lax.axis_index("chan")
    gathered_bytes = record.size * record.dtype.itemsize * minutes * blocks
    if gathered_bytes <= GATHER_BYTES:
        everything = lax.all_gather(record[0], axis_order, axis=0)
        if axis_order[0] == "tm":
            everything = everything.reshape(minutes, blocks, block_rows, NT)
        else:
            everything = everything.reshape(blocks, minutes, block_rows, NT).transpose(1, 0, 2, 3)
        everything = jnp.pad(everything, ((0, 0), (1, 1), (0, 0), (0, 0)))
        near = lax.dynamic_slice_in_dim(everything, position, 3, axis=1)
        far = lax.dynamic_slice_in_dim(everything, blocks - 1 - position, 3, axis=1)
        candidates = jnp.concatenate([near, far], axis=1).reshape(minutes, 6 * block_rows, NT)
        own_minute = lax.axis_index("tm")
    else:
        parts = [record]
        for shift in range(1, minutes):
            parts.append(
                lax.ppermute(record, "tm", [(i, (i + shift) % minutes) for i in range(minutes)])
            )
        own_block = jnp.concatenate(parts, axis=0)
        below = lax.ppermute(own_block, "chan", [(s, s + 1) for s in range(blocks - 1)])
        above = lax.ppermute(own_block, "chan", [(s, s - 1) for s in range(1, blocks)])
        far_low = lax.ppermute(own_block, "chan", [(s, blocks - 2 - s) for s in range(blocks - 1)])
        far_mid = lax.ppermute(own_block, "chan", [(s, blocks - 1 - s) for s in range(blocks)])
        far_high = lax.ppermute(own_block, "chan", [(s, blocks - s) for s in range(1, blocks)])
        candidates = jnp.concatenate([below, own_block, above, far_low, far_mid, far_high], axis=1)
        own_minute = 0
    slot_rows = candidates.shape[1]
    spectrum = jnp.dot(
        candidates.reshape(minutes * slot_rows, NT), forward_table(),
        preferred_element_type=jnp.float32,
    )
    whitened = whiten(spectrum).reshape(minutes, slot_rows, 2 * NF)

    column_index = jnp.arange(pairs.shape[1], dtype=jnp.int32)[None, :]
    is_near = column_index < pairs.shape[1] // 2
    near_slot = pairs - (position - 1) * block_rows
    far_slot = pairs - (blocks - 2 - position) * block_rows + 3 * block_rows
    slot_index = jnp.where(is_near, near_slot, far_slot)
    source_count, recv_count = slot_index.shape
    pair_count = source_count * recv_count
    sources = whitened[:, block_rows:2 * block_rows:8]
    selector = (
        slot_index.reshape(pair_count, 1) == jnp.arange(slot_rows, dtype=jnp.int32)[None, :]
    ).astype(jnp.bfloat16)
    receivers = jnp.einsum(
        "pq,mqk->mpk", selector, whitened, preferred_element_type=jnp.float32
    )
    receivers = receivers.reshape(minutes, source_count, recv_count, 2 * NF)
    crossed = cross_spectrum(sources[:, :, None, :], receivers)
    crossed = crossed.reshape(minutes, pair_count, 2 * NF)
    correlation = jnp.einsum(
        "mpk,kl->mpl", crossed, inverse_table(), preferred_element_type=jnp.float32
    )
    current = lax.dynamic_index_in_dim(correlation, own_minute, axis=0, keepdims=False)
    stacked = jnp.sum(correlation, axis=0)
    current_power = jnp.mean(current * current, axis=-1)
    stretch_count = stretch_index.shape[0]
    picks = (
        jnp.arange(LAGS, dtype=jnp.int32)[:, None, None] == stretch_index[None, 1:, :]
    ).astype(jnp.bfloat16).reshape(LAGS, (stretch_count - 1) * LAGS)
    stacked_round = lax.reduce_precision(stacked, exponent_bits=8, mantissa_bits=7)
    stacked_high = stacked_round.astype(jnp.bfloat16)
    stacked_low = (stacked - stacked_round).astype(jnp.bfloat16)
    moved = jnp.dot(
        jnp.concatenate([stacked_high, stacked_low], axis=0), picks,
        preferred_element_type=jnp.float32,
    )
    moved = (moved[:pair_count] + moved[pair_count:]).reshape(pair_count, stretch_count - 1, LAGS)
    shifted = jnp.concatenate([stacked[:, None, :], moved], axis=1)
    numerator = jnp.mean(current[:, None, :] * shifted, axis=-1)
    shifted_power = jnp.mean(shifted * shifted, axis=-1)
    result = numerator / jnp.sqrt((current_power[:, None] + epsilon) * (shifted_power + epsilon))
    result = result.T
    return result.reshape(1, stretch_count, source_count, recv_count)


def solution(mesh):
    axis_order = tuple(name for name in mesh.axis_names if name in ("tm", "chan"))
    return jax.shard_map(
        functools.partial(body, axis_order),
        mesh=mesh,
        in_specs=(P("tm", "chan", None), P("chan", None), P()),
        out_specs=P("tm", None, "chan", None),
        check_vma=False,
    )
```

```python
import math

import jax
import jax.numpy as jnp
from jax import lax
from jax.experimental import pallas as pl
from jax.experimental.pallas import tpu as pltpu
from jax.sharding import PartitionSpec as P

NT = 1536
LAGS = 1024
NF = 768

epsilon = 1e-05


def unit_angles(numerators, period):
    phase = (numerators % period).astype(jnp.float32) * (2.0 * math.pi / period)
    return jnp.cos(phase), jnp.sin(phase)


def forward_table():
    coarse = NT // 128
    bins = jnp.arange(NF, dtype=jnp.int32)[None, :]
    cos_a, sin_a = unit_angles(jnp.arange(coarse, dtype=jnp.int32)[:, None] * bins, coarse)
    cos_c, sin_c = unit_angles(jnp.arange(128, dtype=jnp.int32)[:, None] * bins, NT)
    cos_t = cos_a[:, None, :] * cos_c[None] - sin_a[:, None, :] * sin_c[None]
    sin_t = sin_a[:, None, :] * cos_c[None] + cos_a[:, None, :] * sin_c[None]
    table = jnp.concatenate([cos_t, -sin_t], axis=-1).astype(jnp.bfloat16)
    return table.reshape(NT, 2 * NF)


def inverse_table():
    coarse = NT // 128
    groups = LAGS // 128
    bins = jnp.arange(NF, dtype=jnp.int32)[:, None]
    cos_a, sin_a = unit_angles(bins * (jnp.arange(groups, dtype=jnp.int32)[None, :] - groups // 2), coarse)
    cos_c, sin_c = unit_angles(bins * jnp.arange(128, dtype=jnp.int32)[None, :], NT)
    cos_t = cos_a[:, :, None] * cos_c[:, None, :] - sin_a[:, :, None] * sin_c[:, None, :]
    sin_t = sin_a[:, :, None] * cos_c[:, None, :] + cos_a[:, :, None] * sin_c[:, None, :]
    weight = jnp.where(bins == 0, 1.0, 2.0).astype(jnp.float32)[:, :, None]
    table = jnp.concatenate([weight * cos_t, -weight * sin_t], axis=0).astype(jnp.bfloat16)
    return table.reshape(2 * NF, LAGS)


def whiten(spectrum):
    power = jnp.mean(spectrum * spectrum, axis=-1, keepdims=True)
    return (spectrum / jnp.sqrt(power + epsilon)).astype(jnp.bfloat16)


def cross_spectrum(source_row, receivers):
    half_width = receivers.shape[-1] // 2
    source_vals = source_row.astype(jnp.float32)
    receiver_vals = receivers.astype(jnp.float32)
    src_re = source_vals[..., :half_width]
    src_im = source_vals[..., half_width:]
    rec_re = receiver_vals[..., :half_width]
    rec_im = receiver_vals[..., half_width:]
    real_part = src_re * rec_re + src_im * rec_im
    imag_part = src_re * rec_im - src_im * rec_re
    return jnp.concatenate([real_part, imag_part], axis=-1).astype(jnp.bfloat16)


PAIR_BLOCK = 128


def coherence_kernel(own_ref, stretch_ref, crossed_ref, inverse_ref, out_ref, picks_ref):
    minutes = crossed_ref.shape[0]
    moves = stretch_ref.shape[0] - 1

    @pl.when(pl.program_id(0) == 0)
    def _():
        rows = lax.broadcasted_iota(jnp.int32, (LAGS, LAGS), 0)
        for move in range(moves):
            picks_ref[:, move * LAGS:(move + 1) * LAGS] = (
                rows == stretch_ref[move + 1:move + 2, :]
            ).astype(jnp.bfloat16)

    inverse = inverse_ref[...]
    own = own_ref[0]
    stacked = None
    current = None
    for minute in range(minutes):
        correlation = jnp.dot(crossed_ref[minute], inverse, preferred_element_type=jnp.float32)
        if stacked is None:
            stacked, current = correlation, correlation
        else:
            stacked = stacked + correlation
            current = jnp.where(own == minute, correlation, current)
    high = stacked.astype(jnp.bfloat16)
    low = (stacked - high.astype(jnp.float32)).astype(jnp.bfloat16)
    picks = picks_ref[...]
    moved = jnp.dot(high, picks, preferred_element_type=jnp.float32) + jnp.dot(
        low, picks, preferred_element_type=jnp.float32
    )
    scale = 1.0 / LAGS
    current_power = jnp.sum(current * current, axis=1, keepdims=True) * scale
    lanes = lax.broadcasted_iota(jnp.int32, out_ref.shape, 1)
    result = jnp.zeros(out_ref.shape, jnp.float32)
    for stretch in range(moves + 1):
        if stretch == 0:
            shifted = stacked
        else:
            shifted = moved[:, (stretch - 1) * LAGS:stretch * LAGS]
        numerator = jnp.sum(current * shifted, axis=1, keepdims=True) * scale
        shifted_power = jnp.sum(shifted * shifted, axis=1, keepdims=True) * scale
        value = numerator / jnp.sqrt((current_power + epsilon) * (shifted_power + epsilon))
        result = jnp.where(lanes == stretch, value, result)
    out_ref[...] = result


def coherence(own_minute, stretch_index, crossed, inverse):
    minutes, pair_count, width = crossed.shape
    stretch_count = stretch_index.shape[0]
    own = jnp.reshape(own_minute, (1,)).astype(jnp.int32)
    out = pl.pallas_call(
        coherence_kernel,
        grid_spec=pltpu.PrefetchScalarGridSpec(
            num_scalar_prefetch=1,
            grid=(pair_count // PAIR_BLOCK,),
            in_specs=[
                pl.BlockSpec(stretch_index.shape, lambda i, own: (0, 0)),
                pl.BlockSpec((minutes, PAIR_BLOCK, width), lambda i, own: (0, i, 0)),
                pl.BlockSpec(inverse.shape, lambda i, own: (0, 0)),
            ],
            out_specs=pl.BlockSpec((PAIR_BLOCK, 128), lambda i, own: (i, 0)),
            scratch_shapes=[pltpu.VMEM((LAGS, (stretch_count - 1) * LAGS), jnp.bfloat16)],
        ),
        out_shape=jax.ShapeDtypeStruct((pair_count, 128), jnp.float32),
        compiler_params=pltpu.CompilerParams(
            dimension_semantics=("arbitrary",), vmem_limit_bytes=48 << 20
        ),
    )(own, stretch_index, crossed, inverse)
    return out[:, :stretch_count].T


def body(record, pairs, stretch_index):
    block_rows = record.shape[1]
    minutes = lax.axis_size("tm")
    blocks = lax.axis_size("chan")
    parts = [record]
    for shift in range(1, minutes):
        parts.append(
            lax.ppermute(record, "tm", [(i, (i + shift) % minutes) for i in range(minutes)])
        )
    own_block = jnp.concatenate(parts, axis=0)
    below = lax.ppermute(own_block, "chan", [(s, s + 1) for s in range(blocks - 1)])
    above = lax.ppermute(own_block, "chan", [(s, s - 1) for s in range(1, blocks)])
    far_low = lax.ppermute(own_block, "chan", [(s, blocks - 2 - s) for s in range(blocks - 1)])
    far_mid = lax.ppermute(own_block, "chan", [(s, blocks - 1 - s) for s in range(blocks)])
    far_high = lax.ppermute(own_block, "chan", [(s, blocks - s) for s in range(1, blocks)])
    candidates = jnp.concatenate([below, own_block, above, far_low, far_mid, far_high], axis=1)
    slot_rows = candidates.shape[1]
    spectrum = jnp.dot(
        candidates.reshape(minutes * slot_rows, NT), forward_table(),
        preferred_element_type=jnp.float32,
    )
    whitened = whiten(spectrum).reshape(minutes, slot_rows, 2 * NF)

    position = lax.axis_index("chan")
    column_index = jnp.arange(pairs.shape[1], dtype=jnp.int32)[None, :]
    is_near = column_index < pairs.shape[1] // 2
    near_slot = pairs - (position - 1) * block_rows
    far_slot = pairs - (blocks - 2 - position) * block_rows + 3 * block_rows
    slot_index = jnp.where(is_near, near_slot, far_slot)
    source_count, recv_count = slot_index.shape
    pair_count = source_count * recv_count
    sources = whitened[:, block_rows:2 * block_rows:8]
    selector = (
        slot_index.reshape(pair_count, 1) == jnp.arange(slot_rows, dtype=jnp.int32)[None, :]
    ).astype(jnp.bfloat16)
    receivers = jnp.einsum(
        "pq,mqk->mpk", selector, whitened, preferred_element_type=jnp.float32
    )
    receivers = receivers.reshape(minutes, source_count, recv_count, 2 * NF)
    crossed = cross_spectrum(sources[:, :, None, :], receivers)
    crossed = crossed.reshape(minutes, pair_count, 2 * NF)
    result = coherence(0, stretch_index, crossed, inverse_table())
    stretch_count = stretch_index.shape[0]
    return result.reshape(1, stretch_count, source_count, recv_count)


def solution(mesh):
    return jax.shard_map(
        body,
        mesh=mesh,
        in_specs=(P("tm", "chan", None), P("chan", None), P()),
        out_specs=P("tm", None, "chan", None),
        check_vma=False,
    )
```

```python
import math

import jax
import jax.numpy as jnp
from jax import lax
from jax.experimental import pallas as pl
from jax.experimental.pallas import tpu as pltpu
from jax.sharding import PartitionSpec as P

NT = 1536
LAGS = 1024
NF = 768

epsilon = 1e-05


def unit_angles(numerators, period):
    phase = (numerators % period).astype(jnp.float32) * (2.0 * math.pi / period)
    return jnp.cos(phase), jnp.sin(phase)


def forward_table():
    coarse = NT // 128
    bins = jnp.arange(NF, dtype=jnp.int32)[None, :]
    cos_a, sin_a = unit_angles(jnp.arange(coarse, dtype=jnp.int32)[:, None] * bins, coarse)
    cos_c, sin_c = unit_angles(jnp.arange(128, dtype=jnp.int32)[:, None] * bins, NT)
    cos_t = cos_a[:, None, :] * cos_c[None] - sin_a[:, None, :] * sin_c[None]
    sin_t = sin_a[:, None, :] * cos_c[None] + cos_a[:, None, :] * sin_c[None]
    table = jnp.concatenate([cos_t, -sin_t], axis=-1).astype(jnp.bfloat16)
    return table.reshape(NT, 2 * NF)


def inverse_table():
    coarse = NT // 128
    groups = LAGS // 128
    bins = jnp.arange(NF, dtype=jnp.int32)[:, None]
    cos_a, sin_a = unit_angles(bins * (jnp.arange(groups, dtype=jnp.int32)[None, :] - groups // 2), coarse)
    cos_c, sin_c = unit_angles(bins * jnp.arange(128, dtype=jnp.int32)[None, :], NT)
    cos_t = cos_a[:, :, None] * cos_c[:, None, :] - sin_a[:, :, None] * sin_c[:, None, :]
    sin_t = sin_a[:, :, None] * cos_c[:, None, :] + cos_a[:, :, None] * sin_c[:, None, :]
    weight = jnp.where(bins == 0, 1.0, 2.0).astype(jnp.float32)[:, :, None]
    table = jnp.concatenate([weight * cos_t, -weight * sin_t], axis=0).astype(jnp.bfloat16)
    return table.reshape(2 * NF, LAGS)


def whiten(spectrum):
    power = jnp.mean(spectrum * spectrum, axis=-1, keepdims=True)
    return (spectrum / jnp.sqrt(power + epsilon)).astype(jnp.bfloat16)


def cross_spectrum(source_row, receivers):
    half_width = receivers.shape[-1] // 2
    source_vals = source_row.astype(jnp.float32)
    receiver_vals = receivers.astype(jnp.float32)
    src_re = source_vals[..., :half_width]
    src_im = source_vals[..., half_width:]
    rec_re = receiver_vals[..., :half_width]
    rec_im = receiver_vals[..., half_width:]
    real_part = src_re * rec_re + src_im * rec_im
    imag_part = src_re * rec_im - src_im * rec_re
    return jnp.concatenate([real_part, imag_part], axis=-1).astype(jnp.bfloat16)


PAIR_BLOCK = 128


def coherence_kernel(own_ref, stretch_ref, crossed_ref, inverse_ref, out_ref, picks_ref):
    minutes = crossed_ref.shape[0]
    moves = stretch_ref.shape[0] - 1

    @pl.when(pl.program_id(0) == 0)
    def _():
        rows = lax.broadcasted_iota(jnp.int32, (LAGS, LAGS), 0)
        for move in range(moves):
            picks_ref[:, move * LAGS:(move + 1) * LAGS] = (
                rows == stretch_ref[move + 1:move + 2, :]
            ).astype(jnp.bfloat16)

    inverse = inverse_ref[...]
    own = own_ref[0]
    stacked = None
    current = None
    for minute in range(minutes):
        correlation = jnp.dot(crossed_ref[minute], inverse, preferred_element_type=jnp.float32)
        if stacked is None:
            stacked, current = correlation, correlation
        else:
            stacked = stacked + correlation
            current = jnp.where(own == minute, correlation, current)
    high = stacked.astype(jnp.bfloat16)
    low = (stacked - high.astype(jnp.float32)).astype(jnp.bfloat16)
    picks = picks_ref[...]
    moved = jnp.dot(high, picks, preferred_element_type=jnp.float32) + jnp.dot(
        low, picks, preferred_element_type=jnp.float32
    )
    scale = 1.0 / LAGS
    current_power = jnp.sum(current * current, axis=1, keepdims=True) * scale
    lanes = lax.broadcasted_iota(jnp.int32, out_ref.shape, 1)
    result = jnp.zeros(out_ref.shape, jnp.float32)
    for stretch in range(moves + 1):
        if stretch == 0:
            shifted = stacked
        else:
            shifted = moved[:, (stretch - 1) * LAGS:stretch * LAGS]
        numerator = jnp.sum(current * shifted, axis=1, keepdims=True) * scale
        shifted_power = jnp.sum(shifted * shifted, axis=1, keepdims=True) * scale
        value = numerator / jnp.sqrt((current_power + epsilon) * (shifted_power + epsilon))
        result = jnp.where(lanes == stretch, value, result)
    out_ref[...] = result


def coherence(own_minute, stretch_index, crossed, inverse):
    minutes, pair_count, width = crossed.shape
    stretch_count = stretch_index.shape[0]
    own = jnp.reshape(own_minute, (1,)).astype(jnp.int32)
    out = pl.pallas_call(
        coherence_kernel,
        grid_spec=pltpu.PrefetchScalarGridSpec(
            num_scalar_prefetch=1,
            grid=(pair_count // PAIR_BLOCK,),
            in_specs=[
                pl.BlockSpec(stretch_index.shape, lambda i, own: (0, 0)),
                pl.BlockSpec((minutes, PAIR_BLOCK, width), lambda i, own: (0, i, 0)),
                pl.BlockSpec(inverse.shape, lambda i, own: (0, 0)),
            ],
            out_specs=pl.BlockSpec((PAIR_BLOCK, 128), lambda i, own: (i, 0)),
            scratch_shapes=[pltpu.VMEM((LAGS, (stretch_count - 1) * LAGS), jnp.bfloat16)],
        ),
        out_shape=jax.ShapeDtypeStruct((pair_count, 128), jnp.float32),
        compiler_params=pltpu.CompilerParams(
            dimension_semantics=("arbitrary",), vmem_limit_bytes=48 << 20
        ),
    )(own, stretch_index, crossed, inverse)
    return out[:, :stretch_count].T


def body(record, pairs, stretch_index):
    block_rows = record.shape[1]
    minutes = lax.axis_size("tm")
    blocks = lax.axis_size("chan")
    parts = [record]
    for shift in range(1, minutes):
        parts.append(
            lax.ppermute(record, "tm", [(i, (i + shift) % minutes) for i in range(minutes)])
        )
    own_block = jnp.concatenate(parts, axis=0)
    below = lax.ppermute(own_block, "chan", [(s, s + 1) for s in range(blocks - 1)])
    above = lax.ppermute(own_block, "chan", [(s, s - 1) for s in range(1, blocks)])
    near = jnp.concatenate([below, own_block, above], axis=1)
    far = lax.ppermute(near, "chan", [(s, blocks - 1 - s) for s in range(blocks)])
    forward = forward_table()
    inverse = inverse_table()
    slot_rows = near.shape[1]

    def spectra(rows):
        spectrum = jnp.dot(
            rows.reshape(minutes * slot_rows, NT), forward, preferred_element_type=jnp.float32
        )
        return whiten(spectrum).reshape(minutes, slot_rows, 2 * NF)

    position = lax.axis_index("chan")
    source_count, recv_count = pairs.shape
    half = recv_count // 2
    whitened_near = spectra(near)
    sources = whitened_near[:, block_rows:2 * block_rows:8]

    def half_coherence(whitened, receiver_ids, first_block):
        slot_index = (receiver_ids - first_block * block_rows).reshape(-1, 1)
        selector = (slot_index == jnp.arange(slot_rows, dtype=jnp.int32)[None, :]).astype(
            jnp.bfloat16
        )
        receivers = jnp.einsum(
            "pq,mqk->mpk", selector, whitened, preferred_element_type=jnp.float32
        )
        receivers = receivers.reshape(minutes, source_count, half, 2 * NF)
        crossed = cross_spectrum(sources[:, :, None, :], receivers)
        crossed = crossed.reshape(minutes, source_count * half, 2 * NF)
        result = coherence(0, stretch_index, crossed, inverse)
        return result.reshape(-1, source_count, half)

    near_result = half_coherence(whitened_near, pairs[:, :half], position - 1)
    far_result = half_coherence(spectra(far), pairs[:, half:], blocks - 2 - position)
    result = jnp.concatenate([near_result, far_result], axis=2)
    stretch_count = stretch_index.shape[0]
    return result.reshape(1, stretch_count, source_count, recv_count)


def solution(mesh):
    return jax.shard_map(
        body,
        mesh=mesh,
        in_specs=(P("tm", "chan", None), P("chan", None), P()),
        out_specs=P("tm", None, "chan", None),
        check_vma=False,
    )
```

```python
import functools
import math

import jax
import jax.numpy as jnp
from jax import lax
from jax.experimental import pallas as pl
from jax.experimental.pallas import tpu as pltpu
from jax.sharding import PartitionSpec as P

NT = 1536
LAGS = 1024
NF = 768

epsilon = 1e-05
EXCHANGE_BYTES = 4 << 20


def unit_angles(numerators, period):
    phase = (numerators % period).astype(jnp.float32) * (2.0 * math.pi / period)
    return jnp.cos(phase), jnp.sin(phase)


def forward_table():
    coarse = NT // 128
    bins = jnp.arange(NF, dtype=jnp.int32)[None, :]
    cos_a, sin_a = unit_angles(jnp.arange(coarse, dtype=jnp.int32)[:, None] * bins, coarse)
    cos_c, sin_c = unit_angles(jnp.arange(128, dtype=jnp.int32)[:, None] * bins, NT)
    cos_t = cos_a[:, None, :] * cos_c[None] - sin_a[:, None, :] * sin_c[None]
    sin_t = sin_a[:, None, :] * cos_c[None] + cos_a[:, None, :] * sin_c[None]
    table = jnp.concatenate([cos_t, -sin_t], axis=-1).astype(jnp.bfloat16)
    return table.reshape(NT, 2 * NF)


def inverse_table():
    coarse = NT // 128
    groups = LAGS // 128
    bins = jnp.arange(NF, dtype=jnp.int32)[:, None]
    cos_a, sin_a = unit_angles(bins * (jnp.arange(groups, dtype=jnp.int32)[None, :] - groups // 2), coarse)
    cos_c, sin_c = unit_angles(bins * jnp.arange(128, dtype=jnp.int32)[None, :], NT)
    cos_t = cos_a[:, :, None] * cos_c[:, None, :] - sin_a[:, :, None] * sin_c[:, None, :]
    sin_t = sin_a[:, :, None] * cos_c[:, None, :] + cos_a[:, :, None] * sin_c[:, None, :]
    weight = jnp.where(bins == 0, 1.0, 2.0).astype(jnp.float32)[:, :, None]
    table = jnp.concatenate([weight * cos_t, -weight * sin_t], axis=0).astype(jnp.bfloat16)
    return table.reshape(2 * NF, LAGS)


def whiten(spectrum):
    power = jnp.mean(spectrum * spectrum, axis=-1, keepdims=True)
    return (spectrum / jnp.sqrt(power + epsilon)).astype(jnp.bfloat16)


def cross_spectrum(source_row, receivers):
    half_width = receivers.shape[-1] // 2
    source_vals = source_row.astype(jnp.float32)
    receiver_vals = receivers.astype(jnp.float32)
    src_re = source_vals[..., :half_width]
    src_im = source_vals[..., half_width:]
    rec_re = receiver_vals[..., :half_width]
    rec_im = receiver_vals[..., half_width:]
    real_part = src_re * rec_re + src_im * rec_im
    imag_part = src_re * rec_im - src_im * rec_re
    return jnp.concatenate([real_part, imag_part], axis=-1).astype(jnp.bfloat16)


PAIR_BLOCK = 128


def coherence_kernel(own_ref, stretch_ref, crossed_ref, inverse_ref, out_ref, picks_ref):
    minutes = crossed_ref.shape[0]
    moves = stretch_ref.shape[0] - 1

    @pl.when(pl.program_id(0) == 0)
    def _():
        rows = lax.broadcasted_iota(jnp.int32, (LAGS, LAGS), 0)
        for move in range(moves):
            picks_ref[:, move * LAGS:(move + 1) * LAGS] = (
                rows == stretch_ref[move + 1:move + 2, :]
            ).astype(jnp.bfloat16)

    inverse = inverse_ref[...]
    own = own_ref[0]
    stacked = None
    current = None
    for minute in range(minutes):
        correlation = jnp.dot(crossed_ref[minute], inverse, preferred_element_type=jnp.float32)
        if stacked is None:
            stacked, current = correlation, correlation
        else:
            stacked = stacked + correlation
            current = jnp.where(own == minute, correlation, current)
    high = stacked.astype(jnp.bfloat16)
    low = (stacked - high.astype(jnp.float32)).astype(jnp.bfloat16)
    picks = picks_ref[...]
    moved = jnp.dot(high, picks, preferred_element_type=jnp.float32) + jnp.dot(
        low, picks, preferred_element_type=jnp.float32
    )
    scale = 1.0 / LAGS
    current_power = jnp.sum(current * current, axis=1, keepdims=True) * scale
    lanes = lax.broadcasted_iota(jnp.int32, out_ref.shape, 1)
    result = jnp.zeros(out_ref.shape, jnp.float32)
    for stretch in range(moves + 1):
        if stretch == 0:
            shifted = stacked
        else:
            shifted = moved[:, (stretch - 1) * LAGS:stretch * LAGS]
        numerator = jnp.sum(current * shifted, axis=1, keepdims=True) * scale
        shifted_power = jnp.sum(shifted * shifted, axis=1, keepdims=True) * scale
        value = numerator / jnp.sqrt((current_power + epsilon) * (shifted_power + epsilon))
        result = jnp.where(lanes == stretch, value, result)
    out_ref[...] = result


def coherence(own_minute, stretch_index, crossed, inverse):
    minutes, pair_count, width = crossed.shape
    stretch_count = stretch_index.shape[0]
    own = jnp.reshape(own_minute, (1,)).astype(jnp.int32)
    out = pl.pallas_call(
        coherence_kernel,
        grid_spec=pltpu.PrefetchScalarGridSpec(
            num_scalar_prefetch=1,
            grid=(pair_count // PAIR_BLOCK,),
            in_specs=[
                pl.BlockSpec(stretch_index.shape, lambda i, own: (0, 0)),
                pl.BlockSpec((minutes, PAIR_BLOCK, width), lambda i, own: (0, i, 0)),
                pl.BlockSpec(inverse.shape, lambda i, own: (0, 0)),
            ],
            out_specs=pl.BlockSpec((PAIR_BLOCK, 128), lambda i, own: (i, 0)),
            scratch_shapes=[pltpu.VMEM((LAGS, (stretch_count - 1) * LAGS), jnp.bfloat16)],
        ),
        out_shape=jax.ShapeDtypeStruct((pair_count, 128), jnp.float32),
        compiler_params=pltpu.CompilerParams(
            dimension_semantics=("arbitrary",), vmem_limit_bytes=48 << 20
        ),
    )(own, stretch_index, crossed, inverse)
    return out[:, :stretch_count].T


def body(axis_order, record, pairs, stretch_index):
    block_rows = record.shape[1]
    minutes = lax.axis_size("tm")
    blocks = lax.axis_size("chan")
    position = lax.axis_index("chan")
    minute = lax.axis_index("tm")
    devices = minutes * blocks
    if devices * record.size * record.dtype.itemsize <= EXCHANGE_BYTES:
        targets = jnp.arange(devices, dtype=jnp.int32)
        if axis_order[0] == "tm":
            target_block = targets % blocks
        else:
            target_block = targets // minutes
        offset = position - target_block
        readers = (jnp.abs(offset) <= 1) | (jnp.abs(position + target_block - (blocks - 1)) <= 1)
        outgoing = jnp.where(readers[:, None, None], record, jnp.zeros_like(record))
        incoming = lax.all_to_all(outgoing, axis_order, 0, 0, tiled=True)
        slot_blocks = jnp.stack(
            [position - 1, position, position + 1,
             blocks - 2 - position, blocks - 1 - position, blocks - position]
        )
        slot_blocks = jnp.clip(slot_blocks, 0, blocks - 1)
        shifts = jnp.arange(minutes, dtype=jnp.int32)
        slot_minutes = (minute + shifts) % minutes
        if axis_order[0] == "tm":
            sources_at = slot_minutes[:, None] * blocks + slot_blocks[None, :]
        else:
            sources_at = slot_blocks[None, :] * minutes + slot_minutes[:, None]
        candidates = jnp.take(incoming, sources_at.reshape(-1), axis=0)
        candidates = candidates.reshape(minutes, 6 * block_rows, NT)
    else:
        parts = [record]
        for shift in range(1, minutes):
            parts.append(
                lax.ppermute(record, "tm", [(i, (i + shift) % minutes) for i in range(minutes)])
            )
        own_block = jnp.concatenate(parts, axis=0)
        below = lax.ppermute(own_block, "chan", [(s, s + 1) for s in range(blocks - 1)])
        above = lax.ppermute(own_block, "chan", [(s, s - 1) for s in range(1, blocks)])
        far_low = lax.ppermute(own_block, "chan", [(s, blocks - 2 - s) for s in range(blocks - 1)])
        far_mid = lax.ppermute(own_block, "chan", [(s, blocks - 1 - s) for s in range(blocks)])
        far_high = lax.ppermute(own_block, "chan", [(s, blocks - s) for s in range(1, blocks)])
        candidates = jnp.concatenate([below, own_block, above, far_low, far_mid, far_high], axis=1)
    slot_rows = candidates.shape[1]
    spectrum = jnp.dot(
        candidates.reshape(minutes * slot_rows, NT), forward_table(),
        preferred_element_type=jnp.float32,
    )
    whitened = whiten(spectrum).reshape(minutes, slot_rows, 2 * NF)

    column_index = jnp.arange(pairs.shape[1], dtype=jnp.int32)[None, :]
    is_near = column_index < pairs.shape[1] // 2
    near_slot = pairs - (position - 1) * block_rows
    far_slot = pairs - (blocks - 2 - position) * block_rows + 3 * block_rows
    slot_index = jnp.where(is_near, near_slot, far_slot)
    source_count, recv_count = slot_index.shape
    pair_count = source_count * recv_count
    sources = whitened[:, block_rows:2 * block_rows:8]
    selector = (
        slot_index.reshape(pair_count, 1) == jnp.arange(slot_rows, dtype=jnp.int32)[None, :]
    ).astype(jnp.bfloat16)
    receivers = jnp.einsum(
        "pq,mqk->mpk", selector, whitened, preferred_element_type=jnp.float32
    )
    receivers = receivers.reshape(minutes, source_count, recv_count, 2 * NF)
    crossed = cross_spectrum(sources[:, :, None, :], receivers)
    crossed = crossed.reshape(minutes, pair_count, 2 * NF)
    result = coherence(0, stretch_index, crossed, inverse_table())
    stretch_count = stretch_index.shape[0]
    return result.reshape(1, stretch_count, source_count, recv_count)


def solution(mesh):
    axis_order = tuple(name for name in mesh.axis_names if name in ("tm", "chan"))
    return jax.shard_map(
        functools.partial(body, axis_order),
        mesh=mesh,
        in_specs=(P("tm", "chan", None), P("chan", None), P()),
        out_specs=P("tm", None, "chan", None),
        check_vma=False,
    )
```

```python
import math

import jax
import jax.numpy as jnp
from jax import lax
from jax.experimental import pallas as pl
from jax.experimental.pallas import tpu as pltpu
from jax.sharding import PartitionSpec as P

NT = 1536
LAGS = 1024
NF = 768

epsilon = 1e-05


def unit_angles(numerators, period):
    phase = (numerators % period).astype(jnp.float32) * (2.0 * math.pi / period)
    return jnp.cos(phase), jnp.sin(phase)


def forward_table():
    coarse = NT // 128
    bins = jnp.arange(NF, dtype=jnp.int32)[None, :]
    cos_a, sin_a = unit_angles(jnp.arange(coarse, dtype=jnp.int32)[:, None] * bins, coarse)
    cos_c, sin_c = unit_angles(jnp.arange(128, dtype=jnp.int32)[:, None] * bins, NT)
    cos_t = cos_a[:, None, :] * cos_c[None] - sin_a[:, None, :] * sin_c[None]
    sin_t = sin_a[:, None, :] * cos_c[None] + cos_a[:, None, :] * sin_c[None]
    table = jnp.concatenate([cos_t, -sin_t], axis=-1).astype(jnp.bfloat16)
    return table.reshape(NT, 2 * NF)


def inverse_table():
    coarse = NT // 128
    groups = LAGS // 128
    bins = jnp.arange(NF, dtype=jnp.int32)[:, None]
    cos_a, sin_a = unit_angles(bins * (jnp.arange(groups, dtype=jnp.int32)[None, :] - groups // 2), coarse)
    cos_c, sin_c = unit_angles(bins * jnp.arange(128, dtype=jnp.int32)[None, :], NT)
    cos_t = cos_a[:, :, None] * cos_c[:, None, :] - sin_a[:, :, None] * sin_c[:, None, :]
    sin_t = sin_a[:, :, None] * cos_c[:, None, :] + cos_a[:, :, None] * sin_c[:, None, :]
    weight = jnp.where(bins == 0, 1.0, 2.0).astype(jnp.float32)[:, :, None]
    table = jnp.concatenate([weight * cos_t, -weight * sin_t], axis=0).astype(jnp.bfloat16)
    return table.reshape(2 * NF, LAGS)


def whiten(spectrum):
    power = jnp.mean(spectrum * spectrum, axis=-1, keepdims=True)
    return (spectrum / jnp.sqrt(power + epsilon)).astype(jnp.bfloat16)


def cross_spectrum(source_row, receivers):
    half_width = receivers.shape[-1] // 2
    source_vals = source_row.astype(jnp.float32)
    receiver_vals = receivers.astype(jnp.float32)
    src_re = source_vals[..., :half_width]
    src_im = source_vals[..., half_width:]
    rec_re = receiver_vals[..., :half_width]
    rec_im = receiver_vals[..., half_width:]
    real_part = src_re * rec_re + src_im * rec_im
    imag_part = src_re * rec_im - src_im * rec_re
    return jnp.concatenate([real_part, imag_part], axis=-1).astype(jnp.bfloat16)


PAIR_BLOCK = 128


def coherence_kernel(own_ref, stretch_ref, crossed_ref, inverse_ref, out_ref, picks_ref):
    minutes = crossed_ref.shape[0]
    moves = stretch_ref.shape[0] - 1

    @pl.when(pl.program_id(0) == 0)
    def _():
        rows = lax.broadcasted_iota(jnp.int32, (LAGS, LAGS), 0)
        for move in range(moves):
            picks_ref[:, move * LAGS:(move + 1) * LAGS] = (
                rows == stretch_ref[move + 1:move + 2, :]
            ).astype(jnp.bfloat16)

    inverse = inverse_ref[...]
    own = own_ref[0]
    stacked = None
    current = None
    for minute in range(minutes):
        correlation = jnp.dot(crossed_ref[minute], inverse, preferred_element_type=jnp.float32)
        if stacked is None:
            stacked, current = correlation, correlation
        else:
            stacked = stacked + correlation
            current = jnp.where(own == minute, correlation, current)
    high = stacked.astype(jnp.bfloat16)
    low = (stacked - high.astype(jnp.float32)).astype(jnp.bfloat16)
    picks = picks_ref[...]
    moved = jnp.dot(high, picks, preferred_element_type=jnp.float32) + jnp.dot(
        low, picks, preferred_element_type=jnp.float32
    )
    scale = 1.0 / LAGS
    current_power = jnp.sum(current * current, axis=1, keepdims=True) * scale
    lanes = lax.broadcasted_iota(jnp.int32, out_ref.shape, 1)
    result = jnp.zeros(out_ref.shape, jnp.float32)
    for stretch in range(moves + 1):
        if stretch == 0:
            shifted = stacked
        else:
            shifted = moved[:, (stretch - 1) * LAGS:stretch * LAGS]
        numerator = jnp.sum(current * shifted, axis=1, keepdims=True) * scale
        shifted_power = jnp.sum(shifted * shifted, axis=1, keepdims=True) * scale
        value = numerator / jnp.sqrt((current_power + epsilon) * (shifted_power + epsilon))
        result = jnp.where(lanes == stretch, value, result)
    out_ref[...] = result


def coherence(own_minute, stretch_index, crossed, inverse):
    minutes, pair_count, width = crossed.shape
    stretch_count = stretch_index.shape[0]
    own = jnp.reshape(own_minute, (1,)).astype(jnp.int32)
    out = pl.pallas_call(
        coherence_kernel,
        grid_spec=pltpu.PrefetchScalarGridSpec(
            num_scalar_prefetch=1,
            grid=(pair_count // PAIR_BLOCK,),
            in_specs=[
                pl.BlockSpec(stretch_index.shape, lambda i, own: (0, 0)),
                pl.BlockSpec((minutes, PAIR_BLOCK, width), lambda i, own: (0, i, 0)),
                pl.BlockSpec(inverse.shape, lambda i, own: (0, 0)),
            ],
            out_specs=pl.BlockSpec((PAIR_BLOCK, 128), lambda i, own: (i, 0)),
            scratch_shapes=[pltpu.VMEM((LAGS, (stretch_count - 1) * LAGS), jnp.bfloat16)],
        ),
        out_shape=jax.ShapeDtypeStruct((pair_count, 128), jnp.float32),
        compiler_params=pltpu.CompilerParams(
            dimension_semantics=("arbitrary",), vmem_limit_bytes=48 << 20
        ),
    )(own, stretch_index, crossed, inverse)
    return out[:, :stretch_count].T


def body(record, pairs, stretch_index):
    block_rows = record.shape[1]
    minutes = lax.axis_size("tm")
    blocks = lax.axis_size("chan")
    parts = [record]
    for shift in range(1, minutes):
        parts.append(
            lax.ppermute(record, "tm", [(i, (i + shift) % minutes) for i in range(minutes)])
        )
    own_block = jnp.concatenate(parts, axis=0)
    below = lax.ppermute(own_block, "chan", [(s, s + 1) for s in range(blocks - 1)])
    above = lax.ppermute(own_block, "chan", [(s, s - 1) for s in range(1, blocks)])
    near = jnp.concatenate([below, own_block, above], axis=1)
    far = lax.ppermute(near, "chan", [(s, blocks - 1 - s) for s in range(blocks)])
    candidates = jnp.concatenate([near, far], axis=1)
    slot_rows = candidates.shape[1]
    spectrum = jnp.dot(
        candidates.reshape(minutes * slot_rows, NT), forward_table(),
        preferred_element_type=jnp.float32,
    )
    whitened = whiten(spectrum).reshape(minutes, slot_rows, 2 * NF)

    position = lax.axis_index("chan")
    column_index = jnp.arange(pairs.shape[1], dtype=jnp.int32)[None, :]
    is_near = column_index < pairs.shape[1] // 2
    near_slot = pairs - (position - 1) * block_rows
    far_slot = pairs - (blocks - 2 - position) * block_rows + 3 * block_rows
    slot_index = jnp.where(is_near, near_slot, far_slot)
    source_count, recv_count = slot_index.shape
    pair_count = source_count * recv_count
    sources = whitened[:, block_rows:2 * block_rows:8]
    selector = (
        slot_index.reshape(pair_count, 1) == jnp.arange(slot_rows, dtype=jnp.int32)[None, :]
    ).astype(jnp.bfloat16)
    receivers = jnp.einsum(
        "pq,mqk->mpk", selector, whitened, preferred_element_type=jnp.float32
    )
    receivers = receivers.reshape(minutes, source_count, recv_count, 2 * NF)
    crossed = cross_spectrum(sources[:, :, None, :], receivers)
    crossed = crossed.reshape(minutes, pair_count, 2 * NF)
    result = coherence(0, stretch_index, crossed, inverse_table())
    stretch_count = stretch_index.shape[0]
    return result.reshape(1, stretch_count, source_count, recv_count)


def solution(mesh):
    return jax.shard_map(
        body,
        mesh=mesh,
        in_specs=(P("tm", "chan", None), P("chan", None), P()),
        out_specs=P("tm", None, "chan", None),
        check_vma=False,
    )
```

```python
import math

import jax
import jax.numpy as jnp
from jax import lax
from jax.experimental import pallas as pl
from jax.experimental.pallas import tpu as pltpu
from jax.sharding import PartitionSpec as P

NT = 1536
LAGS = 1024
NF = 768

epsilon = 1e-05


def unit_angles(numerators, period):
    phase = (numerators % period).astype(jnp.float32) * (2.0 * math.pi / period)
    return jnp.cos(phase), jnp.sin(phase)


def forward_table():
    coarse = NT // 128
    bins = jnp.arange(NF, dtype=jnp.int32)[None, :]
    cos_a, sin_a = unit_angles(jnp.arange(coarse, dtype=jnp.int32)[:, None] * bins, coarse)
    cos_c, sin_c = unit_angles(jnp.arange(128, dtype=jnp.int32)[:, None] * bins, NT)
    cos_t = cos_a[:, None, :] * cos_c[None] - sin_a[:, None, :] * sin_c[None]
    sin_t = sin_a[:, None, :] * cos_c[None] + cos_a[:, None, :] * sin_c[None]
    table = jnp.concatenate([cos_t, -sin_t], axis=-1).astype(jnp.bfloat16)
    return table.reshape(NT, 2 * NF)


def inverse_table():
    coarse = NT // 128
    groups = LAGS // 128
    bins = jnp.arange(NF, dtype=jnp.int32)[:, None]
    cos_a, sin_a = unit_angles(bins * (jnp.arange(groups, dtype=jnp.int32)[None, :] - groups // 2), coarse)
    cos_c, sin_c = unit_angles(bins * jnp.arange(128, dtype=jnp.int32)[None, :], NT)
    cos_t = cos_a[:, :, None] * cos_c[:, None, :] - sin_a[:, :, None] * sin_c[:, None, :]
    sin_t = sin_a[:, :, None] * cos_c[:, None, :] + cos_a[:, :, None] * sin_c[:, None, :]
    weight = jnp.where(bins == 0, 1.0, 2.0).astype(jnp.float32)[:, :, None]
    table = jnp.concatenate([weight * cos_t, -weight * sin_t], axis=0).astype(jnp.bfloat16)
    return table.reshape(2 * NF, LAGS)


def whiten(spectrum):
    power = jnp.mean(spectrum * spectrum, axis=-1, keepdims=True)
    return (spectrum / jnp.sqrt(power + epsilon)).astype(jnp.bfloat16)


def cross_spectrum(source_row, receivers):
    half_width = receivers.shape[-1] // 2
    source_vals = source_row.astype(jnp.float32)
    receiver_vals = receivers.astype(jnp.float32)
    src_re = source_vals[..., :half_width]
    src_im = source_vals[..., half_width:]
    rec_re = receiver_vals[..., :half_width]
    rec_im = receiver_vals[..., half_width:]
    real_part = src_re * rec_re + src_im * rec_im
    imag_part = src_re * rec_im - src_im * rec_re
    return jnp.concatenate([real_part, imag_part], axis=-1).astype(jnp.bfloat16)


PAIR_BLOCK = 128


def coherence_kernel(own_ref, stretch_ref, crossed_ref, inverse_ref, out_ref, picks_ref):
    minutes = crossed_ref.shape[0]
    moves = stretch_ref.shape[0] - 1

    @pl.when(pl.program_id(0) == 0)
    def _():
        rows = lax.broadcasted_iota(jnp.int32, (LAGS, LAGS), 0)
        for move in range(moves):
            picks_ref[:, move * LAGS:(move + 1) * LAGS] = (
                rows == stretch_ref[move + 1:move + 2, :]
            ).astype(jnp.bfloat16)

    inverse = inverse_ref[...]
    own = own_ref[0]
    stacked = None
    current = None
    for minute in range(minutes):
        correlation = jnp.dot(crossed_ref[minute], inverse, preferred_element_type=jnp.float32)
        if stacked is None:
            stacked, current = correlation, correlation
        else:
            stacked = stacked + correlation
            current = jnp.where(own == minute, correlation, current)
    high = stacked.astype(jnp.bfloat16)
    low = (stacked - high.astype(jnp.float32)).astype(jnp.bfloat16)
    picks = picks_ref[...]
    moved = jnp.dot(high, picks, preferred_element_type=jnp.float32) + jnp.dot(
        low, picks, preferred_element_type=jnp.float32
    )
    scale = 1.0 / LAGS
    current_power = jnp.sum(current * current, axis=1, keepdims=True) * scale
    lanes = lax.broadcasted_iota(jnp.int32, out_ref.shape, 1)
    result = jnp.zeros(out_ref.shape, jnp.float32)
    for stretch in range(moves + 1):
        if stretch == 0:
            shifted = stacked
        else:
            shifted = moved[:, (stretch - 1) * LAGS:stretch * LAGS]
        numerator = jnp.sum(current * shifted, axis=1, keepdims=True) * scale
        shifted_power = jnp.sum(shifted * shifted, axis=1, keepdims=True) * scale
        value = numerator / jnp.sqrt((current_power + epsilon) * (shifted_power + epsilon))
        result = jnp.where(lanes == stretch, value, result)
    out_ref[...] = result


def coherence(own_minute, stretch_index, crossed, inverse):
    minutes, pair_count, width = crossed.shape
    stretch_count = stretch_index.shape[0]
    own = jnp.reshape(own_minute, (1,)).astype(jnp.int32)
    out = pl.pallas_call(
        coherence_kernel,
        grid_spec=pltpu.PrefetchScalarGridSpec(
            num_scalar_prefetch=1,
            grid=(pair_count // PAIR_BLOCK,),
            in_specs=[
                pl.BlockSpec(stretch_index.shape, lambda i, own: (0, 0)),
                pl.BlockSpec((minutes, PAIR_BLOCK, width), lambda i, own: (0, i, 0)),
                pl.BlockSpec(inverse.shape, lambda i, own: (0, 0)),
            ],
            out_specs=pl.BlockSpec((PAIR_BLOCK, 128), lambda i, own: (i, 0)),
            scratch_shapes=[pltpu.VMEM((LAGS, (stretch_count - 1) * LAGS), jnp.bfloat16)],
        ),
        out_shape=jax.ShapeDtypeStruct((pair_count, 128), jnp.float32),
        compiler_params=pltpu.CompilerParams(
            dimension_semantics=("arbitrary",), vmem_limit_bytes=48 << 20
        ),
    )(own, stretch_index, crossed, inverse)
    return out[:, :stretch_count].T


def body(record, pairs, stretch_index):
    block_rows = record.shape[1]
    minutes = lax.axis_size("tm")
    blocks = lax.axis_size("chan")
    parts = [record]
    for shift in range(1, minutes):
        parts.append(
            lax.ppermute(record, "tm", [(i, (i + shift) % minutes) for i in range(minutes)])
        )
    own_block = jnp.concatenate(parts, axis=0)
    mirrored = lax.ppermute(own_block, "chan", [(s, blocks - 1 - s) for s in range(blocks)])
    bundle = jnp.concatenate([own_block, mirrored], axis=1)
    from_below = lax.ppermute(bundle, "chan", [(s, s + 1) for s in range(blocks - 1)])
    from_above = lax.ppermute(bundle, "chan", [(s, s - 1) for s in range(1, blocks)])
    candidates = jnp.concatenate(
        [
            from_below[:, :block_rows],
            own_block,
            from_above[:, :block_rows],
            from_above[:, block_rows:],
            mirrored,
            from_below[:, block_rows:],
        ],
        axis=1,
    )
    slot_rows = candidates.shape[1]
    spectrum = jnp.dot(
        candidates.reshape(minutes * slot_rows, NT), forward_table(),
        preferred_element_type=jnp.float32,
    )
    whitened = whiten(spectrum).reshape(minutes, slot_rows, 2 * NF)

    position = lax.axis_index("chan")
    column_index = jnp.arange(pairs.shape[1], dtype=jnp.int32)[None, :]
    is_near = column_index < pairs.shape[1] // 2
    near_slot = pairs - (position - 1) * block_rows
    far_slot = pairs - (blocks - 2 - position) * block_rows + 3 * block_rows
    slot_index = jnp.where(is_near, near_slot, far_slot)
    source_count, recv_count = slot_index.shape
    pair_count = source_count * recv_count
    sources = whitened[:, block_rows:2 * block_rows:8]
    selector = (
        slot_index.reshape(pair_count, 1) == jnp.arange(slot_rows, dtype=jnp.int32)[None, :]
    ).astype(jnp.bfloat16)
    receivers = jnp.einsum(
        "pq,mqk->mpk", selector, whitened, preferred_element_type=jnp.float32
    )
    receivers = receivers.reshape(minutes, source_count, recv_count, 2 * NF)
    crossed = cross_spectrum(sources[:, :, None, :], receivers)
    crossed = crossed.reshape(minutes, pair_count, 2 * NF)
    result = coherence(0, stretch_index, crossed, inverse_table())
    stretch_count = stretch_index.shape[0]
    return result.reshape(1, stretch_count, source_count, recv_count)


def solution(mesh):
    return jax.shard_map(
        body,
        mesh=mesh,
        in_specs=(P("tm", "chan", None), P("chan", None), P()),
        out_specs=P("tm", None, "chan", None),
        check_vma=False,
    )
```

```python
import math

import jax
import jax.numpy as jnp
from jax import lax
from jax.experimental import pallas as pl
from jax.experimental.pallas import tpu as pltpu
from jax.sharding import PartitionSpec as P

NT = 1536
LAGS = 1024
NF = 768

epsilon = 1e-05


def unit_angles(numerators, period):
    phase = (numerators % period).astype(jnp.float32) * (2.0 * math.pi / period)
    return jnp.cos(phase), jnp.sin(phase)


def fine_angles():
    bins = jnp.arange(NF, dtype=jnp.int32)[None, :]
    cos_1, sin_1 = unit_angles(jnp.arange(16, dtype=jnp.int32)[:, None] * bins, NT // 8)
    cos_2, sin_2 = unit_angles(jnp.arange(8, dtype=jnp.int32)[:, None] * bins, NT)
    cos_c = cos_1[:, None] * cos_2[None] - sin_1[:, None] * sin_2[None]
    sin_c = sin_1[:, None] * cos_2[None] + cos_1[:, None] * sin_2[None]
    return cos_c.reshape(128, NF), sin_c.reshape(128, NF)


def forward_table(cos_c, sin_c):
    coarse = NT // 128
    bins = jnp.arange(NF, dtype=jnp.int32)[None, :]
    cos_a, sin_a = unit_angles(jnp.arange(coarse, dtype=jnp.int32)[:, None] * bins, coarse)
    first = jnp.concatenate([cos_a, -sin_a], axis=1)
    second = jnp.concatenate([-sin_a, -cos_a], axis=1)
    fine_cos = jnp.concatenate([cos_c, cos_c], axis=1)
    fine_sin = jnp.concatenate([sin_c, sin_c], axis=1)
    table = first[:, None, :] * fine_cos[None] + second[:, None, :] * fine_sin[None]
    return table.astype(jnp.bfloat16).reshape(NT, 2 * NF)


def inverse_table(cos_c, sin_c):
    coarse = NT // 128
    groups = LAGS // 128
    bins = jnp.arange(NF, dtype=jnp.int32)[:, None]
    cos_a, sin_a = unit_angles(bins * (jnp.arange(groups, dtype=jnp.int32)[None, :] - groups // 2), coarse)
    weight = jnp.where(bins == 0, 1.0, 2.0).astype(jnp.float32)
    first = jnp.concatenate([weight * cos_a, -weight * sin_a], axis=0)
    second = jnp.concatenate([-weight * sin_a, -weight * cos_a], axis=0)
    fine_cos = jnp.concatenate([cos_c.T, cos_c.T], axis=0)
    fine_sin = jnp.concatenate([sin_c.T, sin_c.T], axis=0)
    table = first[:, :, None] * fine_cos[:, None, :] + second[:, :, None] * fine_sin[:, None, :]
    return table.astype(jnp.bfloat16).reshape(2 * NF, LAGS)


def whiten(spectrum):
    power = jnp.mean(spectrum * spectrum, axis=-1, keepdims=True)
    return (spectrum / jnp.sqrt(power + epsilon)).astype(jnp.bfloat16)


def cross_spectrum(source_row, receivers):
    half_width = receivers.shape[-1] // 2
    source_vals = source_row.astype(jnp.float32)
    receiver_vals = receivers.astype(jnp.float32)
    src_re = source_vals[..., :half_width]
    src_im = source_vals[..., half_width:]
    rec_re = receiver_vals[..., :half_width]
    rec_im = receiver_vals[..., half_width:]
    real_part = src_re * rec_re + src_im * rec_im
    imag_part = src_re * rec_im - src_im * rec_re
    return jnp.concatenate([real_part, imag_part], axis=-1).astype(jnp.bfloat16)


PAIR_BLOCK = 128


def coherence_kernel(own_ref, stretch_ref, crossed_ref, inverse_ref, out_ref, picks_ref):
    minutes = crossed_ref.shape[0]
    moves = stretch_ref.shape[0] - 1

    @pl.when(pl.program_id(0) == 0)
    def _():
        rows = lax.broadcasted_iota(jnp.int32, (LAGS, LAGS), 0)
        for move in range(moves):
            picks_ref[:, move * LAGS:(move + 1) * LAGS] = (
                rows == stretch_ref[move + 1:move + 2, :]
            ).astype(jnp.bfloat16)

    inverse = inverse_ref[...]
    own = own_ref[0]
    stacked = None
    current = None
    for minute in range(minutes):
        correlation = jnp.dot(crossed_ref[minute], inverse, preferred_element_type=jnp.float32)
        if stacked is None:
            stacked, current = correlation, correlation
        else:
            stacked = stacked + correlation
            current = jnp.where(own == minute, correlation, current)
    high = stacked.astype(jnp.bfloat16)
    low = (stacked - high.astype(jnp.float32)).astype(jnp.bfloat16)
    picks = picks_ref[...]
    moved = jnp.dot(high, picks, preferred_element_type=jnp.float32) + jnp.dot(
        low, picks, preferred_element_type=jnp.float32
    )
    scale = 1.0 / LAGS
    current_power = jnp.sum(current * current, axis=1, keepdims=True) * scale
    lanes = lax.broadcasted_iota(jnp.int32, out_ref.shape, 1)
    result = jnp.zeros(out_ref.shape, jnp.float32)
    for stretch in range(moves + 1):
        if stretch == 0:
            shifted = stacked
        else:
            shifted = moved[:, (stretch - 1) * LAGS:stretch * LAGS]
        numerator = jnp.sum(current * shifted, axis=1, keepdims=True) * scale
        shifted_power = jnp.sum(shifted * shifted, axis=1, keepdims=True) * scale
        value = numerator / jnp.sqrt((current_power + epsilon) * (shifted_power + epsilon))
        result = jnp.where(lanes == stretch, value, result)
    out_ref[...] = result


def coherence(own_minute, stretch_index, crossed, inverse):
    minutes, pair_count, width = crossed.shape
    stretch_count = stretch_index.shape[0]
    own = jnp.reshape(own_minute, (1,)).astype(jnp.int32)
    out = pl.pallas_call(
        coherence_kernel,
        grid_spec=pltpu.PrefetchScalarGridSpec(
            num_scalar_prefetch=1,
            grid=(pair_count // PAIR_BLOCK,),
            in_specs=[
                pl.BlockSpec(stretch_index.shape, lambda i, own: (0, 0)),
                pl.BlockSpec((minutes, PAIR_BLOCK, width), lambda i, own: (0, i, 0)),
                pl.BlockSpec(inverse.shape, lambda i, own: (0, 0)),
            ],
            out_specs=pl.BlockSpec((PAIR_BLOCK, 128), lambda i, own: (i, 0)),
            scratch_shapes=[pltpu.VMEM((LAGS, (stretch_count - 1) * LAGS), jnp.bfloat16)],
        ),
        out_shape=jax.ShapeDtypeStruct((pair_count, 128), jnp.float32),
        compiler_params=pltpu.CompilerParams(
            dimension_semantics=("arbitrary",), vmem_limit_bytes=48 << 20
        ),
    )(own, stretch_index, crossed, inverse)
    return out[:, :stretch_count].T


def body(record, pairs, stretch_index):
    block_rows = record.shape[1]
    minutes = lax.axis_size("tm")
    blocks = lax.axis_size("chan")
    parts = [record]
    for shift in range(1, minutes):
        parts.append(
            lax.ppermute(record, "tm", [(i, (i + shift) % minutes) for i in range(minutes)])
        )
    own_block = jnp.concatenate(parts, axis=0)
    below = lax.ppermute(own_block, "chan", [(s, s + 1) for s in range(blocks - 1)])
    above = lax.ppermute(own_block, "chan", [(s, s - 1) for s in range(1, blocks)])
    far_low = lax.ppermute(own_block, "chan", [(s, blocks - 2 - s) for s in range(blocks - 1)])
    far_mid = lax.ppermute(own_block, "chan", [(s, blocks - 1 - s) for s in range(blocks)])
    far_high = lax.ppermute(own_block, "chan", [(s, blocks - s) for s in range(1, blocks)])
    candidates = jnp.concatenate([below, own_block, above, far_low, far_mid, far_high], axis=1)
    slot_rows = candidates.shape[1]
    cos_c, sin_c = fine_angles()
    spectrum = jnp.dot(
        candidates.reshape(minutes * slot_rows, NT), forward_table(cos_c, sin_c),
        preferred_element_type=jnp.float32,
    )
    whitened = whiten(spectrum).reshape(minutes, slot_rows, 2 * NF)

    position = lax.axis_index("chan")
    column_index = jnp.arange(pairs.shape[1], dtype=jnp.int32)[None, :]
    is_near = column_index < pairs.shape[1] // 2
    near_slot = pairs - (position - 1) * block_rows
    far_slot = pairs - (blocks - 2 - position) * block_rows + 3 * block_rows
    slot_index = jnp.where(is_near, near_slot, far_slot)
    source_count, recv_count = slot_index.shape
    pair_count = source_count * recv_count
    sources = whitened[:, block_rows:2 * block_rows:8]
    selector = (
        slot_index.reshape(pair_count, 1) == jnp.arange(slot_rows, dtype=jnp.int32)[None, :]
    ).astype(jnp.bfloat16)
    receivers = jnp.einsum(
        "pq,mqk->mpk", selector, whitened, preferred_element_type=jnp.float32
    )
    receivers = receivers.reshape(minutes, source_count, recv_count, 2 * NF)
    crossed = cross_spectrum(sources[:, :, None, :], receivers)
    crossed = crossed.reshape(minutes, pair_count, 2 * NF)
    result = coherence(0, stretch_index, crossed, inverse_table(cos_c, sin_c))
    stretch_count = stretch_index.shape[0]
    return result.reshape(1, stretch_count, source_count, recv_count)


def solution(mesh):
    return jax.shard_map(
        body,
        mesh=mesh,
        in_specs=(P("tm", "chan", None), P("chan", None), P()),
        out_specs=P("tm", None, "chan", None),
        check_vma=False,
    )
```

```python
import math

import jax
import jax.numpy as jnp
from jax import lax
from jax.experimental import pallas as pl
from jax.experimental.pallas import tpu as pltpu
from jax.sharding import PartitionSpec as P

NT = 1536
LAGS = 1024
NF = 768

epsilon = 1e-05


def unit_angles(numerators, period):
    phase = (numerators % period).astype(jnp.float32) * (2.0 * math.pi / period)
    return jnp.cos(phase), jnp.sin(phase)


def forward_table():
    coarse = NT // 128
    bins = jnp.arange(NF, dtype=jnp.int32)[None, :]
    cos_a, sin_a = unit_angles(jnp.arange(coarse, dtype=jnp.int32)[:, None] * bins, coarse)
    cos_c, sin_c = unit_angles(jnp.arange(128, dtype=jnp.int32)[:, None] * bins, NT)
    cos_t = cos_a[:, None, :] * cos_c[None] - sin_a[:, None, :] * sin_c[None]
    sin_t = sin_a[:, None, :] * cos_c[None] + cos_a[:, None, :] * sin_c[None]
    table = jnp.concatenate([cos_t, -sin_t], axis=-1).astype(jnp.bfloat16)
    return table.reshape(NT, 2 * NF)


def inverse_factors():
    coarse = NT // 128
    groups = LAGS // 128
    bins = jnp.arange(NF, dtype=jnp.int32)[:, None]
    cos_a, sin_a = unit_angles(bins * (jnp.arange(groups, dtype=jnp.int32)[None, :] - groups // 2), coarse)
    cos_c, sin_c = unit_angles(bins * jnp.arange(128, dtype=jnp.int32)[None, :], NT)
    weight = jnp.where(bins == 0, 1.0, 2.0).astype(jnp.float32)
    return weight * cos_a, weight * sin_a, cos_c, sin_c


def whiten(spectrum):
    power = jnp.mean(spectrum * spectrum, axis=-1, keepdims=True)
    return (spectrum / jnp.sqrt(power + epsilon)).astype(jnp.bfloat16)


def cross_spectrum(source_row, receivers):
    half_width = receivers.shape[-1] // 2
    source_vals = source_row.astype(jnp.float32)
    receiver_vals = receivers.astype(jnp.float32)
    src_re = source_vals[..., :half_width]
    src_im = source_vals[..., half_width:]
    rec_re = receiver_vals[..., :half_width]
    rec_im = receiver_vals[..., half_width:]
    real_part = src_re * rec_re + src_im * rec_im
    imag_part = src_re * rec_im - src_im * rec_re
    return jnp.concatenate([real_part, imag_part], axis=-1).astype(jnp.bfloat16)


PAIR_BLOCK = 128


def coherence_kernel(
    own_ref, stretch_ref, crossed_ref, wcos_ref, wsin_ref, fcos_ref, fsin_ref,
    out_ref, picks_ref, inverse_ref,
):
    minutes = crossed_ref.shape[0]
    moves = stretch_ref.shape[0] - 1
    groups = wcos_ref.shape[1]
    fine = fcos_ref.shape[1]

    @pl.when(pl.program_id(0) == 0)
    def _():
        fine_cos = fcos_ref[...]
        fine_sin = fsin_ref[...]
        for group in range(groups):
            coarse_cos = wcos_ref[:, group:group + 1]
            coarse_sin = wsin_ref[:, group:group + 1]
            lags = slice(group * fine, (group + 1) * fine)
            inverse_ref[:NF, lags] = (coarse_cos * fine_cos - coarse_sin * fine_sin).astype(
                jnp.bfloat16
            )
            inverse_ref[NF:, lags] = (-(coarse_sin * fine_cos + coarse_cos * fine_sin)).astype(
                jnp.bfloat16
            )

    @pl.when(pl.program_id(0) == 0)
    def _():
        rows = lax.broadcasted_iota(jnp.int32, (LAGS, LAGS), 0)
        for move in range(moves):
            picks_ref[:, move * LAGS:(move + 1) * LAGS] = (
                rows == stretch_ref[move + 1:move + 2, :]
            ).astype(jnp.bfloat16)

    inverse = inverse_ref[...]
    own = own_ref[0]
    stacked = None
    current = None
    for minute in range(minutes):
        correlation = jnp.dot(crossed_ref[minute], inverse, preferred_element_type=jnp.float32)
        if stacked is None:
            stacked, current = correlation, correlation
        else:
            stacked = stacked + correlation
            current = jnp.where(own == minute, correlation, current)
    high = stacked.astype(jnp.bfloat16)
    low = (stacked - high.astype(jnp.float32)).astype(jnp.bfloat16)
    picks = picks_ref[...]
    moved = jnp.dot(high, picks, preferred_element_type=jnp.float32) + jnp.dot(
        low, picks, preferred_element_type=jnp.float32
    )
    scale = 1.0 / LAGS
    current_power = jnp.sum(current * current, axis=1, keepdims=True) * scale
    lanes = lax.broadcasted_iota(jnp.int32, out_ref.shape, 1)
    result = jnp.zeros(out_ref.shape, jnp.float32)
    for stretch in range(moves + 1):
        if stretch == 0:
            shifted = stacked
        else:
            shifted = moved[:, (stretch - 1) * LAGS:stretch * LAGS]
        numerator = jnp.sum(current * shifted, axis=1, keepdims=True) * scale
        shifted_power = jnp.sum(shifted * shifted, axis=1, keepdims=True) * scale
        value = numerator / jnp.sqrt((current_power + epsilon) * (shifted_power + epsilon))
        result = jnp.where(lanes == stretch, value, result)
    out_ref[...] = result


def coherence(own_minute, stretch_index, crossed, factors):
    minutes, pair_count, width = crossed.shape
    stretch_count = stretch_index.shape[0]
    own = jnp.reshape(own_minute, (1,)).astype(jnp.int32)
    out = pl.pallas_call(
        coherence_kernel,
        grid_spec=pltpu.PrefetchScalarGridSpec(
            num_scalar_prefetch=1,
            grid=(pair_count // PAIR_BLOCK,),
            in_specs=[
                pl.BlockSpec(stretch_index.shape, lambda i, own: (0, 0)),
                pl.BlockSpec((minutes, PAIR_BLOCK, width), lambda i, own: (0, i, 0)),
            ] + [pl.BlockSpec(factor.shape, lambda i, own: (0, 0)) for factor in factors],
            out_specs=pl.BlockSpec((PAIR_BLOCK, 128), lambda i, own: (i, 0)),
            scratch_shapes=[
                pltpu.VMEM((LAGS, (stretch_count - 1) * LAGS), jnp.bfloat16),
                pltpu.VMEM((width, LAGS), jnp.bfloat16),
            ],
        ),
        out_shape=jax.ShapeDtypeStruct((pair_count, 128), jnp.float32),
        compiler_params=pltpu.CompilerParams(
            dimension_semantics=("arbitrary",), vmem_limit_bytes=48 << 20
        ),
    )(own, stretch_index, crossed, *factors)
    return out[:, :stretch_count].T


def body(record, pairs, stretch_index):
    block_rows = record.shape[1]
    minutes = lax.axis_size("tm")
    blocks = lax.axis_size("chan")
    parts = [record]
    for shift in range(1, minutes):
        parts.append(
            lax.ppermute(record, "tm", [(i, (i + shift) % minutes) for i in range(minutes)])
        )
    own_block = jnp.concatenate(parts, axis=0)
    below = lax.ppermute(own_block, "chan", [(s, s + 1) for s in range(blocks - 1)])
    above = lax.ppermute(own_block, "chan", [(s, s - 1) for s in range(1, blocks)])
    far_low = lax.ppermute(own_block, "chan", [(s, blocks - 2 - s) for s in range(blocks - 1)])
    far_mid = lax.ppermute(own_block, "chan", [(s, blocks - 1 - s) for s in range(blocks)])
    far_high = lax.ppermute(own_block, "chan", [(s, blocks - s) for s in range(1, blocks)])
    candidates = jnp.concatenate([below, own_block, above, far_low, far_mid, far_high], axis=1)
    slot_rows = candidates.shape[1]
    spectrum = jnp.dot(
        candidates.reshape(minutes * slot_rows, NT), forward_table(),
        preferred_element_type=jnp.float32,
    )
    whitened = whiten(spectrum).reshape(minutes, slot_rows, 2 * NF)

    position = lax.axis_index("chan")
    column_index = jnp.arange(pairs.shape[1], dtype=jnp.int32)[None, :]
    is_near = column_index < pairs.shape[1] // 2
    near_slot = pairs - (position - 1) * block_rows
    far_slot = pairs - (blocks - 2 - position) * block_rows + 3 * block_rows
    slot_index = jnp.where(is_near, near_slot, far_slot)
    source_count, recv_count = slot_index.shape
    pair_count = source_count * recv_count
    sources = whitened[:, block_rows:2 * block_rows:8]
    selector = (
        slot_index.reshape(pair_count, 1) == jnp.arange(slot_rows, dtype=jnp.int32)[None, :]
    ).astype(jnp.bfloat16)
    receivers = jnp.einsum(
        "pq,mqk->mpk", selector, whitened, preferred_element_type=jnp.float32
    )
    receivers = receivers.reshape(minutes, source_count, recv_count, 2 * NF)
    crossed = cross_spectrum(sources[:, :, None, :], receivers)
    crossed = crossed.reshape(minutes, pair_count, 2 * NF)
    result = coherence(0, stretch_index, crossed, inverse_factors())
    stretch_count = stretch_index.shape[0]
    return result.reshape(1, stretch_count, source_count, recv_count)


def solution(mesh):
    return jax.shard_map(
        body,
        mesh=mesh,
        in_specs=(P("tm", "chan", None), P("chan", None), P()),
        out_specs=P("tm", None, "chan", None),
        check_vma=False,
    )
```

```python
import math

import jax
import jax.numpy as jnp
from jax import lax
from jax.experimental import pallas as pl
from jax.experimental.pallas import tpu as pltpu
from jax.sharding import PartitionSpec as P

NT = 1536
LAGS = 1024
NF = 768

epsilon = 1e-05


def unit_angles(numerators, period):
    phase = (numerators % period).astype(jnp.float32) * (2.0 * math.pi / period)
    return jnp.cos(phase), jnp.sin(phase)


def forward_table():
    coarse = NT // 128
    bins = jnp.arange(NF, dtype=jnp.int32)[None, :]
    cos_a, sin_a = unit_angles(jnp.arange(coarse, dtype=jnp.int32)[:, None] * bins, coarse)
    cos_c, sin_c = unit_angles(jnp.arange(128, dtype=jnp.int32)[:, None] * bins, NT)
    cos_t = cos_a[:, None, :] * cos_c[None] - sin_a[:, None, :] * sin_c[None]
    sin_t = sin_a[:, None, :] * cos_c[None] + cos_a[:, None, :] * sin_c[None]
    table = jnp.concatenate([cos_t, -sin_t], axis=-1).astype(jnp.bfloat16)
    return table.reshape(NT, 2 * NF)


def inverse_factors():
    coarse = NT // 128
    groups = LAGS // 128
    bins = jnp.arange(NF, dtype=jnp.int32)[:, None]
    cos_a, sin_a = unit_angles(bins * (jnp.arange(groups, dtype=jnp.int32)[None, :] - groups // 2), coarse)
    cos_c, sin_c = unit_angles(bins * jnp.arange(128, dtype=jnp.int32)[None, :], NT)
    weight = jnp.where(bins == 0, 1.0, 2.0).astype(jnp.float32)
    return weight * cos_a, weight * sin_a, cos_c, sin_c


def whiten(spectrum):
    power = jnp.mean(spectrum * spectrum, axis=-1, keepdims=True)
    return (spectrum / jnp.sqrt(power + epsilon)).astype(jnp.bfloat16)


def cross_spectrum(source_row, receivers):
    half_width = receivers.shape[-1] // 2
    source_vals = source_row.astype(jnp.float32)
    receiver_vals = receivers.astype(jnp.float32)
    src_re = source_vals[..., :half_width]
    src_im = source_vals[..., half_width:]
    rec_re = receiver_vals[..., :half_width]
    rec_im = receiver_vals[..., half_width:]
    real_part = src_re * rec_re + src_im * rec_im
    imag_part = src_re * rec_im - src_im * rec_re
    return jnp.concatenate([real_part, imag_part], axis=-1).astype(jnp.bfloat16)


PAIR_BLOCK = 128


def coherence_kernel(
    own_ref, stretch_ref, crossed_ref, wcos_ref, wsin_ref, fcos_ref, fsin_ref,
    out_ref, picks_ref, inverse_ref,
):
    minutes = crossed_ref.shape[0]
    moves = stretch_ref.shape[0] - 1
    groups = wcos_ref.shape[1]
    fine = fcos_ref.shape[1]

    @pl.when(pl.program_id(0) == 0)
    def _():
        fine_cos = fcos_ref[...]
        fine_sin = fsin_ref[...]
        for group in range(groups):
            coarse_cos = wcos_ref[:, group:group + 1]
            coarse_sin = wsin_ref[:, group:group + 1]
            lags = slice(group * fine, (group + 1) * fine)
            inverse_ref[:NF, lags] = (coarse_cos * fine_cos - coarse_sin * fine_sin).astype(
                jnp.bfloat16
            )
            inverse_ref[NF:, lags] = (-(coarse_sin * fine_cos + coarse_cos * fine_sin)).astype(
                jnp.bfloat16
            )

    @pl.when(pl.program_id(0) == 0)
    def _():
        rows = lax.broadcasted_iota(jnp.int32, (LAGS, LAGS), 0)
        for move in range(moves):
            picks_ref[:, move * LAGS:(move + 1) * LAGS] = (
                rows == stretch_ref[move + 1:move + 2, :]
            ).astype(jnp.bfloat16)

    inverse = inverse_ref[...]
    own = own_ref[0]
    stacked = None
    current = None
    for minute in range(minutes):
        correlation = jnp.dot(crossed_ref[minute], inverse, preferred_element_type=jnp.float32)
        if stacked is None:
            stacked, current = correlation, correlation
        else:
            stacked = stacked + correlation
            current = jnp.where(own == minute, correlation, current)
    high = stacked.astype(jnp.bfloat16)
    low = (stacked - high.astype(jnp.float32)).astype(jnp.bfloat16)
    picks = picks_ref[...]
    moved = jnp.dot(high, picks, preferred_element_type=jnp.float32) + jnp.dot(
        low, picks, preferred_element_type=jnp.float32
    )
    scale = 1.0 / LAGS
    current_power = jnp.sum(current * current, axis=1, keepdims=True) * scale
    lanes = lax.broadcasted_iota(jnp.int32, out_ref.shape, 1)
    result = jnp.zeros(out_ref.shape, jnp.float32)
    for stretch in range(moves + 1):
        if stretch == 0:
            shifted = stacked
        else:
            shifted = moved[:, (stretch - 1) * LAGS:stretch * LAGS]
        numerator = jnp.sum(current * shifted, axis=1, keepdims=True) * scale
        shifted_power = jnp.sum(shifted * shifted, axis=1, keepdims=True) * scale
        value = numerator / jnp.sqrt((current_power + epsilon) * (shifted_power + epsilon))
        result = jnp.where(lanes == stretch, value, result)
    out_ref[...] = result


def coherence(own_minute, stretch_index, crossed, factors):
    minutes, pair_count, width = crossed.shape
    stretch_count = stretch_index.shape[0]
    own = jnp.reshape(own_minute, (1,)).astype(jnp.int32)
    out = pl.pallas_call(
        coherence_kernel,
        grid_spec=pltpu.PrefetchScalarGridSpec(
            num_scalar_prefetch=1,
            grid=(pair_count // PAIR_BLOCK,),
            in_specs=[
                pl.BlockSpec(stretch_index.shape, lambda i, own: (0, 0)),
                pl.BlockSpec((minutes, PAIR_BLOCK, width), lambda i, own: (0, i, 0)),
            ] + [pl.BlockSpec(factor.shape, lambda i, own: (0, 0)) for factor in factors],
            out_specs=pl.BlockSpec((PAIR_BLOCK, 128), lambda i, own: (i, 0)),
            scratch_shapes=[
                pltpu.VMEM((LAGS, (stretch_count - 1) * LAGS), jnp.bfloat16),
                pltpu.VMEM((width, LAGS), jnp.bfloat16),
            ],
        ),
        out_shape=jax.ShapeDtypeStruct((pair_count, 128), jnp.float32),
        compiler_params=pltpu.CompilerParams(
            dimension_semantics=("arbitrary",), vmem_limit_bytes=48 << 20
        ),
    )(own, stretch_index, crossed, *factors)
    return out[:, :stretch_count].T


def body(record, pairs, stretch_index):
    block_rows = record.shape[1]
    minutes = lax.axis_size("tm")
    blocks = lax.axis_size("chan")
    parts = [record]
    for shift in range(1, minutes):
        parts.append(
            lax.ppermute(record, "tm", [(i, (i + shift) % minutes) for i in range(minutes)])
        )
    own_block = jnp.concatenate(parts, axis=0)
    mirrored = lax.ppermute(own_block, "chan", [(s, blocks - 1 - s) for s in range(blocks)])
    bundle = jnp.concatenate([own_block, mirrored], axis=1)
    from_below = lax.ppermute(bundle, "chan", [(s, s + 1) for s in range(blocks - 1)])
    from_above = lax.ppermute(bundle, "chan", [(s, s - 1) for s in range(1, blocks)])
    candidates = jnp.concatenate(
        [
            from_below[:, :block_rows],
            own_block,
            from_above[:, :block_rows],
            from_above[:, block_rows:],
            mirrored,
            from_below[:, block_rows:],
        ],
        axis=1,
    )
    slot_rows = candidates.shape[1]
    spectrum = jnp.dot(
        candidates.reshape(minutes * slot_rows, NT), forward_table(),
        preferred_element_type=jnp.float32,
    )
    whitened = whiten(spectrum).reshape(minutes, slot_rows, 2 * NF)

    position = lax.axis_index("chan")
    column_index = jnp.arange(pairs.shape[1], dtype=jnp.int32)[None, :]
    is_near = column_index < pairs.shape[1] // 2
    near_slot = pairs - (position - 1) * block_rows
    far_slot = pairs - (blocks - 2 - position) * block_rows + 3 * block_rows
    slot_index = jnp.where(is_near, near_slot, far_slot)
    source_count, recv_count = slot_index.shape
    pair_count = source_count * recv_count
    sources = whitened[:, block_rows:2 * block_rows:8]
    selector = (
        slot_index.reshape(pair_count, 1) == jnp.arange(slot_rows, dtype=jnp.int32)[None, :]
    ).astype(jnp.bfloat16)
    receivers = jnp.einsum(
        "pq,mqk->mpk", selector, whitened, preferred_element_type=jnp.float32
    )
    receivers = receivers.reshape(minutes, source_count, recv_count, 2 * NF)
    crossed = cross_spectrum(sources[:, :, None, :], receivers)
    crossed = crossed.reshape(minutes, pair_count, 2 * NF)
    result = coherence(0, stretch_index, crossed, inverse_factors())
    stretch_count = stretch_index.shape[0]
    return result.reshape(1, stretch_count, source_count, recv_count)


def solution(mesh):
    return jax.shard_map(
        body,
        mesh=mesh,
        in_specs=(P("tm", "chan", None), P("chan", None), P()),
        out_specs=P("tm", None, "chan", None),
        check_vma=False,
    )
```

```python
import math

import jax
import jax.numpy as jnp
from jax import lax
from jax.experimental import pallas as pl
from jax.experimental.pallas import tpu as pltpu
from jax.sharding import PartitionSpec as P

NT = 1536
LAGS = 1024
NF = 768

epsilon = 1e-05


def unit_angles(numerators, period):
    phase = (numerators % period).astype(jnp.float32) * (2.0 * math.pi / period)
    return jnp.cos(phase), jnp.sin(phase)


def forward_table():
    coarse = NT // 128
    bins = jnp.arange(NF, dtype=jnp.int32)[None, :]
    cos_a, sin_a = unit_angles(jnp.arange(coarse, dtype=jnp.int32)[:, None] * bins, coarse)
    cos_c, sin_c = unit_angles(jnp.arange(128, dtype=jnp.int32)[:, None] * bins, NT)
    cos_t = cos_a[:, None, :] * cos_c[None] - sin_a[:, None, :] * sin_c[None]
    sin_t = sin_a[:, None, :] * cos_c[None] + cos_a[:, None, :] * sin_c[None]
    table = jnp.concatenate([cos_t, -sin_t], axis=-1).astype(jnp.bfloat16)
    return table.reshape(NT, 2 * NF)


def inverse_factors():
    coarse = NT // 128
    groups = LAGS // 128
    bins = jnp.arange(NF, dtype=jnp.int32)[:, None]
    cos_a, sin_a = unit_angles(bins * (jnp.arange(groups, dtype=jnp.int32)[None, :] - groups // 2), coarse)
    cos_c, sin_c = unit_angles(bins * jnp.arange(128, dtype=jnp.int32)[None, :], NT)
    weight = jnp.where(bins == 0, 1.0, 2.0).astype(jnp.float32)
    return weight * cos_a, weight * sin_a, cos_c, sin_c


def whiten(spectrum):
    power = jnp.mean(spectrum * spectrum, axis=-1, keepdims=True)
    return (spectrum / jnp.sqrt(power + epsilon)).astype(jnp.bfloat16)


def cross_spectrum(source_row, receivers):
    half_width = receivers.shape[-1] // 2
    source_vals = source_row.astype(jnp.float32)
    receiver_vals = receivers.astype(jnp.float32)
    src_re = source_vals[..., :half_width]
    src_im = source_vals[..., half_width:]
    rec_re = receiver_vals[..., :half_width]
    rec_im = receiver_vals[..., half_width:]
    real_part = src_re * rec_re + src_im * rec_im
    imag_part = src_re * rec_im - src_im * rec_re
    return jnp.concatenate([real_part, imag_part], axis=-1).astype(jnp.bfloat16)


PAIR_BLOCK = 256


def coherence_kernel(
    own_ref, stretch_ref, crossed_ref, wcos_ref, wsin_ref, fcos_ref, fsin_ref,
    out_ref, picks_ref, inverse_ref,
):
    minutes = crossed_ref.shape[0]
    moves = stretch_ref.shape[0] - 1
    groups = wcos_ref.shape[1]
    fine = fcos_ref.shape[1]

    @pl.when(pl.program_id(0) == 0)
    def _():
        fine_cos = fcos_ref[...]
        fine_sin = fsin_ref[...]
        for group in range(groups):
            coarse_cos = wcos_ref[:, group:group + 1]
            coarse_sin = wsin_ref[:, group:group + 1]
            lags = slice(group * fine, (group + 1) * fine)
            inverse_ref[:NF, lags] = (coarse_cos * fine_cos - coarse_sin * fine_sin).astype(
                jnp.bfloat16
            )
            inverse_ref[NF:, lags] = (-(coarse_sin * fine_cos + coarse_cos * fine_sin)).astype(
                jnp.bfloat16
            )

    @pl.when(pl.program_id(0) == 0)
    def _():
        rows = lax.broadcasted_iota(jnp.int32, (LAGS, LAGS), 0)
        for move in range(moves):
            picks_ref[:, move * LAGS:(move + 1) * LAGS] = (
                rows == stretch_ref[move + 1:move + 2, :]
            ).astype(jnp.bfloat16)

    inverse = inverse_ref[...]
    own = own_ref[0]
    stacked = None
    current = None
    for minute in range(minutes):
        correlation = jnp.dot(crossed_ref[minute], inverse, preferred_element_type=jnp.float32)
        if stacked is None:
            stacked, current = correlation, correlation
        else:
            stacked = stacked + correlation
            current = jnp.where(own == minute, correlation, current)
    high = stacked.astype(jnp.bfloat16)
    low = (stacked - high.astype(jnp.float32)).astype(jnp.bfloat16)
    rows = stacked.shape[0]
    moved = jnp.dot(
        jnp.concatenate([high, low], axis=0), picks_ref[...], preferred_element_type=jnp.float32
    )
    moved = moved[:rows] + moved[rows:]
    scale = 1.0 / LAGS
    current_power = jnp.sum(current * current, axis=1, keepdims=True) * scale
    lanes = lax.broadcasted_iota(jnp.int32, out_ref.shape, 1)
    result = jnp.zeros(out_ref.shape, jnp.float32)
    for stretch in range(moves + 1):
        if stretch == 0:
            shifted = stacked
        else:
            shifted = moved[:, (stretch - 1) * LAGS:stretch * LAGS]
        numerator = jnp.sum(current * shifted, axis=1, keepdims=True) * scale
        shifted_power = jnp.sum(shifted * shifted, axis=1, keepdims=True) * scale
        value = numerator / jnp.sqrt((current_power + epsilon) * (shifted_power + epsilon))
        result = jnp.where(lanes == stretch, value, result)
    out_ref[...] = result


def coherence(own_minute, stretch_index, crossed, factors):
    minutes, pair_count, width = crossed.shape
    stretch_count = stretch_index.shape[0]
    own = jnp.reshape(own_minute, (1,)).astype(jnp.int32)
    block = min(PAIR_BLOCK, pair_count)
    out = pl.pallas_call(
        coherence_kernel,
        grid_spec=pltpu.PrefetchScalarGridSpec(
            num_scalar_prefetch=1,
            grid=(pair_count // block,),
            in_specs=[
                pl.BlockSpec(stretch_index.shape, lambda i, own: (0, 0)),
                pl.BlockSpec((minutes, block, width), lambda i, own: (0, i, 0)),
            ] + [pl.BlockSpec(factor.shape, lambda i, own: (0, 0)) for factor in factors],
            out_specs=pl.BlockSpec((block, 128), lambda i, own: (i, 0)),
            scratch_shapes=[
                pltpu.VMEM((LAGS, (stretch_count - 1) * LAGS), jnp.bfloat16),
                pltpu.VMEM((width, LAGS), jnp.bfloat16),
            ],
        ),
        out_shape=jax.ShapeDtypeStruct((pair_count, 128), jnp.float32),
        compiler_params=pltpu.CompilerParams(
            dimension_semantics=("arbitrary",), vmem_limit_bytes=48 << 20
        ),
    )(own, stretch_index, crossed, *factors)
    return out[:, :stretch_count].T


def body(record, pairs, stretch_index):
    block_rows = record.shape[1]
    minutes = lax.axis_size("tm")
    blocks = lax.axis_size("chan")
    parts = [record]
    for shift in range(1, minutes):
        parts.append(
            lax.ppermute(record, "tm", [(i, (i + shift) % minutes) for i in range(minutes)])
        )
    own_block = jnp.concatenate(parts, axis=0)
    mirrored = lax.ppermute(own_block, "chan", [(s, blocks - 1 - s) for s in range(blocks)])
    bundle = jnp.concatenate([own_block, mirrored], axis=1)
    from_below = lax.ppermute(bundle, "chan", [(s, s + 1) for s in range(blocks - 1)])
    from_above = lax.ppermute(bundle, "chan", [(s, s - 1) for s in range(1, blocks)])
    candidates = jnp.concatenate(
        [
            from_below[:, :block_rows],
            own_block,
            from_above[:, :block_rows],
            from_above[:, block_rows:],
            mirrored,
            from_below[:, block_rows:],
        ],
        axis=1,
    )
    slot_rows = candidates.shape[1]
    spectrum = jnp.dot(
        candidates.reshape(minutes * slot_rows, NT), forward_table(),
        preferred_element_type=jnp.float32,
    )
    whitened = whiten(spectrum).reshape(minutes, slot_rows, 2 * NF)

    position = lax.axis_index("chan")
    column_index = jnp.arange(pairs.shape[1], dtype=jnp.int32)[None, :]
    is_near = column_index < pairs.shape[1] // 2
    near_slot = pairs - (position - 1) * block_rows
    far_slot = pairs - (blocks - 2 - position) * block_rows + 3 * block_rows
    slot_index = jnp.where(is_near, near_slot, far_slot)
    source_count, recv_count = slot_index.shape
    pair_count = source_count * recv_count
    sources = whitened[:, block_rows:2 * block_rows:8]
    selector = (
        slot_index.reshape(pair_count, 1) == jnp.arange(slot_rows, dtype=jnp.int32)[None, :]
    ).astype(jnp.bfloat16)
    receivers = jnp.einsum(
        "pq,mqk->mpk", selector, whitened, preferred_element_type=jnp.float32
    )
    receivers = receivers.reshape(minutes, source_count, recv_count, 2 * NF)
    crossed = cross_spectrum(sources[:, :, None, :], receivers)
    crossed = crossed.reshape(minutes, pair_count, 2 * NF)
    result = coherence(0, stretch_index, crossed, inverse_factors())
    stretch_count = stretch_index.shape[0]
    return result.reshape(1, stretch_count, source_count, recv_count)


def solution(mesh):
    return jax.shard_map(
        body,
        mesh=mesh,
        in_specs=(P("tm", "chan", None), P("chan", None), P()),
        out_specs=P("tm", None, "chan", None),
        check_vma=False,
    )
```

```python
import math

import jax
import jax.numpy as jnp
from jax import lax
from jax.experimental import pallas as pl
from jax.experimental.pallas import tpu as pltpu
from jax.sharding import PartitionSpec as P

NT = 1536
LAGS = 1024
NF = 768

epsilon = 1e-05


def unit_angles(numerators, period):
    phase = (numerators % period).astype(jnp.float32) * (2.0 * math.pi / period)
    return jnp.cos(phase), jnp.sin(phase)


def forward_table():
    coarse = NT // 128
    bins = jnp.arange(NF, dtype=jnp.int32)[None, :]
    cos_a, sin_a = unit_angles(jnp.arange(coarse, dtype=jnp.int32)[:, None] * bins, coarse)
    cos_c, sin_c = unit_angles(jnp.arange(128, dtype=jnp.int32)[:, None] * bins, NT)
    cos_t = cos_a[:, None, :] * cos_c[None] - sin_a[:, None, :] * sin_c[None]
    sin_t = sin_a[:, None, :] * cos_c[None] + cos_a[:, None, :] * sin_c[None]
    table = jnp.concatenate([cos_t, -sin_t], axis=-1).astype(jnp.bfloat16)
    return table.reshape(NT, 2 * NF)


def inverse_factors():
    coarse = NT // 128
    groups = LAGS // 128
    bins = jnp.arange(NF, dtype=jnp.int32)[:, None]
    cos_a, sin_a = unit_angles(bins * (jnp.arange(groups, dtype=jnp.int32)[None, :] - groups // 2), coarse)
    cos_c, sin_c = unit_angles(bins * jnp.arange(128, dtype=jnp.int32)[None, :], NT)
    weight = jnp.where(bins == 0, 1.0, 2.0).astype(jnp.float32)
    return weight * cos_a, weight * sin_a, cos_c, sin_c


def whiten(spectrum):
    power = jnp.mean(spectrum * spectrum, axis=-1, keepdims=True)
    return (spectrum / jnp.sqrt(power + epsilon)).astype(jnp.bfloat16)


def cross_spectrum(source_row, receivers):
    half_width = receivers.shape[-1] // 2
    source_vals = source_row.astype(jnp.float32)
    receiver_vals = receivers.astype(jnp.float32)
    src_re = source_vals[..., :half_width]
    src_im = source_vals[..., half_width:]
    rec_re = receiver_vals[..., :half_width]
    rec_im = receiver_vals[..., half_width:]
    real_part = src_re * rec_re + src_im * rec_im
    imag_part = src_re * rec_im - src_im * rec_re
    return jnp.concatenate([real_part, imag_part], axis=-1).astype(jnp.bfloat16)


PAIR_BLOCK = 256


def coherence_kernel(
    own_ref, stretch_ref, crossed_ref, wcos_ref, wsin_ref, fcos_ref, fsin_ref,
    out_ref, picks_ref, inverse_ref,
):
    minutes = crossed_ref.shape[0]
    moves = stretch_ref.shape[0] - 1
    groups = wcos_ref.shape[1]
    fine = fcos_ref.shape[1]

    @pl.when(pl.program_id(0) == 0)
    def _():
        fine_cos = fcos_ref[...]
        fine_sin = fsin_ref[...]
        for group in range(groups):
            coarse_cos = wcos_ref[:, group:group + 1]
            coarse_sin = wsin_ref[:, group:group + 1]
            lags = slice(group * fine, (group + 1) * fine)
            inverse_ref[:NF, lags] = (coarse_cos * fine_cos - coarse_sin * fine_sin).astype(
                jnp.bfloat16
            )
            inverse_ref[NF:, lags] = (-(coarse_sin * fine_cos + coarse_cos * fine_sin)).astype(
                jnp.bfloat16
            )

    @pl.when(pl.program_id(0) == 0)
    def _():
        rows = lax.broadcasted_iota(jnp.int32, (LAGS, LAGS), 0)
        for move in range(moves):
            picks_ref[:, move * LAGS:(move + 1) * LAGS] = (
                rows == stretch_ref[move + 1:move + 2, :]
            ).astype(jnp.bfloat16)

    inverse = inverse_ref[...]
    own = own_ref[0]
    stacked = None
    current = None
    for minute in range(minutes):
        correlation = jnp.dot(crossed_ref[minute], inverse, preferred_element_type=jnp.float32)
        if stacked is None:
            stacked, current = correlation, correlation
        else:
            stacked = stacked + correlation
            current = jnp.where(own == minute, correlation, current)
    high = stacked.astype(jnp.bfloat16)
    low = (stacked - high.astype(jnp.float32)).astype(jnp.bfloat16)
    rows = stacked.shape[0]
    moved = jnp.dot(
        jnp.concatenate([high, low], axis=0), picks_ref[...], preferred_element_type=jnp.float32
    )
    moved = moved[:rows] + moved[rows:]
    scale = 1.0 / LAGS
    current_power = jnp.sum(current * current, axis=1, keepdims=True) * scale
    lanes = lax.broadcasted_iota(jnp.int32, out_ref.shape, 1)
    result = jnp.zeros(out_ref.shape, jnp.float32)
    for stretch in range(moves + 1):
        if stretch == 0:
            shifted = stacked
        else:
            shifted = moved[:, (stretch - 1) * LAGS:stretch * LAGS]
        numerator = jnp.sum(current * shifted, axis=1, keepdims=True) * scale
        shifted_power = jnp.sum(shifted * shifted, axis=1, keepdims=True) * scale
        value = numerator / jnp.sqrt((current_power + epsilon) * (shifted_power + epsilon))
        result = jnp.where(lanes == stretch, value, result)
    out_ref[...] = result


def coherence(own_minute, stretch_index, crossed, factors):
    minutes, pair_count, width = crossed.shape
    stretch_count = stretch_index.shape[0]
    own = jnp.reshape(own_minute, (1,)).astype(jnp.int32)
    block = min(PAIR_BLOCK, pair_count)
    out = pl.pallas_call(
        coherence_kernel,
        grid_spec=pltpu.PrefetchScalarGridSpec(
            num_scalar_prefetch=1,
            grid=(pair_count // block,),
            in_specs=[
                pl.BlockSpec(stretch_index.shape, lambda i, own: (0, 0)),
                pl.BlockSpec((minutes, block, width), lambda i, own: (0, i, 0)),
            ] + [pl.BlockSpec(factor.shape, lambda i, own: (0, 0)) for factor in factors],
            out_specs=pl.BlockSpec((block, 128), lambda i, own: (i, 0)),
            scratch_shapes=[
                pltpu.VMEM((LAGS, (stretch_count - 1) * LAGS), jnp.bfloat16),
                pltpu.VMEM((width, LAGS), jnp.bfloat16),
            ],
        ),
        out_shape=jax.ShapeDtypeStruct((pair_count, 128), jnp.float32),
        compiler_params=pltpu.CompilerParams(
            dimension_semantics=("arbitrary",), vmem_limit_bytes=48 << 20
        ),
    )(own, stretch_index, crossed, *factors)
    return out[:, :stretch_count].T


def body(record, pairs, stretch_index):
    block_rows = record.shape[1]
    minutes = lax.axis_size("tm")
    blocks = lax.axis_size("chan")
    mirrored = lax.ppermute(record, "chan", [(s, blocks - 1 - s) for s in range(blocks)])
    pair = jnp.concatenate([record, mirrored], axis=1)
    parts = [pair]
    for shift in range(1, minutes):
        parts.append(
            lax.ppermute(pair, "tm", [(i, (i + shift) % minutes) for i in range(minutes)])
        )
    bundle = jnp.concatenate(parts, axis=0)
    from_below = lax.ppermute(bundle, "chan", [(s, s + 1) for s in range(blocks - 1)])
    from_above = lax.ppermute(bundle, "chan", [(s, s - 1) for s in range(1, blocks)])
    candidates = jnp.concatenate(
        [
            from_below[:, :block_rows],
            bundle[:, :block_rows],
            from_above[:, :block_rows],
            from_above[:, block_rows:],
            bundle[:, block_rows:],
            from_below[:, block_rows:],
        ],
        axis=1,
    )
    slot_rows = candidates.shape[1]
    spectrum = jnp.dot(
        candidates.reshape(minutes * slot_rows, NT), forward_table(),
        preferred_element_type=jnp.float32,
    )
    whitened = whiten(spectrum).reshape(minutes, slot_rows, 2 * NF)

    position = lax.axis_index("chan")
    column_index = jnp.arange(pairs.shape[1], dtype=jnp.int32)[None, :]
    is_near = column_index < pairs.shape[1] // 2
    near_slot = pairs - (position - 1) * block_rows
    far_slot = pairs - (blocks - 2 - position) * block_rows + 3 * block_rows
    slot_index = jnp.where(is_near, near_slot, far_slot)
    source_count, recv_count = slot_index.shape
    pair_count = source_count * recv_count
    sources = whitened[:, block_rows:2 * block_rows:8]
    selector = (
        slot_index.reshape(pair_count, 1) == jnp.arange(slot_rows, dtype=jnp.int32)[None, :]
    ).astype(jnp.bfloat16)
    receivers = jnp.einsum(
        "pq,mqk->mpk", selector, whitened, preferred_element_type=jnp.float32
    )
    receivers = receivers.reshape(minutes, source_count, recv_count, 2 * NF)
    crossed = cross_spectrum(sources[:, :, None, :], receivers)
    crossed = crossed.reshape(minutes, pair_count, 2 * NF)
    result = coherence(0, stretch_index, crossed, inverse_factors())
    stretch_count = stretch_index.shape[0]
    return result.reshape(1, stretch_count, source_count, recv_count)


def solution(mesh):
    return jax.shard_map(
        body,
        mesh=mesh,
        in_specs=(P("tm", "chan", None), P("chan", None), P()),
        out_specs=P("tm", None, "chan", None),
        check_vma=False,
    )
```

```python
import math

import jax
import jax.numpy as jnp
from jax import lax
from jax.experimental import pallas as pl
from jax.experimental.pallas import tpu as pltpu
from jax.sharding import PartitionSpec as P

NT = 1536
LAGS = 1024
NF = 768

epsilon = 1e-05


def unit_angles(numerators, period):
    phase = (numerators % period).astype(jnp.float32) * (2.0 * math.pi / period)
    return jnp.cos(phase), jnp.sin(phase)


def forward_table():
    coarse = NT // 128
    bins = jnp.arange(NF, dtype=jnp.int32)[None, :]
    cos_a, sin_a = unit_angles(jnp.arange(coarse, dtype=jnp.int32)[:, None] * bins, coarse)
    cos_c, sin_c = unit_angles(jnp.arange(128, dtype=jnp.int32)[:, None] * bins, NT)
    cos_t = cos_a[:, None, :] * cos_c[None] - sin_a[:, None, :] * sin_c[None]
    sin_t = sin_a[:, None, :] * cos_c[None] + cos_a[:, None, :] * sin_c[None]
    table = jnp.concatenate([cos_t, -sin_t], axis=-1).astype(jnp.bfloat16)
    return table.reshape(NT, 2 * NF)


def inverse_factors():
    coarse = NT // 128
    groups = LAGS // 128
    bins = jnp.arange(NF, dtype=jnp.int32)[:, None]
    cos_a, sin_a = unit_angles(bins * (jnp.arange(groups, dtype=jnp.int32)[None, :] - groups // 2), coarse)
    cos_c, sin_c = unit_angles(bins * jnp.arange(128, dtype=jnp.int32)[None, :], NT)
    weight = jnp.where(bins == 0, 1.0, 2.0).astype(jnp.float32)
    return weight * cos_a, weight * sin_a, cos_c, sin_c


def whiten(spectrum):
    power = jnp.mean(spectrum * spectrum, axis=-1, keepdims=True)
    return (spectrum / jnp.sqrt(power + epsilon)).astype(jnp.bfloat16)


def cross_spectrum(source_row, receivers):
    half_width = receivers.shape[-1] // 2
    source_vals = source_row.astype(jnp.float32)
    receiver_vals = receivers.astype(jnp.float32)
    src_re = source_vals[..., :half_width]
    src_im = source_vals[..., half_width:]
    rec_re = receiver_vals[..., :half_width]
    rec_im = receiver_vals[..., half_width:]
    real_part = src_re * rec_re + src_im * rec_im
    imag_part = src_re * rec_im - src_im * rec_re
    return jnp.concatenate([real_part, imag_part], axis=-1).astype(jnp.bfloat16)


PAIR_BLOCK = 256


def coherence_kernel(
    own_ref, stretch_ref, crossed_ref, wcos_ref, wsin_ref, fcos_ref, fsin_ref,
    out_ref, inverse_ref,
):
    minutes = crossed_ref.shape[0]
    moves = stretch_ref.shape[0] - 1
    groups = wcos_ref.shape[1]
    fine = fcos_ref.shape[1]

    @pl.when(pl.program_id(0) == 0)
    def _():
        fine_cos = fcos_ref[...]
        fine_sin = fsin_ref[...]
        for group in range(groups):
            coarse_cos = wcos_ref[:, group:group + 1]
            coarse_sin = wsin_ref[:, group:group + 1]
            lags = slice(group * fine, (group + 1) * fine)
            inverse_ref[:NF, lags] = (coarse_cos * fine_cos - coarse_sin * fine_sin).astype(
                jnp.bfloat16
            )
            inverse_ref[NF:, lags] = (-(coarse_sin * fine_cos + coarse_cos * fine_sin)).astype(
                jnp.bfloat16
            )

    inverse = inverse_ref[...]
    own = own_ref[0]
    stacked = None
    current = None
    for minute in range(minutes):
        correlation = jnp.dot(crossed_ref[minute], inverse, preferred_element_type=jnp.float32)
        if stacked is None:
            stacked, current = correlation, correlation
        else:
            stacked = stacked + correlation
            current = jnp.where(own == minute, correlation, current)
    high = stacked.astype(jnp.bfloat16)
    low = (stacked - high.astype(jnp.float32)).astype(jnp.bfloat16)
    rows = stacked.shape[0]
    parts = jnp.concatenate([high, low], axis=0)
    lag_rows = lax.broadcasted_iota(jnp.int32, (LAGS, LAGS), 0)
    moved = []
    for move in range(moves):
        picks = (lag_rows == stretch_ref[move + 1:move + 2, :]).astype(jnp.bfloat16)
        product = jnp.dot(parts, picks, preferred_element_type=jnp.float32)
        moved.append(product[:rows] + product[rows:])
    scale = 1.0 / LAGS
    current_power = jnp.sum(current * current, axis=1, keepdims=True) * scale
    lanes = lax.broadcasted_iota(jnp.int32, out_ref.shape, 1)
    result = jnp.zeros(out_ref.shape, jnp.float32)
    for stretch in range(moves + 1):
        if stretch == 0:
            shifted = stacked
        else:
            shifted = moved[stretch - 1]
        numerator = jnp.sum(current * shifted, axis=1, keepdims=True) * scale
        shifted_power = jnp.sum(shifted * shifted, axis=1, keepdims=True) * scale
        value = numerator / jnp.sqrt((current_power + epsilon) * (shifted_power + epsilon))
        result = jnp.where(lanes == stretch, value, result)
    out_ref[...] = result


def coherence(own_minute, stretch_index, crossed, factors):
    minutes, pair_count, width = crossed.shape
    stretch_count = stretch_index.shape[0]
    own = jnp.reshape(own_minute, (1,)).astype(jnp.int32)
    block = min(PAIR_BLOCK, pair_count)
    out = pl.pallas_call(
        coherence_kernel,
        grid_spec=pltpu.PrefetchScalarGridSpec(
            num_scalar_prefetch=1,
            grid=(pair_count // block,),
            in_specs=[
                pl.BlockSpec(stretch_index.shape, lambda i, own: (0, 0)),
                pl.BlockSpec((minutes, block, width), lambda i, own: (0, i, 0)),
            ] + [pl.BlockSpec(factor.shape, lambda i, own: (0, 0)) for factor in factors],
            out_specs=pl.BlockSpec((block, 128), lambda i, own: (i, 0)),
            scratch_shapes=[
                pltpu.VMEM((width, LAGS), jnp.bfloat16),
            ],
        ),
        out_shape=jax.ShapeDtypeStruct((pair_count, 128), jnp.float32),
        compiler_params=pltpu.CompilerParams(
            dimension_semantics=("arbitrary",), vmem_limit_bytes=48 << 20
        ),
    )(own, stretch_index, crossed, *factors)
    return out[:, :stretch_count].T


def body(record, pairs, stretch_index):
    block_rows = record.shape[1]
    minutes = lax.axis_size("tm")
    blocks = lax.axis_size("chan")
    mirrored = lax.ppermute(record, "chan", [(s, blocks - 1 - s) for s in range(blocks)])
    pair = jnp.concatenate([record, mirrored], axis=1)
    parts = [pair]
    for shift in range(1, minutes):
        parts.append(
            lax.ppermute(pair, "tm", [(i, (i + shift) % minutes) for i in range(minutes)])
        )
    bundle = jnp.concatenate(parts, axis=0)
    from_below = lax.ppermute(bundle, "chan", [(s, s + 1) for s in range(blocks - 1)])
    from_above = lax.ppermute(bundle, "chan", [(s, s - 1) for s in range(1, blocks)])
    candidates = jnp.concatenate(
        [
            from_below[:, :block_rows],
            bundle[:, :block_rows],
            from_above[:, :block_rows],
            from_above[:, block_rows:],
            bundle[:, block_rows:],
            from_below[:, block_rows:],
        ],
        axis=1,
    )
    slot_rows = candidates.shape[1]
    spectrum = jnp.dot(
        candidates.reshape(minutes * slot_rows, NT), forward_table(),
        preferred_element_type=jnp.float32,
    )
    whitened = whiten(spectrum).reshape(minutes, slot_rows, 2 * NF)

    position = lax.axis_index("chan")
    column_index = jnp.arange(pairs.shape[1], dtype=jnp.int32)[None, :]
    is_near = column_index < pairs.shape[1] // 2
    near_slot = pairs - (position - 1) * block_rows
    far_slot = pairs - (blocks - 2 - position) * block_rows + 3 * block_rows
    slot_index = jnp.where(is_near, near_slot, far_slot)
    source_count, recv_count = slot_index.shape
    pair_count = source_count * recv_count
    sources = whitened[:, block_rows:2 * block_rows:8]
    selector = (
        slot_index.reshape(pair_count, 1) == jnp.arange(slot_rows, dtype=jnp.int32)[None, :]
    ).astype(jnp.bfloat16)
    receivers = jnp.einsum(
        "pq,mqk->mpk", selector, whitened, preferred_element_type=jnp.float32
    )
    receivers = receivers.reshape(minutes, source_count, recv_count, 2 * NF)
    crossed = cross_spectrum(sources[:, :, None, :], receivers)
    crossed = crossed.reshape(minutes, pair_count, 2 * NF)
    result = coherence(0, stretch_index, crossed, inverse_factors())
    stretch_count = stretch_index.shape[0]
    return result.reshape(1, stretch_count, source_count, recv_count)


def solution(mesh):
    return jax.shard_map(
        body,
        mesh=mesh,
        in_specs=(P("tm", "chan", None), P("chan", None), P()),
        out_specs=P("tm", None, "chan", None),
        check_vma=False,
    )
```

```python
import math

import jax
import jax.numpy as jnp
from jax import lax
from jax.experimental import pallas as pl
from jax.experimental.pallas import tpu as pltpu
from jax.sharding import PartitionSpec as P

NT = 1536
LAGS = 1024
NF = 768

epsilon = 1e-05


def unit_angles(numerators, period):
    phase = (numerators % period).astype(jnp.float32) * (2.0 * math.pi / period)
    return jnp.cos(phase), jnp.sin(phase)


def forward_table():
    coarse = NT // 128
    bins = jnp.arange(NF, dtype=jnp.int32)[None, :]
    cos_a, sin_a = unit_angles(jnp.arange(coarse, dtype=jnp.int32)[:, None] * bins, coarse)
    cos_c, sin_c = unit_angles(jnp.arange(128, dtype=jnp.int32)[:, None] * bins, NT)
    cos_t = cos_a[:, None, :] * cos_c[None] - sin_a[:, None, :] * sin_c[None]
    sin_t = sin_a[:, None, :] * cos_c[None] + cos_a[:, None, :] * sin_c[None]
    table = jnp.concatenate([cos_t, -sin_t], axis=-1).astype(jnp.bfloat16)
    return table.reshape(NT, 2 * NF)


def inverse_factors():
    coarse = NT // 128
    groups = LAGS // 128
    bins = jnp.arange(NF, dtype=jnp.int32)[:, None]
    cos_a, sin_a = unit_angles(bins * (jnp.arange(groups, dtype=jnp.int32)[None, :] - groups // 2), coarse)
    cos_c, sin_c = unit_angles(bins * jnp.arange(128, dtype=jnp.int32)[None, :], NT)
    weight = jnp.where(bins == 0, 1.0, 2.0).astype(jnp.float32)
    return weight * cos_a, weight * sin_a, cos_c, sin_c


def whiten(spectrum):
    power = jnp.mean(spectrum * spectrum, axis=-1, keepdims=True)
    return (spectrum / jnp.sqrt(power + epsilon)).astype(jnp.bfloat16)


def cross_spectrum(source_row, receivers):
    half_width = receivers.shape[-1] // 2
    source_vals = source_row.astype(jnp.float32)
    receiver_vals = receivers.astype(jnp.float32)
    src_re = source_vals[..., :half_width]
    src_im = source_vals[..., half_width:]
    rec_re = receiver_vals[..., :half_width]
    rec_im = receiver_vals[..., half_width:]
    real_part = src_re * rec_re + src_im * rec_im
    imag_part = src_re * rec_im - src_im * rec_re
    return jnp.concatenate([real_part, imag_part], axis=-1).astype(jnp.bfloat16)


PAIR_BLOCK = 256


def coherence_kernel(
    own_ref, stretch_ref, crossed_ref, wcos_ref, wsin_ref, fcos_ref, fsin_ref,
    out_ref,
):
    minutes = crossed_ref.shape[0]
    moves = stretch_ref.shape[0] - 1
    groups = wcos_ref.shape[1]
    fine = fcos_ref.shape[1]

    fine_cos = fcos_ref[...]
    fine_sin = fsin_ref[...]
    own = own_ref[0]
    pieces = [[] for _ in range(minutes)]
    for pair_group in range(groups // 2):
        columns = []
        for group in (2 * pair_group, 2 * pair_group + 1):
            coarse_cos = wcos_ref[:, group:group + 1]
            coarse_sin = wsin_ref[:, group:group + 1]
            columns.append(
                jnp.concatenate(
                    [
                        coarse_cos * fine_cos - coarse_sin * fine_sin,
                        -(coarse_sin * fine_cos + coarse_cos * fine_sin),
                    ],
                    axis=0,
                ).astype(jnp.bfloat16)
            )
        inverse = jnp.concatenate(columns, axis=1)
        for minute in range(minutes):
            pieces[minute].append(
                jnp.dot(crossed_ref[minute], inverse, preferred_element_type=jnp.float32)
            )
    stacked = None
    current = None
    for minute in range(minutes):
        correlation = jnp.concatenate(pieces[minute], axis=1)
        if stacked is None:
            stacked, current = correlation, correlation
        else:
            stacked = stacked + correlation
            current = jnp.where(own == minute, correlation, current)
    high = stacked.astype(jnp.bfloat16)
    low = (stacked - high.astype(jnp.float32)).astype(jnp.bfloat16)
    rows = stacked.shape[0]
    parts = jnp.concatenate([high, low], axis=0)
    lag_rows = lax.broadcasted_iota(jnp.int32, (LAGS, LAGS), 0)
    moved = []
    for move in range(moves):
        picks = (lag_rows == stretch_ref[move + 1:move + 2, :]).astype(jnp.bfloat16)
        product = jnp.dot(parts, picks, preferred_element_type=jnp.float32)
        moved.append(product[:rows] + product[rows:])
    scale = 1.0 / LAGS
    current_power = jnp.sum(current * current, axis=1, keepdims=True) * scale
    lanes = lax.broadcasted_iota(jnp.int32, out_ref.shape, 1)
    result = jnp.zeros(out_ref.shape, jnp.float32)
    for stretch in range(moves + 1):
        if stretch == 0:
            shifted = stacked
        else:
            shifted = moved[stretch - 1]
        numerator = jnp.sum(current * shifted, axis=1, keepdims=True) * scale
        shifted_power = jnp.sum(shifted * shifted, axis=1, keepdims=True) * scale
        value = numerator / jnp.sqrt((current_power + epsilon) * (shifted_power + epsilon))
        result = jnp.where(lanes == stretch, value, result)
    out_ref[...] = result


def coherence(own_minute, stretch_index, crossed, factors):
    minutes, pair_count, width = crossed.shape
    stretch_count = stretch_index.shape[0]
    own = jnp.reshape(own_minute, (1,)).astype(jnp.int32)
    block = min(PAIR_BLOCK, pair_count)
    out = pl.pallas_call(
        coherence_kernel,
        grid_spec=pltpu.PrefetchScalarGridSpec(
            num_scalar_prefetch=1,
            grid=(pair_count // block,),
            in_specs=[
                pl.BlockSpec(stretch_index.shape, lambda i, own: (0, 0)),
                pl.BlockSpec((minutes, block, width), lambda i, own: (0, i, 0)),
            ] + [pl.BlockSpec(factor.shape, lambda i, own: (0, 0)) for factor in factors],
            out_specs=pl.BlockSpec((block, 128), lambda i, own: (i, 0)),
        ),
        out_shape=jax.ShapeDtypeStruct((pair_count, 128), jnp.float32),
        compiler_params=pltpu.CompilerParams(
            dimension_semantics=("arbitrary",), vmem_limit_bytes=48 << 20
        ),
    )(own, stretch_index, crossed, *factors)
    return out[:, :stretch_count].T


def body(record, pairs, stretch_index):
    block_rows = record.shape[1]
    minutes = lax.axis_size("tm")
    blocks = lax.axis_size("chan")
    mirrored = lax.ppermute(record, "chan", [(s, blocks - 1 - s) for s in range(blocks)])
    pair = jnp.concatenate([record, mirrored], axis=1)
    parts = [pair]
    for shift in range(1, minutes):
        parts.append(
            lax.ppermute(pair, "tm", [(i, (i + shift) % minutes) for i in range(minutes)])
        )
    bundle = jnp.concatenate(parts, axis=0)
    from_below = lax.ppermute(bundle, "chan", [(s, s + 1) for s in range(blocks - 1)])
    from_above = lax.ppermute(bundle, "chan", [(s, s - 1) for s in range(1, blocks)])
    candidates = jnp.concatenate(
        [
            from_below[:, :block_rows],
            bundle[:, :block_rows],
            from_above[:, :block_rows],
            from_above[:, block_rows:],
            bundle[:, block_rows:],
            from_below[:, block_rows:],
        ],
        axis=1,
    )
    slot_rows = candidates.shape[1]
    spectrum = jnp.dot(
        candidates.reshape(minutes * slot_rows, NT), forward_table(),
        preferred_element_type=jnp.float32,
    )
    whitened = whiten(spectrum).reshape(minutes, slot_rows, 2 * NF)

    position = lax.axis_index("chan")
    column_index = jnp.arange(pairs.shape[1], dtype=jnp.int32)[None, :]
    is_near = column_index < pairs.shape[1] // 2
    near_slot = pairs - (position - 1) * block_rows
    far_slot = pairs - (blocks - 2 - position) * block_rows + 3 * block_rows
    slot_index = jnp.where(is_near, near_slot, far_slot)
    source_count, recv_count = slot_index.shape
    pair_count = source_count * recv_count
    sources = whitened[:, block_rows:2 * block_rows:8]
    selector = (
        slot_index.reshape(pair_count, 1) == jnp.arange(slot_rows, dtype=jnp.int32)[None, :]
    ).astype(jnp.bfloat16)
    receivers = jnp.einsum(
        "pq,mqk->mpk", selector, whitened, preferred_element_type=jnp.float32
    )
    receivers = receivers.reshape(minutes, source_count, recv_count, 2 * NF)
    crossed = cross_spectrum(sources[:, :, None, :], receivers)
    crossed = crossed.reshape(minutes, pair_count, 2 * NF)
    result = coherence(0, stretch_index, crossed, inverse_factors())
    stretch_count = stretch_index.shape[0]
    return result.reshape(1, stretch_count, source_count, recv_count)


def solution(mesh):
    return jax.shard_map(
        body,
        mesh=mesh,
        in_specs=(P("tm", "chan", None), P("chan", None), P()),
        out_specs=P("tm", None, "chan", None),
        check_vma=False,
    )
```

```python
import functools
import math

import jax
import jax.numpy as jnp
from jax import lax
from jax.experimental import pallas as pl
from jax.experimental.pallas import tpu as pltpu
from jax.sharding import PartitionSpec as P

NT = 1536
LAGS = 1024
NF = 768

epsilon = 1e-05


def unit_angles(numerators, period):
    phase = (numerators % period).astype(jnp.float32) * (2.0 * math.pi / period)
    return jnp.cos(phase), jnp.sin(phase)


def forward_table():
    coarse = NT // 128
    bins = jnp.arange(NF, dtype=jnp.int32)[None, :]
    cos_a, sin_a = unit_angles(jnp.arange(coarse, dtype=jnp.int32)[:, None] * bins, coarse)
    cos_c, sin_c = unit_angles(jnp.arange(128, dtype=jnp.int32)[:, None] * bins, NT)
    cos_t = cos_a[:, None, :] * cos_c[None] - sin_a[:, None, :] * sin_c[None]
    sin_t = sin_a[:, None, :] * cos_c[None] + cos_a[:, None, :] * sin_c[None]
    table = jnp.concatenate([cos_t, -sin_t], axis=-1).astype(jnp.bfloat16)
    return table.reshape(NT, 2 * NF)


def inverse_factors():
    coarse = NT // 128
    groups = LAGS // 128
    bins = jnp.arange(NF, dtype=jnp.int32)[:, None]
    cos_a, sin_a = unit_angles(bins * (jnp.arange(groups, dtype=jnp.int32)[None, :] - groups // 2), coarse)
    cos_c, sin_c = unit_angles(bins * jnp.arange(128, dtype=jnp.int32)[None, :], NT)
    weight = jnp.where(bins == 0, 1.0, 2.0).astype(jnp.float32)
    return weight * cos_a, weight * sin_a, cos_c, sin_c


def whiten(spectrum):
    power = jnp.mean(spectrum * spectrum, axis=-1, keepdims=True)
    return (spectrum / jnp.sqrt(power + epsilon)).astype(jnp.bfloat16)


def cross_spectrum(source_row, receivers):
    half_width = receivers.shape[-1] // 2
    source_vals = source_row.astype(jnp.float32)
    receiver_vals = receivers.astype(jnp.float32)
    src_re = source_vals[..., :half_width]
    src_im = source_vals[..., half_width:]
    rec_re = receiver_vals[..., :half_width]
    rec_im = receiver_vals[..., half_width:]
    real_part = src_re * rec_re + src_im * rec_im
    imag_part = src_re * rec_im - src_im * rec_re
    return jnp.concatenate([real_part, imag_part], axis=-1).astype(jnp.bfloat16)


PAIR_BLOCK = 256


def coherence_kernel(
    own_ref, stretch_ref, crossed_ref, wcos_ref, wsin_ref, fcos_ref, fsin_ref,
    out_ref, inverse_ref,
):
    minutes = crossed_ref.shape[0]
    moves = stretch_ref.shape[0] - 1
    groups = wcos_ref.shape[1]
    fine = fcos_ref.shape[1]

    @pl.when(pl.program_id(0) == 0)
    def _():
        fine_cos = fcos_ref[...]
        fine_sin = fsin_ref[...]
        for group in range(groups):
            coarse_cos = wcos_ref[:, group:group + 1]
            coarse_sin = wsin_ref[:, group:group + 1]
            lags = slice(group * fine, (group + 1) * fine)
            inverse_ref[:NF, lags] = (coarse_cos * fine_cos - coarse_sin * fine_sin).astype(
                jnp.bfloat16
            )
            inverse_ref[NF:, lags] = (-(coarse_sin * fine_cos + coarse_cos * fine_sin)).astype(
                jnp.bfloat16
            )

    inverse = inverse_ref[...]
    own = own_ref[0]
    stacked = None
    current = None
    for minute in range(minutes):
        correlation = jnp.dot(crossed_ref[minute], inverse, preferred_element_type=jnp.float32)
        if stacked is None:
            stacked, current = correlation, correlation
        else:
            stacked = stacked + correlation
            current = jnp.where(own == minute, correlation, current)
    high = stacked.astype(jnp.bfloat16)
    low = (stacked - high.astype(jnp.float32)).astype(jnp.bfloat16)
    rows = stacked.shape[0]
    parts = jnp.concatenate([high, low], axis=0)
    lag_rows = lax.broadcasted_iota(jnp.int32, (LAGS, LAGS), 0)
    moved = []
    for move in range(moves):
        picks = (lag_rows == stretch_ref[move + 1:move + 2, :]).astype(jnp.bfloat16)
        product = jnp.dot(parts, picks, preferred_element_type=jnp.float32)
        moved.append(product[:rows] + product[rows:])
    scale = 1.0 / LAGS
    current_power = jnp.sum(current * current, axis=1, keepdims=True) * scale
    lanes = lax.broadcasted_iota(jnp.int32, out_ref.shape, 1)
    result = jnp.zeros(out_ref.shape, jnp.float32)
    for stretch in range(moves + 1):
        if stretch == 0:
            shifted = stacked
        else:
            shifted = moved[stretch - 1]
        numerator = jnp.sum(current * shifted, axis=1, keepdims=True) * scale
        shifted_power = jnp.sum(shifted * shifted, axis=1, keepdims=True) * scale
        value = numerator / jnp.sqrt((current_power + epsilon) * (shifted_power + epsilon))
        result = jnp.where(lanes == stretch, value, result)
    out_ref[...] = result


def coherence(own_minute, stretch_index, crossed, factors):
    minutes, pair_count, width = crossed.shape
    stretch_count = stretch_index.shape[0]
    own = jnp.reshape(own_minute, (1,)).astype(jnp.int32)
    block = min(PAIR_BLOCK, pair_count)
    out = pl.pallas_call(
        coherence_kernel,
        grid_spec=pltpu.PrefetchScalarGridSpec(
            num_scalar_prefetch=1,
            grid=(pair_count // block,),
            in_specs=[
                pl.BlockSpec(stretch_index.shape, lambda i, own: (0, 0)),
                pl.BlockSpec((minutes, block, width), lambda i, own: (0, i, 0)),
            ] + [pl.BlockSpec(factor.shape, lambda i, own: (0, 0)) for factor in factors],
            out_specs=pl.BlockSpec((block, 128), lambda i, own: (i, 0)),
            scratch_shapes=[
                pltpu.VMEM((width, LAGS), jnp.bfloat16),
            ],
        ),
        out_shape=jax.ShapeDtypeStruct((pair_count, 128), jnp.float32),
        compiler_params=pltpu.CompilerParams(
            dimension_semantics=("arbitrary",), vmem_limit_bytes=48 << 20
        ),
    )(own, stretch_index, crossed, *factors)
    return out[:, :stretch_count].T


def body(axis_order, record, pairs, stretch_index):
    block_rows = record.shape[1]
    minutes = lax.axis_size("tm")
    blocks = lax.axis_size("chan")
    def linear(t, b):
        return t * blocks + b if axis_order[0] == "tm" else b * minutes + t

    parts = []
    for shift in range(minutes):
        if shift == 0:
            own = record
        else:
            own = lax.ppermute(record, "tm", [(i, (i + shift) % minutes) for i in range(minutes)])
        route = [
            (linear(t, b), linear((t + shift) % minutes, blocks - 1 - b))
            for t in range(minutes)
            for b in range(blocks)
        ]
        mirrored = lax.ppermute(record, axis_order, route)
        parts.append(jnp.concatenate([own, mirrored], axis=1))
    bundle = jnp.concatenate(parts, axis=0)
    from_below = lax.ppermute(bundle, "chan", [(s, s + 1) for s in range(blocks - 1)])
    from_above = lax.ppermute(bundle, "chan", [(s, s - 1) for s in range(1, blocks)])
    candidates = jnp.concatenate(
        [
            from_below[:, :block_rows],
            bundle[:, :block_rows],
            from_above[:, :block_rows],
            from_above[:, block_rows:],
            bundle[:, block_rows:],
            from_below[:, block_rows:],
        ],
        axis=1,
    )
    slot_rows = candidates.shape[1]
    spectrum = jnp.dot(
        candidates.reshape(minutes * slot_rows, NT), forward_table(),
        preferred_element_type=jnp.float32,
    )
    whitened = whiten(spectrum).reshape(minutes, slot_rows, 2 * NF)

    position = lax.axis_index("chan")
    column_index = jnp.arange(pairs.shape[1], dtype=jnp.int32)[None, :]
    is_near = column_index < pairs.shape[1] // 2
    near_slot = pairs - (position - 1) * block_rows
    far_slot = pairs - (blocks - 2 - position) * block_rows + 3 * block_rows
    slot_index = jnp.where(is_near, near_slot, far_slot)
    source_count, recv_count = slot_index.shape
    pair_count = source_count * recv_count
    sources = whitened[:, block_rows:2 * block_rows:8]
    selector = (
        slot_index.reshape(pair_count, 1) == jnp.arange(slot_rows, dtype=jnp.int32)[None, :]
    ).astype(jnp.bfloat16)
    receivers = jnp.einsum(
        "pq,mqk->mpk", selector, whitened, preferred_element_type=jnp.float32
    )
    receivers = receivers.reshape(minutes, source_count, recv_count, 2 * NF)
    crossed = cross_spectrum(sources[:, :, None, :], receivers)
    crossed = crossed.reshape(minutes, pair_count, 2 * NF)
    result = coherence(0, stretch_index, crossed, inverse_factors())
    stretch_count = stretch_index.shape[0]
    return result.reshape(1, stretch_count, source_count, recv_count)


def solution(mesh):
    axis_order = tuple(name for name in mesh.axis_names if name in ("tm", "chan"))
    return jax.shard_map(
        functools.partial(body, axis_order),
        mesh=mesh,
        in_specs=(P("tm", "chan", None), P("chan", None), P()),
        out_specs=P("tm", None, "chan", None),
        check_vma=False,
    )
```

```python
import functools
import math

import jax
import jax.numpy as jnp
from jax import lax
from jax.experimental import pallas as pl
from jax.experimental.pallas import tpu as pltpu
from jax.sharding import PartitionSpec as P

NT = 1536
LAGS = 1024
NF = 768

epsilon = 1e-05


def unit_angles(numerators, period):
    phase = (numerators % period).astype(jnp.float32) * (2.0 * math.pi / period)
    return jnp.cos(phase), jnp.sin(phase)


def forward_table():
    coarse = NT // 128
    bins = jnp.arange(NF, dtype=jnp.int32)[None, :]
    cos_a, sin_a = unit_angles(jnp.arange(coarse, dtype=jnp.int32)[:, None] * bins, coarse)
    cos_1, sin_1 = unit_angles(jnp.arange(16, dtype=jnp.int32)[:, None] * bins, NT // 8)
    cos_2, sin_2 = unit_angles(jnp.arange(8, dtype=jnp.int32)[:, None] * bins, NT)
    cos_c = (cos_1[:, None] * cos_2[None] - sin_1[:, None] * sin_2[None]).reshape(128, NF)
    sin_c = (sin_1[:, None] * cos_2[None] + cos_1[:, None] * sin_2[None]).reshape(128, NF)
    cos_t = cos_a[:, None, :] * cos_c[None] - sin_a[:, None, :] * sin_c[None]
    sin_t = sin_a[:, None, :] * cos_c[None] + cos_a[:, None, :] * sin_c[None]
    table = jnp.concatenate([cos_t, -sin_t], axis=-1).astype(jnp.bfloat16)
    return table.reshape(NT, 2 * NF)


def inverse_factors():
    coarse = NT // 128
    groups = LAGS // 128
    bins = jnp.arange(NF, dtype=jnp.int32)[:, None]
    cos_a, sin_a = unit_angles(bins * (jnp.arange(groups, dtype=jnp.int32)[None, :] - groups // 2), coarse)
    cos_c, sin_c = unit_angles(bins * jnp.arange(128, dtype=jnp.int32)[None, :], NT)
    weight = jnp.where(bins == 0, 1.0, 2.0).astype(jnp.float32)
    return weight * cos_a, weight * sin_a, cos_c, sin_c


def whiten(spectrum):
    power = jnp.mean(spectrum * spectrum, axis=-1, keepdims=True)
    return (spectrum / jnp.sqrt(power + epsilon)).astype(jnp.bfloat16)


def cross_spectrum(source_row, receivers):
    half_width = receivers.shape[-1] // 2
    source_vals = source_row.astype(jnp.float32)
    receiver_vals = receivers.astype(jnp.float32)
    src_re = source_vals[..., :half_width]
    src_im = source_vals[..., half_width:]
    rec_re = receiver_vals[..., :half_width]
    rec_im = receiver_vals[..., half_width:]
    real_part = src_re * rec_re + src_im * rec_im
    imag_part = src_re * rec_im - src_im * rec_re
    return jnp.concatenate([real_part, imag_part], axis=-1).astype(jnp.bfloat16)


PAIR_BLOCK = 256


def coherence_kernel(
    own_ref, stretch_ref, crossed_ref, wcos_ref, wsin_ref, fcos_ref, fsin_ref,
    out_ref, inverse_ref,
):
    minutes = crossed_ref.shape[0]
    moves = stretch_ref.shape[0] - 1
    groups = wcos_ref.shape[1]
    fine = fcos_ref.shape[1]

    @pl.when(pl.program_id(0) == 0)
    def _():
        fine_cos = fcos_ref[...]
        fine_sin = fsin_ref[...]
        for group in range(groups):
            coarse_cos = wcos_ref[:, group:group + 1]
            coarse_sin = wsin_ref[:, group:group + 1]
            lags = slice(group * fine, (group + 1) * fine)
            inverse_ref[:NF, lags] = (coarse_cos * fine_cos - coarse_sin * fine_sin).astype(
                jnp.bfloat16
            )
            inverse_ref[NF:, lags] = (-(coarse_sin * fine_cos + coarse_cos * fine_sin)).astype(
                jnp.bfloat16
            )

    inverse = inverse_ref[...]
    own = own_ref[0]
    stacked = None
    current = None
    for minute in range(minutes):
        correlation = jnp.dot(crossed_ref[minute], inverse, preferred_element_type=jnp.float32)
        if stacked is None:
            stacked, current = correlation, correlation
        else:
            stacked = stacked + correlation
            current = jnp.where(own == minute, correlation, current)
    high = stacked.astype(jnp.bfloat16)
    low = (stacked - high.astype(jnp.float32)).astype(jnp.bfloat16)
    rows = stacked.shape[0]
    parts = jnp.concatenate([high, low], axis=0)
    lag_rows = lax.broadcasted_iota(jnp.int32, (LAGS, LAGS), 0)
    moved = []
    for move in range(moves):
        picks = (lag_rows == stretch_ref[move + 1:move + 2, :]).astype(jnp.bfloat16)
        product = jnp.dot(parts, picks, preferred_element_type=jnp.float32)
        moved.append(product[:rows] + product[rows:])
    scale = 1.0 / LAGS
    current_power = jnp.sum(current * current, axis=1, keepdims=True) * scale
    lanes = lax.broadcasted_iota(jnp.int32, out_ref.shape, 1)
    result = jnp.zeros(out_ref.shape, jnp.float32)
    for stretch in range(moves + 1):
        if stretch == 0:
            shifted = stacked
        else:
            shifted = moved[stretch - 1]
        numerator = jnp.sum(current * shifted, axis=1, keepdims=True) * scale
        shifted_power = jnp.sum(shifted * shifted, axis=1, keepdims=True) * scale
        value = numerator / jnp.sqrt((current_power + epsilon) * (shifted_power + epsilon))
        result = jnp.where(lanes == stretch, value, result)
    out_ref[...] = result


def coherence(own_minute, stretch_index, crossed, factors):
    minutes, pair_count, width = crossed.shape
    stretch_count = stretch_index.shape[0]
    own = jnp.reshape(own_minute, (1,)).astype(jnp.int32)
    block = min(PAIR_BLOCK, pair_count)
    out = pl.pallas_call(
        coherence_kernel,
        grid_spec=pltpu.PrefetchScalarGridSpec(
            num_scalar_prefetch=1,
            grid=(pair_count // block,),
            in_specs=[
                pl.BlockSpec(stretch_index.shape, lambda i, own: (0, 0)),
                pl.BlockSpec((minutes, block, width), lambda i, own: (0, i, 0)),
            ] + [pl.BlockSpec(factor.shape, lambda i, own: (0, 0)) for factor in factors],
            out_specs=pl.BlockSpec((block, 128), lambda i, own: (i, 0)),
            scratch_shapes=[
                pltpu.VMEM((width, LAGS), jnp.bfloat16),
            ],
        ),
        out_shape=jax.ShapeDtypeStruct((pair_count, 128), jnp.float32),
        compiler_params=pltpu.CompilerParams(
            dimension_semantics=("arbitrary",), vmem_limit_bytes=48 << 20
        ),
    )(own, stretch_index, crossed, *factors)
    return out[:, :stretch_count].T


def body(axis_order, record, pairs, stretch_index):
    block_rows = record.shape[1]
    minutes = lax.axis_size("tm")
    blocks = lax.axis_size("chan")
    def linear(t, b):
        return t * blocks + b if axis_order[0] == "tm" else b * minutes + t

    parts = []
    for shift in range(minutes):
        if shift == 0:
            own = record
        else:
            own = lax.ppermute(record, "tm", [(i, (i + shift) % minutes) for i in range(minutes)])
        route = [
            (linear(t, b), linear((t + shift) % minutes, blocks - 1 - b))
            for t in range(minutes)
            for b in range(blocks)
        ]
        mirrored = lax.ppermute(record, axis_order, route)
        parts.append(jnp.concatenate([own, mirrored], axis=1))
    bundle = jnp.concatenate(parts, axis=0)
    from_below = lax.ppermute(bundle, "chan", [(s, s + 1) for s in range(blocks - 1)])
    from_above = lax.ppermute(bundle, "chan", [(s, s - 1) for s in range(1, blocks)])
    candidates = jnp.concatenate(
        [
            from_below[:, :block_rows],
            bundle[:, :block_rows],
            from_above[:, :block_rows],
            from_above[:, block_rows:],
            bundle[:, block_rows:],
            from_below[:, block_rows:],
        ],
        axis=1,
    )
    slot_rows = candidates.shape[1]
    spectrum = jnp.dot(
        candidates.reshape(minutes * slot_rows, NT), forward_table(),
        preferred_element_type=jnp.float32,
    )
    whitened = whiten(spectrum).reshape(minutes, slot_rows, 2 * NF)

    position = lax.axis_index("chan")
    column_index = jnp.arange(pairs.shape[1], dtype=jnp.int32)[None, :]
    is_near = column_index < pairs.shape[1] // 2
    near_slot = pairs - (position - 1) * block_rows
    far_slot = pairs - (blocks - 2 - position) * block_rows + 3 * block_rows
    slot_index = jnp.where(is_near, near_slot, far_slot)
    source_count, recv_count = slot_index.shape
    pair_count = source_count * recv_count
    sources = whitened[:, block_rows:2 * block_rows:8]
    selector = (
        slot_index.reshape(pair_count, 1) == jnp.arange(slot_rows, dtype=jnp.int32)[None, :]
    ).astype(jnp.bfloat16)
    receivers = jnp.einsum(
        "pq,mqk->mpk", selector, whitened, preferred_element_type=jnp.float32
    )
    receivers = receivers.reshape(minutes, source_count, recv_count, 2 * NF)
    crossed = cross_spectrum(sources[:, :, None, :], receivers)
    crossed = crossed.reshape(minutes, pair_count, 2 * NF)
    result = coherence(0, stretch_index, crossed, inverse_factors())
    stretch_count = stretch_index.shape[0]
    return result.reshape(1, stretch_count, source_count, recv_count)


def solution(mesh):
    axis_order = tuple(name for name in mesh.axis_names if name in ("tm", "chan"))
    return jax.shard_map(
        functools.partial(body, axis_order),
        mesh=mesh,
        in_specs=(P("tm", "chan", None), P("chan", None), P()),
        out_specs=P("tm", None, "chan", None),
        check_vma=False,
    )
```

```python
import functools
import math

import jax
import jax.numpy as jnp
from jax import lax
from jax.experimental import pallas as pl
from jax.experimental.pallas import tpu as pltpu
from jax.sharding import PartitionSpec as P

NT = 1536
LAGS = 1024
NF = 768

epsilon = 1e-05


def unit_angles(numerators, period):
    phase = (numerators % period).astype(jnp.float32) * (2.0 * math.pi / period)
    return jnp.cos(phase), jnp.sin(phase)


def forward_table():
    coarse = NT // 128
    bins = jnp.arange(NF, dtype=jnp.int32)[None, :]
    cos_a, sin_a = unit_angles(jnp.arange(coarse, dtype=jnp.int32)[:, None] * bins, coarse)
    cos_c, sin_c = unit_angles(jnp.arange(128, dtype=jnp.int32)[:, None] * bins, NT)
    cos_t = cos_a[:, None, :] * cos_c[None] - sin_a[:, None, :] * sin_c[None]
    sin_t = sin_a[:, None, :] * cos_c[None] + cos_a[:, None, :] * sin_c[None]
    table = jnp.concatenate([cos_t, -sin_t], axis=-1).astype(jnp.bfloat16)
    return table.reshape(NT, 2 * NF)


def inverse_factors():
    coarse = NT // 128
    groups = LAGS // 128
    bins = jnp.arange(NF, dtype=jnp.int32)[:, None]
    cos_a, sin_a = unit_angles(bins * (jnp.arange(groups, dtype=jnp.int32)[None, :] - groups // 2), coarse)
    cos_c, sin_c = unit_angles(bins * jnp.arange(128, dtype=jnp.int32)[None, :], NT)
    weight = jnp.where(bins == 0, 1.0, 2.0).astype(jnp.float32)
    return weight * cos_a, weight * sin_a, cos_c, sin_c


def whiten(spectrum):
    power = jnp.mean(spectrum * spectrum, axis=-1, keepdims=True)
    return (spectrum / jnp.sqrt(power + epsilon)).astype(jnp.bfloat16)


def cross_spectrum(source_row, receivers):
    half_width = receivers.shape[-1] // 2
    source_vals = source_row.astype(jnp.float32)
    receiver_vals = receivers.astype(jnp.float32)
    src_re = source_vals[..., :half_width]
    src_im = source_vals[..., half_width:]
    rec_re = receiver_vals[..., :half_width]
    rec_im = receiver_vals[..., half_width:]
    real_part = src_re * rec_re + src_im * rec_im
    imag_part = src_re * rec_im - src_im * rec_re
    return jnp.concatenate([real_part, imag_part], axis=-1).astype(jnp.bfloat16)


PAIR_BLOCK = 256


def coherence_kernel(
    own_ref, stretch_ref, crossed_ref, wcos_ref, wsin_ref, fcos_ref, fsin_ref,
    out_ref, inverse_ref,
):
    minutes = crossed_ref.shape[0]
    moves = stretch_ref.shape[0] - 1
    groups = wcos_ref.shape[1]
    fine = fcos_ref.shape[1]

    @pl.when(pl.program_id(0) == 0)
    def _():
        fine_cos = fcos_ref[...]
        fine_sin = fsin_ref[...]
        for group in range(groups):
            coarse_cos = wcos_ref[:, group:group + 1]
            coarse_sin = wsin_ref[:, group:group + 1]
            lags = slice(group * fine, (group + 1) * fine)
            inverse_ref[:NF, lags] = (coarse_cos * fine_cos - coarse_sin * fine_sin).astype(
                jnp.bfloat16
            )
            inverse_ref[NF:, lags] = (-(coarse_sin * fine_cos + coarse_cos * fine_sin)).astype(
                jnp.bfloat16
            )

    inverse = inverse_ref[...]
    own = own_ref[0]
    stacked = None
    current = None
    for minute in range(minutes):
        correlation = jnp.dot(crossed_ref[minute], inverse, preferred_element_type=jnp.float32)
        if stacked is None:
            stacked, current = correlation, correlation
        else:
            stacked = stacked + correlation
            current = jnp.where(own == minute, correlation, current)
    high = stacked.astype(jnp.bfloat16)
    low = (stacked - high.astype(jnp.float32)).astype(jnp.bfloat16)
    rows = stacked.shape[0]
    parts = jnp.concatenate([high, low], axis=0)
    lag_rows = lax.broadcasted_iota(jnp.int32, (LAGS, LAGS), 0)
    moved = []
    for move in range(moves):
        picks = (lag_rows == stretch_ref[move + 1:move + 2, :]).astype(jnp.bfloat16)
        product = jnp.dot(parts, picks, preferred_element_type=jnp.float32)
        moved.append(product[:rows] + product[rows:])
    scale = 1.0 / LAGS
    current_power = jnp.sum(current * current, axis=1, keepdims=True) * scale
    lanes = lax.broadcasted_iota(jnp.int32, out_ref.shape, 1)
    result = jnp.zeros(out_ref.shape, jnp.float32)
    for stretch in range(moves + 1):
        if stretch == 0:
            shifted = stacked
        else:
            shifted = moved[stretch - 1]
        numerator = jnp.sum(current * shifted, axis=1, keepdims=True) * scale
        shifted_power = jnp.sum(shifted * shifted, axis=1, keepdims=True) * scale
        value = numerator / jnp.sqrt((current_power + epsilon) * (shifted_power + epsilon))
        result = jnp.where(lanes == stretch, value, result)
    out_ref[...] = result


def coherence(own_minute, stretch_index, crossed, factors):
    minutes, pair_count, width = crossed.shape
    stretch_count = stretch_index.shape[0]
    own = jnp.reshape(own_minute, (1,)).astype(jnp.int32)
    block = min(PAIR_BLOCK, pair_count)
    out = pl.pallas_call(
        coherence_kernel,
        grid_spec=pltpu.PrefetchScalarGridSpec(
            num_scalar_prefetch=1,
            grid=(pair_count // block,),
            in_specs=[
                pl.BlockSpec(stretch_index.shape, lambda i, own: (0, 0)),
                pl.BlockSpec((minutes, block, width), lambda i, own: (0, i, 0)),
            ] + [pl.BlockSpec(factor.shape, lambda i, own: (0, 0)) for factor in factors],
            out_specs=pl.BlockSpec((block, 128), lambda i, own: (i, 0)),
            scratch_shapes=[
                pltpu.VMEM((width, LAGS), jnp.bfloat16),
            ],
        ),
        out_shape=jax.ShapeDtypeStruct((pair_count, 128), jnp.float32),
        compiler_params=pltpu.CompilerParams(
            dimension_semantics=("arbitrary",), vmem_limit_bytes=48 << 20
        ),
    )(own, stretch_index, crossed, *factors)
    return out[:, :stretch_count].T


def body(axis_order, record, pairs, stretch_index):
    block_rows = record.shape[1]
    minutes = lax.axis_size("tm")
    blocks = lax.axis_size("chan")
    def linear(t, b):
        return t * blocks + b if axis_order[0] == "tm" else b * minutes + t

    parts = []
    for shift in range(minutes):
        if shift == 0:
            own = record
        else:
            own = lax.ppermute(record, "tm", [(i, (i + shift) % minutes) for i in range(minutes)])
        route = [
            (linear(t, b), linear((t + shift) % minutes, blocks - 1 - b))
            for t in range(minutes)
            for b in range(blocks)
        ]
        mirrored = lax.ppermute(record, axis_order, route)
        parts.append(jnp.concatenate([own, mirrored], axis=1))
    bundle = jnp.concatenate(parts, axis=0)
    from_below = lax.ppermute(bundle, "chan", [(s, s + 1) for s in range(blocks - 1)])
    from_above = lax.ppermute(bundle, "chan", [(s, s - 1) for s in range(1, blocks)])
    forward = forward_table()

    def spectra(rows):
        count = rows.shape[1]
        spectrum = jnp.dot(
            rows.reshape(minutes * count, NT), forward, preferred_element_type=jnp.float32
        )
        return whiten(spectrum).reshape(minutes, count, 2 * NF)

    local = spectra(bundle)
    below_rows = spectra(from_below)
    above_rows = spectra(from_above)
    whitened = jnp.concatenate(
        [
            below_rows[:, :block_rows],
            local[:, :block_rows],
            above_rows[:, :block_rows],
            above_rows[:, block_rows:],
            local[:, block_rows:],
            below_rows[:, block_rows:],
        ],
        axis=1,
    )
    slot_rows = whitened.shape[1]

    position = lax.axis_index("chan")
    column_index = jnp.arange(pairs.shape[1], dtype=jnp.int32)[None, :]
    is_near = column_index < pairs.shape[1] // 2
    near_slot = pairs - (position - 1) * block_rows
    far_slot = pairs - (blocks - 2 - position) * block_rows + 3 * block_rows
    slot_index = jnp.where(is_near, near_slot, far_slot)
    source_count, recv_count = slot_index.shape
    pair_count = source_count * recv_count
    sources = whitened[:, block_rows:2 * block_rows:8]
    selector = (
        slot_index.reshape(pair_count, 1) == jnp.arange(slot_rows, dtype=jnp.int32)[None, :]
    ).astype(jnp.bfloat16)
    receivers = jnp.einsum(
        "pq,mqk->mpk", selector, whitened, preferred_element_type=jnp.float32
    )
    receivers = receivers.reshape(minutes, source_count, recv_count, 2 * NF)
    crossed = cross_spectrum(sources[:, :, None, :], receivers)
    crossed = crossed.reshape(minutes, pair_count, 2 * NF)
    result = coherence(0, stretch_index, crossed, inverse_factors())
    stretch_count = stretch_index.shape[0]
    return result.reshape(1, stretch_count, source_count, recv_count)


def solution(mesh):
    axis_order = tuple(name for name in mesh.axis_names if name in ("tm", "chan"))
    return jax.shard_map(
        functools.partial(body, axis_order),
        mesh=mesh,
        in_specs=(P("tm", "chan", None), P("chan", None), P()),
        out_specs=P("tm", None, "chan", None),
        check_vma=False,
    )
```

```python
import functools
import math

import jax
import jax.numpy as jnp
from jax import lax
from jax.experimental import pallas as pl
from jax.experimental.pallas import tpu as pltpu
from jax.sharding import PartitionSpec as P

NT = 1536
LAGS = 1024
NF = 768

epsilon = 1e-05


def unit_angles(numerators, period):
    phase = (numerators % period).astype(jnp.float32) * (2.0 * math.pi / period)
    return jnp.cos(phase), jnp.sin(phase)


def forward_table():
    coarse = NT // 128
    bins = jnp.arange(NF, dtype=jnp.int32)[None, :]
    cos_a, sin_a = unit_angles(jnp.arange(coarse, dtype=jnp.int32)[:, None] * bins, coarse)
    cos_c, sin_c = unit_angles(jnp.arange(128, dtype=jnp.int32)[:, None] * bins, NT)
    cos_t = cos_a[:, None, :] * cos_c[None] - sin_a[:, None, :] * sin_c[None]
    sin_t = sin_a[:, None, :] * cos_c[None] + cos_a[:, None, :] * sin_c[None]
    table = jnp.concatenate([cos_t, -sin_t], axis=-1).astype(jnp.bfloat16)
    return table.reshape(NT, 2 * NF)


def inverse_factors():
    coarse = NT // 128
    groups = LAGS // 128
    bins = jnp.arange(NF, dtype=jnp.int32)[:, None]
    cos_a, sin_a = unit_angles(bins * (jnp.arange(groups, dtype=jnp.int32)[None, :] - groups // 2), coarse)
    cos_c, sin_c = unit_angles(bins * jnp.arange(128, dtype=jnp.int32)[None, :], NT)
    weight = jnp.where(bins == 0, 1.0, 2.0).astype(jnp.float32)
    return weight * cos_a, weight * sin_a, cos_c, sin_c


def whiten(spectrum):
    power = jnp.mean(spectrum * spectrum, axis=-1, keepdims=True)
    return (spectrum / jnp.sqrt(power + epsilon)).astype(jnp.bfloat16)


def cross_spectrum(source_row, receivers):
    half_width = receivers.shape[-1] // 2
    source_vals = source_row.astype(jnp.float32)
    receiver_vals = receivers.astype(jnp.float32)
    src_re = source_vals[..., :half_width]
    src_im = source_vals[..., half_width:]
    rec_re = receiver_vals[..., :half_width]
    rec_im = receiver_vals[..., half_width:]
    real_part = src_re * rec_re + src_im * rec_im
    imag_part = src_re * rec_im - src_im * rec_re
    return jnp.concatenate([real_part, imag_part], axis=-1).astype(jnp.bfloat16)


PAIR_BLOCK = 512


def coherence_kernel(
    own_ref, stretch_ref, crossed_ref, wcos_ref, wsin_ref, fcos_ref, fsin_ref,
    out_ref, inverse_ref,
):
    minutes = crossed_ref.shape[0]
    moves = stretch_ref.shape[0] - 1
    groups = wcos_ref.shape[1]
    fine = fcos_ref.shape[1]

    @pl.when(pl.program_id(0) == 0)
    def _():
        fine_cos = fcos_ref[...]
        fine_sin = fsin_ref[...]
        for group in range(groups):
            coarse_cos = wcos_ref[:, group:group + 1]
            coarse_sin = wsin_ref[:, group:group + 1]
            lags = slice(group * fine, (group + 1) * fine)
            inverse_ref[:NF, lags] = (coarse_cos * fine_cos - coarse_sin * fine_sin).astype(
                jnp.bfloat16
            )
            inverse_ref[NF:, lags] = (-(coarse_sin * fine_cos + coarse_cos * fine_sin)).astype(
                jnp.bfloat16
            )

    inverse = inverse_ref[...]
    own = own_ref[0]
    stacked = None
    current = None
    for minute in range(minutes):
        correlation = jnp.dot(crossed_ref[minute], inverse, preferred_element_type=jnp.float32)
        if stacked is None:
            stacked, current = correlation, correlation
        else:
            stacked = stacked + correlation
            current = jnp.where(own == minute, correlation, current)
    high = stacked.astype(jnp.bfloat16)
    low = (stacked - high.astype(jnp.float32)).astype(jnp.bfloat16)
    rows = stacked.shape[0]
    parts = jnp.concatenate([high, low], axis=0)
    lag_rows = lax.broadcasted_iota(jnp.int32, (LAGS, LAGS), 0)
    moved = []
    for move in range(moves):
        picks = (lag_rows == stretch_ref[move + 1:move + 2, :]).astype(jnp.bfloat16)
        product = jnp.dot(parts, picks, preferred_element_type=jnp.float32)
        moved.append(product[:rows] + product[rows:])
    scale = 1.0 / LAGS
    current_power = jnp.sum(current * current, axis=1, keepdims=True) * scale
    lanes = lax.broadcasted_iota(jnp.int32, out_ref.shape, 1)
    result = jnp.zeros(out_ref.shape, jnp.float32)
    for stretch in range(moves + 1):
        if stretch == 0:
            shifted = stacked
        else:
            shifted = moved[stretch - 1]
        numerator = jnp.sum(current * shifted, axis=1, keepdims=True) * scale
        shifted_power = jnp.sum(shifted * shifted, axis=1, keepdims=True) * scale
        value = numerator / jnp.sqrt((current_power + epsilon) * (shifted_power + epsilon))
        result = jnp.where(lanes == stretch, value, result)
    out_ref[...] = result


def coherence(own_minute, stretch_index, crossed, factors):
    minutes, pair_count, width = crossed.shape
    stretch_count = stretch_index.shape[0]
    own = jnp.reshape(own_minute, (1,)).astype(jnp.int32)
    block = min(PAIR_BLOCK, pair_count)
    out = pl.pallas_call(
        coherence_kernel,
        grid_spec=pltpu.PrefetchScalarGridSpec(
            num_scalar_prefetch=1,
            grid=(pair_count // block,),
            in_specs=[
                pl.BlockSpec(stretch_index.shape, lambda i, own: (0, 0)),
                pl.BlockSpec((minutes, block, width), lambda i, own: (0, i, 0)),
            ] + [pl.BlockSpec(factor.shape, lambda i, own: (0, 0)) for factor in factors],
            out_specs=pl.BlockSpec((block, 128), lambda i, own: (i, 0)),
            scratch_shapes=[
                pltpu.VMEM((width, LAGS), jnp.bfloat16),
            ],
        ),
        out_shape=jax.ShapeDtypeStruct((pair_count, 128), jnp.float32),
        compiler_params=pltpu.CompilerParams(
            dimension_semantics=("arbitrary",), vmem_limit_bytes=48 << 20
        ),
    )(own, stretch_index, crossed, *factors)
    return out[:, :stretch_count].T


def body(axis_order, record, pairs, stretch_index):
    block_rows = record.shape[1]
    minutes = lax.axis_size("tm")
    blocks = lax.axis_size("chan")
    def linear(t, b):
        return t * blocks + b if axis_order[0] == "tm" else b * minutes + t

    parts = []
    for shift in range(minutes):
        if shift == 0:
            own = record
        else:
            own = lax.ppermute(record, "tm", [(i, (i + shift) % minutes) for i in range(minutes)])
        route = [
            (linear(t, b), linear((t + shift) % minutes, blocks - 1 - b))
            for t in range(minutes)
            for b in range(blocks)
        ]
        mirrored = lax.ppermute(record, axis_order, route)
        parts.append(jnp.concatenate([own, mirrored], axis=1))
    bundle = jnp.concatenate(parts, axis=0)
    from_below = lax.ppermute(bundle, "chan", [(s, s + 1) for s in range(blocks - 1)])
    from_above = lax.ppermute(bundle, "chan", [(s, s - 1) for s in range(1, blocks)])
    forward = forward_table()

    def spectra(rows):
        count = rows.shape[1]
        spectrum = jnp.dot(
            rows.reshape(minutes * count, NT), forward, preferred_element_type=jnp.float32
        )
        return whiten(spectrum).reshape(minutes, count, 2 * NF)

    local = spectra(bundle)
    below_rows = spectra(from_below)
    above_rows = spectra(from_above)
    whitened = jnp.concatenate(
        [
            below_rows[:, :block_rows],
            local[:, :block_rows],
            above_rows[:, :block_rows],
            above_rows[:, block_rows:],
            local[:, block_rows:],
            below_rows[:, block_rows:],
        ],
        axis=1,
    )
    slot_rows = whitened.shape[1]

    position = lax.axis_index("chan")
    column_index = jnp.arange(pairs.shape[1], dtype=jnp.int32)[None, :]
    is_near = column_index < pairs.shape[1] // 2
    near_slot = pairs - (position - 1) * block_rows
    far_slot = pairs - (blocks - 2 - position) * block_rows + 3 * block_rows
    slot_index = jnp.where(is_near, near_slot, far_slot)
    source_count, recv_count = slot_index.shape
    pair_count = source_count * recv_count
    sources = whitened[:, block_rows:2 * block_rows:8]
    selector = (
        slot_index.reshape(pair_count, 1) == jnp.arange(slot_rows, dtype=jnp.int32)[None, :]
    ).astype(jnp.bfloat16)
    receivers = jnp.einsum(
        "pq,mqk->mpk", selector, whitened, preferred_element_type=jnp.float32
    )
    receivers = receivers.reshape(minutes, source_count, recv_count, 2 * NF)
    crossed = cross_spectrum(sources[:, :, None, :], receivers)
    crossed = crossed.reshape(minutes, pair_count, 2 * NF)
    result = coherence(0, stretch_index, crossed, inverse_factors())
    stretch_count = stretch_index.shape[0]
    return result.reshape(1, stretch_count, source_count, recv_count)


def solution(mesh):
    axis_order = tuple(name for name in mesh.axis_names if name in ("tm", "chan"))
    return jax.shard_map(
        functools.partial(body, axis_order),
        mesh=mesh,
        in_specs=(P("tm", "chan", None), P("chan", None), P()),
        out_specs=P("tm", None, "chan", None),
        check_vma=False,
    )
```

```python
import functools
import math

import jax
import jax.numpy as jnp
from jax import lax
from jax.experimental import pallas as pl
from jax.experimental.pallas import tpu as pltpu
from jax.sharding import PartitionSpec as P

NT = 1536
LAGS = 1024
NF = 768

epsilon = 1e-05


def unit_angles(numerators, period):
    phase = (numerators % period).astype(jnp.float32) * (2.0 * math.pi / period)
    return jnp.cos(phase), jnp.sin(phase)


def forward_table():
    coarse = NT // 128
    bins = jnp.arange(NF, dtype=jnp.int32)[None, :]
    cos_a, sin_a = unit_angles(jnp.arange(coarse, dtype=jnp.int32)[:, None] * bins, coarse)
    cos_c, sin_c = unit_angles(jnp.arange(128, dtype=jnp.int32)[:, None] * bins, NT)
    cos_t = cos_a[:, None, :] * cos_c[None] - sin_a[:, None, :] * sin_c[None]
    sin_t = sin_a[:, None, :] * cos_c[None] + cos_a[:, None, :] * sin_c[None]
    table = jnp.concatenate([cos_t, -sin_t], axis=-1).astype(jnp.bfloat16)
    return table.reshape(NT, 2 * NF)


def inverse_factors():
    coarse = NT // 128
    groups = LAGS // 128
    bins = jnp.arange(NF, dtype=jnp.int32)[:, None]
    cos_a, sin_a = unit_angles(bins * (jnp.arange(groups, dtype=jnp.int32)[None, :] - groups // 2), coarse)
    cos_c, sin_c = unit_angles(bins * jnp.arange(128, dtype=jnp.int32)[None, :], NT)
    weight = jnp.where(bins == 0, 1.0, 2.0).astype(jnp.float32)
    return weight * cos_a, weight * sin_a, cos_c, sin_c


def whiten(spectrum):
    power = jnp.mean(spectrum * spectrum, axis=-1, keepdims=True)
    return (spectrum / jnp.sqrt(power + epsilon)).astype(jnp.bfloat16)


def cross_spectrum(source_row, receivers):
    half_width = receivers.shape[-1] // 2
    source_vals = source_row.astype(jnp.float32)
    receiver_vals = receivers.astype(jnp.float32)
    src_re = source_vals[..., :half_width]
    src_im = source_vals[..., half_width:]
    rec_re = receiver_vals[..., :half_width]
    rec_im = receiver_vals[..., half_width:]
    real_part = src_re * rec_re + src_im * rec_im
    imag_part = src_re * rec_im - src_im * rec_re
    return jnp.concatenate([real_part, imag_part], axis=-1).astype(jnp.bfloat16)


PAIR_BLOCK = 512


def coherence_kernel(
    own_ref, stretch_ref, crossed_ref, wcos_ref, wsin_ref, fcos_ref, fsin_ref,
    out_ref,
):
    minutes = crossed_ref.shape[0]
    moves = stretch_ref.shape[0] - 1
    groups = wcos_ref.shape[1]
    fine = fcos_ref.shape[1]

    fine_cos = fcos_ref[...]
    fine_sin = fsin_ref[...]
    own = own_ref[0]
    pieces = [[] for _ in range(minutes)]
    for pair_group in range(groups // 2):
        columns = []
        for group in (2 * pair_group, 2 * pair_group + 1):
            coarse_cos = wcos_ref[:, group:group + 1]
            coarse_sin = wsin_ref[:, group:group + 1]
            columns.append(
                jnp.concatenate(
                    [
                        coarse_cos * fine_cos - coarse_sin * fine_sin,
                        -(coarse_sin * fine_cos + coarse_cos * fine_sin),
                    ],
                    axis=0,
                ).astype(jnp.bfloat16)
            )
        inverse = jnp.concatenate(columns, axis=1)
        for minute in range(minutes):
            pieces[minute].append(
                jnp.dot(crossed_ref[minute], inverse, preferred_element_type=jnp.float32)
            )
    stacked = None
    current = None
    for minute in range(minutes):
        correlation = jnp.concatenate(pieces[minute], axis=1)
        if stacked is None:
            stacked, current = correlation, correlation
        else:
            stacked = stacked + correlation
            current = jnp.where(own == minute, correlation, current)
    high = stacked.astype(jnp.bfloat16)
    low = (stacked - high.astype(jnp.float32)).astype(jnp.bfloat16)
    rows = stacked.shape[0]
    parts = jnp.concatenate([high, low], axis=0)
    lag_rows = lax.broadcasted_iota(jnp.int32, (LAGS, LAGS), 0)
    moved = []
    for move in range(moves):
        picks = (lag_rows == stretch_ref[move + 1:move + 2, :]).astype(jnp.bfloat16)
        product = jnp.dot(parts, picks, preferred_element_type=jnp.float32)
        moved.append(product[:rows] + product[rows:])
    scale = 1.0 / LAGS
    current_power = jnp.sum(current * current, axis=1, keepdims=True) * scale
    lanes = lax.broadcasted_iota(jnp.int32, out_ref.shape, 1)
    result = jnp.zeros(out_ref.shape, jnp.float32)
    for stretch in range(moves + 1):
        if stretch == 0:
            shifted = stacked
        else:
            shifted = moved[stretch - 1]
        numerator = jnp.sum(current * shifted, axis=1, keepdims=True) * scale
        shifted_power = jnp.sum(shifted * shifted, axis=1, keepdims=True) * scale
        value = numerator / jnp.sqrt((current_power + epsilon) * (shifted_power + epsilon))
        result = jnp.where(lanes == stretch, value, result)
    out_ref[...] = result


def coherence(own_minute, stretch_index, crossed, factors):
    minutes, pair_count, width = crossed.shape
    stretch_count = stretch_index.shape[0]
    own = jnp.reshape(own_minute, (1,)).astype(jnp.int32)
    block = min(PAIR_BLOCK, pair_count)
    out = pl.pallas_call(
        coherence_kernel,
        grid_spec=pltpu.PrefetchScalarGridSpec(
            num_scalar_prefetch=1,
            grid=(pair_count // block,),
            in_specs=[
                pl.BlockSpec(stretch_index.shape, lambda i, own: (0, 0)),
                pl.BlockSpec((minutes, block, width), lambda i, own: (0, i, 0)),
            ] + [pl.BlockSpec(factor.shape, lambda i, own: (0, 0)) for factor in factors],
            out_specs=pl.BlockSpec((block, 128), lambda i, own: (i, 0)),
        ),
        out_shape=jax.ShapeDtypeStruct((pair_count, 128), jnp.float32),
        compiler_params=pltpu.CompilerParams(
            dimension_semantics=("arbitrary",), vmem_limit_bytes=48 << 20
        ),
    )(own, stretch_index, crossed, *factors)
    return out[:, :stretch_count].T


def body(axis_order, record, pairs, stretch_index):
    block_rows = record.shape[1]
    minutes = lax.axis_size("tm")
    blocks = lax.axis_size("chan")
    def linear(t, b):
        return t * blocks + b if axis_order[0] == "tm" else b * minutes + t

    parts = []
    for shift in range(minutes):
        if shift == 0:
            own = record
        else:
            own = lax.ppermute(record, "tm", [(i, (i + shift) % minutes) for i in range(minutes)])
        route = [
            (linear(t, b), linear((t + shift) % minutes, blocks - 1 - b))
            for t in range(minutes)
            for b in range(blocks)
        ]
        mirrored = lax.ppermute(record, axis_order, route)
        parts.append(jnp.concatenate([own, mirrored], axis=1))
    bundle = jnp.concatenate(parts, axis=0)
    from_below = lax.ppermute(bundle, "chan", [(s, s + 1) for s in range(blocks - 1)])
    from_above = lax.ppermute(bundle, "chan", [(s, s - 1) for s in range(1, blocks)])
    forward = forward_table()

    def spectra(rows):
        count = rows.shape[1]
        spectrum = jnp.dot(
            rows.reshape(minutes * count, NT), forward, preferred_element_type=jnp.float32
        )
        return whiten(spectrum).reshape(minutes, count, 2 * NF)

    local = spectra(bundle)
    below_rows = spectra(from_below)
    above_rows = spectra(from_above)
    whitened = jnp.concatenate(
        [
            below_rows[:, :block_rows],
            local[:, :block_rows],
            above_rows[:, :block_rows],
            above_rows[:, block_rows:],
            local[:, block_rows:],
            below_rows[:, block_rows:],
        ],
        axis=1,
    )
    slot_rows = whitened.shape[1]

    position = lax.axis_index("chan")
    column_index = jnp.arange(pairs.shape[1], dtype=jnp.int32)[None, :]
    is_near = column_index < pairs.shape[1] // 2
    near_slot = pairs - (position - 1) * block_rows
    far_slot = pairs - (blocks - 2 - position) * block_rows + 3 * block_rows
    slot_index = jnp.where(is_near, near_slot, far_slot)
    source_count, recv_count = slot_index.shape
    pair_count = source_count * recv_count
    sources = whitened[:, block_rows:2 * block_rows:8]
    selector = (
        slot_index.reshape(pair_count, 1) == jnp.arange(slot_rows, dtype=jnp.int32)[None, :]
    ).astype(jnp.bfloat16)
    receivers = jnp.einsum(
        "pq,mqk->mpk", selector, whitened, preferred_element_type=jnp.float32
    )
    receivers = receivers.reshape(minutes, source_count, recv_count, 2 * NF)
    crossed = cross_spectrum(sources[:, :, None, :], receivers)
    crossed = crossed.reshape(minutes, pair_count, 2 * NF)
    result = coherence(0, stretch_index, crossed, inverse_factors())
    stretch_count = stretch_index.shape[0]
    return result.reshape(1, stretch_count, source_count, recv_count)


def solution(mesh):
    axis_order = tuple(name for name in mesh.axis_names if name in ("tm", "chan"))
    return jax.shard_map(
        functools.partial(body, axis_order),
        mesh=mesh,
        in_specs=(P("tm", "chan", None), P("chan", None), P()),
        out_specs=P("tm", None, "chan", None),
        check_vma=False,
    )
```

```python
import functools
import math

import jax
import jax.numpy as jnp
from jax import lax
from jax.experimental import pallas as pl
from jax.experimental.pallas import tpu as pltpu
from jax.sharding import PartitionSpec as P

NT = 1536
LAGS = 1024
NF = 768

epsilon = 1e-05


def unit_angles(numerators, period):
    phase = (numerators % period).astype(jnp.float32) * (2.0 * math.pi / period)
    return jnp.cos(phase), jnp.sin(phase)


def forward_table():
    coarse = NT // 128
    bins = jnp.arange(NF, dtype=jnp.int32)[None, :]
    cos_a, sin_a = unit_angles(jnp.arange(coarse, dtype=jnp.int32)[:, None] * bins, coarse)
    cos_c, sin_c = unit_angles(jnp.arange(128, dtype=jnp.int32)[:, None] * bins, NT)
    cos_t = cos_a[:, None, :] * cos_c[None] - sin_a[:, None, :] * sin_c[None]
    sin_t = sin_a[:, None, :] * cos_c[None] + cos_a[:, None, :] * sin_c[None]
    table = jnp.concatenate([cos_t, -sin_t], axis=-1).astype(jnp.bfloat16)
    return table.reshape(NT, 2 * NF)


def inverse_factors():
    coarse = NT // 128
    groups = LAGS // 128
    bins = jnp.arange(NF, dtype=jnp.int32)[:, None]
    cos_a, sin_a = unit_angles(bins * (jnp.arange(groups, dtype=jnp.int32)[None, :] - groups // 2), coarse)
    cos_c, sin_c = unit_angles(bins * jnp.arange(128, dtype=jnp.int32)[None, :], NT)
    weight = jnp.where(bins == 0, 1.0, 2.0).astype(jnp.float32)
    return weight * cos_a, weight * sin_a, cos_c, sin_c


def whiten(spectrum):
    power = jnp.mean(spectrum * spectrum, axis=-1, keepdims=True)
    return (spectrum / jnp.sqrt(power + epsilon)).astype(jnp.bfloat16)


def cross_spectrum(source_row, receivers):
    half_width = receivers.shape[-1] // 2
    source_vals = source_row.astype(jnp.float32)
    receiver_vals = receivers.astype(jnp.float32)
    src_re = source_vals[..., :half_width]
    src_im = source_vals[..., half_width:]
    rec_re = receiver_vals[..., :half_width]
    rec_im = receiver_vals[..., half_width:]
    real_part = src_re * rec_re + src_im * rec_im
    imag_part = src_re * rec_im - src_im * rec_re
    return jnp.concatenate([real_part, imag_part], axis=-1).astype(jnp.bfloat16)


PAIR_BLOCK = 512


def coherence_kernel(
    own_ref, stretch_ref, crossed_ref, wcos_ref, wsin_ref, fcos_ref, fsin_ref,
    out_ref,
):
    minutes = crossed_ref.shape[0]
    moves = stretch_ref.shape[0] - 1
    groups = wcos_ref.shape[1]
    fine = fcos_ref.shape[1]

    fine_cos = fcos_ref[...]
    fine_sin = fsin_ref[...]
    own = own_ref[0]
    pieces = [[] for _ in range(minutes)]
    for pair_group in range(groups // 2):
        columns = []
        for group in (2 * pair_group, 2 * pair_group + 1):
            coarse_cos = wcos_ref[:, group:group + 1]
            coarse_sin = wsin_ref[:, group:group + 1]
            columns.append(
                jnp.concatenate(
                    [
                        coarse_cos * fine_cos - coarse_sin * fine_sin,
                        -(coarse_sin * fine_cos + coarse_cos * fine_sin),
                    ],
                    axis=0,
                ).astype(jnp.bfloat16)
            )
        inverse = jnp.concatenate(columns, axis=1)
        for minute in range(minutes):
            pieces[minute].append(
                jnp.dot(crossed_ref[minute], inverse, preferred_element_type=jnp.float32)
            )
    stacked = None
    current = None
    for minute in range(minutes):
        correlation = jnp.concatenate(pieces[minute], axis=1)
        if stacked is None:
            stacked, current = correlation, correlation
        else:
            stacked = stacked + correlation
            current = jnp.where(own == minute, correlation, current)
    high = stacked.astype(jnp.bfloat16)
    low = (stacked - high.astype(jnp.float32)).astype(jnp.bfloat16)
    rows = stacked.shape[0]
    parts = jnp.concatenate([high, low], axis=0)
    lag_rows = lax.broadcasted_iota(jnp.int32, (LAGS, LAGS), 0)
    moved = []
    for move in range(moves):
        picks = (lag_rows == stretch_ref[move + 1:move + 2, :]).astype(jnp.bfloat16)
        product = jnp.dot(parts, picks, preferred_element_type=jnp.float32)
        moved.append(product[:rows] + product[rows:])
    scale = 1.0 / LAGS
    current_power = jnp.sum(current * current, axis=1, keepdims=True) * scale
    lanes = lax.broadcasted_iota(jnp.int32, out_ref.shape, 1)
    result = jnp.zeros(out_ref.shape, jnp.float32)
    for stretch in range(moves + 1):
        if stretch == 0:
            shifted = stacked
        else:
            shifted = moved[stretch - 1]
        numerator = jnp.sum(current * shifted, axis=1, keepdims=True) * scale
        shifted_power = jnp.sum(shifted * shifted, axis=1, keepdims=True) * scale
        value = numerator / jnp.sqrt((current_power + epsilon) * (shifted_power + epsilon))
        result = jnp.where(lanes == stretch, value, result)
    out_ref[...] = result


def coherence(own_minute, stretch_index, crossed, factors):
    minutes, pair_count, width = crossed.shape
    stretch_count = stretch_index.shape[0]
    own = jnp.reshape(own_minute, (1,)).astype(jnp.int32)
    block = min(PAIR_BLOCK, pair_count)
    out = pl.pallas_call(
        coherence_kernel,
        grid_spec=pltpu.PrefetchScalarGridSpec(
            num_scalar_prefetch=1,
            grid=(pair_count // block,),
            in_specs=[
                pl.BlockSpec(stretch_index.shape, lambda i, own: (0, 0)),
                pl.BlockSpec((minutes, block, width), lambda i, own: (0, i, 0)),
            ] + [pl.BlockSpec(factor.shape, lambda i, own: (0, 0)) for factor in factors],
            out_specs=pl.BlockSpec((block, stretch_count), lambda i, own: (i, 0)),
        ),
        out_shape=jax.ShapeDtypeStruct((pair_count, stretch_count), jnp.float32),
        compiler_params=pltpu.CompilerParams(
            dimension_semantics=("arbitrary",), vmem_limit_bytes=48 << 20
        ),
    )(own, stretch_index, crossed, *factors)
    return out.T


def body(axis_order, record, pairs, stretch_index):
    block_rows = record.shape[1]
    minutes = lax.axis_size("tm")
    blocks = lax.axis_size("chan")
    def linear(t, b):
        return t * blocks + b if axis_order[0] == "tm" else b * minutes + t

    parts = []
    for shift in range(minutes):
        if shift == 0:
            own = record
        else:
            own = lax.ppermute(record, "tm", [(i, (i + shift) % minutes) for i in range(minutes)])
        route = [
            (linear(t, b), linear((t + shift) % minutes, blocks - 1 - b))
            for t in range(minutes)
            for b in range(blocks)
        ]
        mirrored = lax.ppermute(record, axis_order, route)
        parts.append(jnp.concatenate([own, mirrored], axis=1))
    bundle = jnp.concatenate(parts, axis=0)
    from_below = lax.ppermute(bundle, "chan", [(s, s + 1) for s in range(blocks - 1)])
    from_above = lax.ppermute(bundle, "chan", [(s, s - 1) for s in range(1, blocks)])
    forward = forward_table()

    def spectra(rows):
        count = rows.shape[1]
        spectrum = jnp.dot(
            rows.reshape(minutes * count, NT), forward, preferred_element_type=jnp.float32
        )
        return whiten(spectrum).reshape(minutes, count, 2 * NF)

    local = spectra(bundle)
    below_rows = spectra(from_below)
    above_rows = spectra(from_above)
    whitened = jnp.concatenate(
        [
            below_rows[:, :block_rows],
            local[:, :block_rows],
            above_rows[:, :block_rows],
            above_rows[:, block_rows:],
            local[:, block_rows:],
            below_rows[:, block_rows:],
        ],
        axis=1,
    )
    slot_rows = whitened.shape[1]

    position = lax.axis_index("chan")
    column_index = jnp.arange(pairs.shape[1], dtype=jnp.int32)[None, :]
    is_near = column_index < pairs.shape[1] // 2
    near_slot = pairs - (position - 1) * block_rows
    far_slot = pairs - (blocks - 2 - position) * block_rows + 3 * block_rows
    slot_index = jnp.where(is_near, near_slot, far_slot)
    source_count, recv_count = slot_index.shape
    pair_count = source_count * recv_count
    sources = whitened[:, block_rows:2 * block_rows:8]
    selector = (
        slot_index.reshape(pair_count, 1) == jnp.arange(slot_rows, dtype=jnp.int32)[None, :]
    ).astype(jnp.bfloat16)
    receivers = jnp.einsum(
        "pq,mqk->mpk", selector, whitened, preferred_element_type=jnp.float32
    )
    receivers = receivers.reshape(minutes, source_count, recv_count, 2 * NF)
    crossed = cross_spectrum(sources[:, :, None, :], receivers)
    crossed = crossed.reshape(minutes, pair_count, 2 * NF)
    result = coherence(0, stretch_index, crossed, inverse_factors())
    stretch_count = stretch_index.shape[0]
    return result.reshape(1, stretch_count, source_count, recv_count)


def solution(mesh):
    axis_order = tuple(name for name in mesh.axis_names if name in ("tm", "chan"))
    return jax.shard_map(
        functools.partial(body, axis_order),
        mesh=mesh,
        in_specs=(P("tm", "chan", None), P("chan", None), P()),
        out_specs=P("tm", None, "chan", None),
        check_vma=False,
    )
```

```python
import functools
import math

import jax
import jax.numpy as jnp
from jax import lax
from jax.experimental import pallas as pl
from jax.experimental.pallas import tpu as pltpu
from jax.sharding import PartitionSpec as P

NT = 1536
LAGS = 1024
NF = 768

epsilon = 1e-05


def unit_angles(numerators, period):
    phase = (numerators % period).astype(jnp.float32) * (2.0 * math.pi / period)
    return jnp.cos(phase), jnp.sin(phase)


def forward_table():
    coarse = NT // 128
    bins = jnp.arange(NF, dtype=jnp.int32)[None, :]
    cos_a, sin_a = unit_angles(jnp.arange(coarse, dtype=jnp.int32)[:, None] * bins, coarse)
    cos_c, sin_c = unit_angles(jnp.arange(128, dtype=jnp.int32)[:, None] * bins, NT)
    cos_t = cos_a[:, None, :] * cos_c[None] - sin_a[:, None, :] * sin_c[None]
    sin_t = sin_a[:, None, :] * cos_c[None] + cos_a[:, None, :] * sin_c[None]
    table = jnp.concatenate([cos_t, -sin_t], axis=-1).astype(jnp.bfloat16)
    return table.reshape(NT, 2 * NF)


def inverse_factors():
    coarse = NT // 128
    groups = LAGS // 128
    bins = jnp.arange(NF, dtype=jnp.int32)[:, None]
    cos_a, sin_a = unit_angles(bins * (jnp.arange(groups, dtype=jnp.int32)[None, :] - groups // 2), coarse)
    cos_c, sin_c = unit_angles(bins * jnp.arange(128, dtype=jnp.int32)[None, :], NT)
    weight = jnp.where(bins == 0, 1.0, 2.0).astype(jnp.float32)
    return weight * cos_a, weight * sin_a, cos_c, sin_c


def whiten(spectrum):
    power = jnp.mean(spectrum * spectrum, axis=-1, keepdims=True)
    return (spectrum / jnp.sqrt(power + epsilon)).astype(jnp.bfloat16)


def cross_spectrum(source_row, receivers):
    half_width = receivers.shape[-1] // 2
    source_vals = source_row.astype(jnp.float32)
    receiver_vals = receivers.astype(jnp.float32)
    src_re = source_vals[..., :half_width]
    src_im = source_vals[..., half_width:]
    rec_re = receiver_vals[..., :half_width]
    rec_im = receiver_vals[..., half_width:]
    real_part = src_re * rec_re + src_im * rec_im
    imag_part = src_re * rec_im - src_im * rec_re
    return jnp.concatenate([real_part, imag_part], axis=-1).astype(jnp.bfloat16)


PAIR_BLOCK = 512


def coherence_kernel(
    own_ref, stretch_ref, crossed_ref, wcos_ref, wsin_ref, fcos_ref, fsin_ref,
    out_ref,
):
    minutes = crossed_ref.shape[0]
    moves = stretch_ref.shape[0] - 1
    groups = wcos_ref.shape[1]
    fine = fcos_ref.shape[1]

    fine_cos = fcos_ref[...]
    fine_sin = fsin_ref[...]
    own = own_ref[0]
    pieces = [[] for _ in range(minutes)]
    block = crossed_ref.shape[1]
    all_rows = crossed_ref[...].reshape(minutes * block, crossed_ref.shape[2])
    for pair_group in range(groups // 2):
        columns = []
        for group in (2 * pair_group, 2 * pair_group + 1):
            coarse_cos = wcos_ref[:, group:group + 1]
            coarse_sin = wsin_ref[:, group:group + 1]
            columns.append(
                jnp.concatenate(
                    [
                        coarse_cos * fine_cos - coarse_sin * fine_sin,
                        -(coarse_sin * fine_cos + coarse_cos * fine_sin),
                    ],
                    axis=0,
                ).astype(jnp.bfloat16)
            )
        inverse = jnp.concatenate(columns, axis=1)
        product = jnp.dot(all_rows, inverse, preferred_element_type=jnp.float32)
        for minute in range(minutes):
            pieces[minute].append(product[minute * block:(minute + 1) * block])
    stacked = None
    current = None
    for minute in range(minutes):
        correlation = jnp.concatenate(pieces[minute], axis=1)
        if stacked is None:
            stacked, current = correlation, correlation
        else:
            stacked = stacked + correlation
            current = jnp.where(own == minute, correlation, current)
    high = stacked.astype(jnp.bfloat16)
    low = (stacked - high.astype(jnp.float32)).astype(jnp.bfloat16)
    rows = stacked.shape[0]
    parts = jnp.concatenate([high, low], axis=0)
    lag_rows = lax.broadcasted_iota(jnp.int32, (LAGS, LAGS), 0)
    moved = []
    for move in range(moves):
        picks = (lag_rows == stretch_ref[move + 1:move + 2, :]).astype(jnp.bfloat16)
        product = jnp.dot(parts, picks, preferred_element_type=jnp.float32)
        moved.append(product[:rows] + product[rows:])
    scale = 1.0 / LAGS
    current_power = jnp.sum(current * current, axis=1, keepdims=True) * scale
    lanes = lax.broadcasted_iota(jnp.int32, out_ref.shape, 1)
    result = jnp.zeros(out_ref.shape, jnp.float32)
    for stretch in range(moves + 1):
        if stretch == 0:
            shifted = stacked
        else:
            shifted = moved[stretch - 1]
        numerator = jnp.sum(current * shifted, axis=1, keepdims=True) * scale
        shifted_power = jnp.sum(shifted * shifted, axis=1, keepdims=True) * scale
        value = numerator / jnp.sqrt((current_power + epsilon) * (shifted_power + epsilon))
        result = jnp.where(lanes == stretch, value, result)
    out_ref[...] = result


def coherence(own_minute, stretch_index, crossed, factors):
    minutes, pair_count, width = crossed.shape
    stretch_count = stretch_index.shape[0]
    own = jnp.reshape(own_minute, (1,)).astype(jnp.int32)
    block = min(PAIR_BLOCK, pair_count)
    out = pl.pallas_call(
        coherence_kernel,
        grid_spec=pltpu.PrefetchScalarGridSpec(
            num_scalar_prefetch=1,
            grid=(pair_count // block,),
            in_specs=[
                pl.BlockSpec(stretch_index.shape, lambda i, own: (0, 0)),
                pl.BlockSpec((minutes, block, width), lambda i, own: (0, i, 0)),
            ] + [pl.BlockSpec(factor.shape, lambda i, own: (0, 0)) for factor in factors],
            out_specs=pl.BlockSpec((block, stretch_count), lambda i, own: (i, 0)),
        ),
        out_shape=jax.ShapeDtypeStruct((pair_count, stretch_count), jnp.float32),
        compiler_params=pltpu.CompilerParams(
            dimension_semantics=("arbitrary",), vmem_limit_bytes=48 << 20
        ),
    )(own, stretch_index, crossed, *factors)
    return out.T


def body(axis_order, record, pairs, stretch_index):
    block_rows = record.shape[1]
    minutes = lax.axis_size("tm")
    blocks = lax.axis_size("chan")
    def linear(t, b):
        return t * blocks + b if axis_order[0] == "tm" else b * minutes + t

    parts = []
    for shift in range(minutes):
        if shift == 0:
            own = record
        else:
            own = lax.ppermute(record, "tm", [(i, (i + shift) % minutes) for i in range(minutes)])
        route = [
            (linear(t, b), linear((t + shift) % minutes, blocks - 1 - b))
            for t in range(minutes)
            for b in range(blocks)
        ]
        mirrored = lax.ppermute(record, axis_order, route)
        parts.append(jnp.concatenate([own, mirrored], axis=1))
    bundle = jnp.concatenate(parts, axis=0)
    from_below = lax.ppermute(bundle, "chan", [(s, s + 1) for s in range(blocks - 1)])
    from_above = lax.ppermute(bundle, "chan", [(s, s - 1) for s in range(1, blocks)])
    forward = forward_table()

    def spectra(rows):
        count = rows.shape[1]
        spectrum = jnp.dot(
            rows.reshape(minutes * count, NT), forward, preferred_element_type=jnp.float32
        )
        return whiten(spectrum).reshape(minutes, count, 2 * NF)

    local = spectra(bundle)
    below_rows = spectra(from_below)
    above_rows = spectra(from_above)
    whitened = jnp.concatenate(
        [
            below_rows[:, :block_rows],
            local[:, :block_rows],
            above_rows[:, :block_rows],
            above_rows[:, block_rows:],
            local[:, block_rows:],
            below_rows[:, block_rows:],
        ],
        axis=1,
    )
    slot_rows = whitened.shape[1]

    position = lax.axis_index("chan")
    column_index = jnp.arange(pairs.shape[1], dtype=jnp.int32)[None, :]
    is_near = column_index < pairs.shape[1] // 2
    near_slot = pairs - (position - 1) * block_rows
    far_slot = pairs - (blocks - 2 - position) * block_rows + 3 * block_rows
    slot_index = jnp.where(is_near, near_slot, far_slot)
    source_count, recv_count = slot_index.shape
    pair_count = source_count * recv_count
    sources = whitened[:, block_rows:2 * block_rows:8]
    selector = (
        slot_index.reshape(pair_count, 1) == jnp.arange(slot_rows, dtype=jnp.int32)[None, :]
    ).astype(jnp.bfloat16)
    receivers = jnp.einsum(
        "pq,mqk->mpk", selector, whitened, preferred_element_type=jnp.float32
    )
    receivers = receivers.reshape(minutes, source_count, recv_count, 2 * NF)
    crossed = cross_spectrum(sources[:, :, None, :], receivers)
    crossed = crossed.reshape(minutes, pair_count, 2 * NF)
    result = coherence(0, stretch_index, crossed, inverse_factors())
    stretch_count = stretch_index.shape[0]
    return result.reshape(1, stretch_count, source_count, recv_count)


def solution(mesh):
    axis_order = tuple(name for name in mesh.axis_names if name in ("tm", "chan"))
    return jax.shard_map(
        functools.partial(body, axis_order),
        mesh=mesh,
        in_specs=(P("tm", "chan", None), P("chan", None), P()),
        out_specs=P("tm", None, "chan", None),
        check_vma=False,
    )
```

```python
import functools
import math

import jax
import jax.numpy as jnp
from jax import lax
from jax.experimental import pallas as pl
from jax.experimental.pallas import tpu as pltpu
from jax.sharding import PartitionSpec as P

NT = 1536
LAGS = 1024
NF = 768

epsilon = 1e-05


def unit_angles(numerators, period):
    phase = (numerators % period).astype(jnp.float32) * (2.0 * math.pi / period)
    return jnp.cos(phase), jnp.sin(phase)


def forward_table():
    coarse = NT // 128
    bins = jnp.arange(NF, dtype=jnp.int32)[None, :]
    cos_a, sin_a = unit_angles(jnp.arange(coarse, dtype=jnp.int32)[:, None] * bins, coarse)
    cos_c, sin_c = unit_angles(jnp.arange(128, dtype=jnp.int32)[:, None] * bins, NT)
    cos_t = cos_a[:, None, :] * cos_c[None] - sin_a[:, None, :] * sin_c[None]
    sin_t = sin_a[:, None, :] * cos_c[None] + cos_a[:, None, :] * sin_c[None]
    table = jnp.concatenate([cos_t, -sin_t], axis=-1).astype(jnp.bfloat16)
    return table.reshape(NT, 2 * NF)


def inverse_factors():
    coarse = NT // 128
    groups = LAGS // 128
    bins = jnp.arange(NF, dtype=jnp.int32)[:, None]
    cos_a, sin_a = unit_angles(bins * (jnp.arange(groups, dtype=jnp.int32)[None, :] - groups // 2), coarse)
    cos_c, sin_c = unit_angles(bins * jnp.arange(128, dtype=jnp.int32)[None, :], NT)
    weight = jnp.where(bins == 0, 1.0, 2.0).astype(jnp.float32)
    return weight * cos_a, weight * sin_a, cos_c, sin_c


def whiten(spectrum):
    power = jnp.mean(spectrum * spectrum, axis=-1, keepdims=True)
    return (spectrum / jnp.sqrt(power + epsilon)).astype(jnp.bfloat16)


def cross_spectrum(source_row, receivers):
    half_width = receivers.shape[-1] // 2
    source_vals = source_row.astype(jnp.float32)
    receiver_vals = receivers.astype(jnp.float32)
    src_re = source_vals[..., :half_width]
    src_im = source_vals[..., half_width:]
    rec_re = receiver_vals[..., :half_width]
    rec_im = receiver_vals[..., half_width:]
    real_part = src_re * rec_re + src_im * rec_im
    imag_part = src_re * rec_im - src_im * rec_re
    return jnp.concatenate([real_part, imag_part], axis=-1).astype(jnp.bfloat16)


PAIR_BLOCK = 512


def coherence_kernel(
    own_ref, stretch_ref, crossed_ref, wcos_ref, wsin_ref, fcos_ref, fsin_ref,
    out_ref,
):
    minutes = crossed_ref.shape[0]
    moves = stretch_ref.shape[0] - 1
    groups = wcos_ref.shape[1]
    fine = fcos_ref.shape[1]

    fine_cos = fcos_ref[...]
    fine_sin = fsin_ref[...]
    own = own_ref[0]
    pieces = [[] for _ in range(minutes)]
    for pair_group in range(groups // 2):
        columns = []
        for group in (2 * pair_group, 2 * pair_group + 1):
            coarse_cos = wcos_ref[:, group:group + 1]
            coarse_sin = wsin_ref[:, group:group + 1]
            columns.append(
                jnp.concatenate(
                    [
                        coarse_cos * fine_cos - coarse_sin * fine_sin,
                        -(coarse_sin * fine_cos + coarse_cos * fine_sin),
                    ],
                    axis=0,
                ).astype(jnp.bfloat16)
            )
        inverse = jnp.concatenate(columns, axis=1)
        for minute in range(minutes):
            pieces[minute].append(
                jnp.dot(crossed_ref[minute], inverse, preferred_element_type=jnp.float32)
            )
    stacked = None
    current = None
    for minute in range(minutes):
        correlation = jnp.concatenate(pieces[minute], axis=1)
        if stacked is None:
            stacked, current = correlation, correlation
        else:
            stacked = stacked + correlation
            current = jnp.where(own == minute, correlation, current)
    high = stacked.astype(jnp.bfloat16)
    low = (stacked - high.astype(jnp.float32)).astype(jnp.bfloat16)
    rows = stacked.shape[0]
    parts = jnp.concatenate([high, low], axis=0)
    lag_rows = lax.broadcasted_iota(jnp.int32, (LAGS, LAGS), 0)
    moved = []
    for move in range(moves):
        picks = (lag_rows == stretch_ref[move + 1:move + 2, :]).astype(jnp.bfloat16)
        product = jnp.dot(parts, picks, preferred_element_type=jnp.float32)
        moved.append(product[:rows] + product[rows:])
    scale = 1.0 / LAGS
    current_power = jnp.sum(current * current, axis=1, keepdims=True) * scale
    lanes = lax.broadcasted_iota(jnp.int32, out_ref.shape, 1)
    result = jnp.zeros(out_ref.shape, jnp.float32)
    for stretch in range(moves + 1):
        if stretch == 0:
            shifted = stacked
        else:
            shifted = moved[stretch - 1]
        numerator = jnp.sum(current * shifted, axis=1, keepdims=True) * scale
        shifted_power = jnp.sum(shifted * shifted, axis=1, keepdims=True) * scale
        value = numerator / jnp.sqrt((current_power + epsilon) * (shifted_power + epsilon))
        result = jnp.where(lanes == stretch, value, result)
    out_ref[...] = result


def coherence(own_minute, stretch_index, crossed, factors):
    minutes, pair_count, width = crossed.shape
    stretch_count = stretch_index.shape[0]
    own = jnp.reshape(own_minute, (1,)).astype(jnp.int32)
    block = min(PAIR_BLOCK, pair_count)
    out = pl.pallas_call(
        coherence_kernel,
        grid_spec=pltpu.PrefetchScalarGridSpec(
            num_scalar_prefetch=1,
            grid=(pair_count // block,),
            in_specs=[
                pl.BlockSpec(stretch_index.shape, lambda i, own: (0, 0)),
                pl.BlockSpec((minutes, block, width), lambda i, own: (0, i, 0)),
            ] + [pl.BlockSpec(factor.shape, lambda i, own: (0, 0)) for factor in factors],
            out_specs=pl.BlockSpec((block, stretch_count), lambda i, own: (i, 0)),
        ),
        out_shape=jax.ShapeDtypeStruct((pair_count, stretch_count), jnp.float32),
        compiler_params=pltpu.CompilerParams(
            dimension_semantics=("arbitrary",), vmem_limit_bytes=48 << 20
        ),
    )(own, stretch_index, crossed, *factors)
    return out.T


def body(axis_order, record, pairs, stretch_index):
    block_rows = record.shape[1]
    minutes = lax.axis_size("tm")
    blocks = lax.axis_size("chan")
    def linear(t, b):
        return t * blocks + b if axis_order[0] == "tm" else b * minutes + t

    parts = []
    for shift in range(minutes):
        if shift == 0:
            own = record
        else:
            own = lax.ppermute(record, "tm", [(i, (i + shift) % minutes) for i in range(minutes)])
        route = [
            (linear(t, b), linear((t + shift) % minutes, blocks - 1 - b))
            for t in range(minutes)
            for b in range(blocks)
        ]
        mirrored = lax.ppermute(record, axis_order, route)
        parts.append(jnp.concatenate([own, mirrored], axis=1))
    bundle = jnp.concatenate(parts, axis=0)
    from_below = lax.ppermute(bundle, "chan", [(s, s + 1) for s in range(blocks - 1)])
    from_above = lax.ppermute(bundle, "chan", [(s, s - 1) for s in range(1, blocks)])
    forward = forward_table()

    def spectra(rows):
        count = rows.shape[1]
        spectrum = jnp.dot(
            rows.reshape(minutes * count, NT), forward, preferred_element_type=jnp.float32
        )
        return whiten(spectrum).reshape(minutes, count, 2 * NF)

    local = spectra(bundle)
    below_rows = spectra(from_below)
    above_rows = spectra(from_above)
    whitened = jnp.concatenate(
        [
            below_rows[:, :block_rows],
            local[:, :block_rows],
            above_rows[:, :block_rows],
            above_rows[:, block_rows:],
            local[:, block_rows:],
            below_rows[:, block_rows:],
        ],
        axis=1,
    )
    slot_rows = whitened.shape[1]

    position = lax.axis_index("chan")
    column_index = jnp.arange(pairs.shape[1], dtype=jnp.int32)[None, :]
    is_near = column_index < pairs.shape[1] // 2
    near_slot = pairs - (position - 1) * block_rows
    far_slot = pairs - (blocks - 2 - position) * block_rows + 3 * block_rows
    slot_index = jnp.where(is_near, near_slot, far_slot)
    source_count, recv_count = slot_index.shape
    pair_count = source_count * recv_count
    sources = whitened[:, block_rows:2 * block_rows:8]
    selector = (
        slot_index.reshape(pair_count, 1) == jnp.arange(slot_rows, dtype=jnp.int32)[None, :]
    ).astype(jnp.bfloat16)
    receivers = jnp.einsum(
        "pq,mqk->mpk", selector, whitened, preferred_element_type=jnp.bfloat16
    )
    receivers = receivers.reshape(minutes, source_count, recv_count, 2 * NF)
    crossed = cross_spectrum(sources[:, :, None, :], receivers)
    crossed = crossed.reshape(minutes, pair_count, 2 * NF)
    result = coherence(0, stretch_index, crossed, inverse_factors())
    stretch_count = stretch_index.shape[0]
    return result.reshape(1, stretch_count, source_count, recv_count)


def solution(mesh):
    axis_order = tuple(name for name in mesh.axis_names if name in ("tm", "chan"))
    return jax.shard_map(
        functools.partial(body, axis_order),
        mesh=mesh,
        in_specs=(P("tm", "chan", None), P("chan", None), P()),
        out_specs=P("tm", None, "chan", None),
        check_vma=False,
    )
```

```python
import functools
import math

import jax
import jax.numpy as jnp
from jax import lax
from jax.experimental import pallas as pl
from jax.experimental.pallas import tpu as pltpu
from jax.sharding import PartitionSpec as P

NT = 1536
LAGS = 1024
NF = 768

epsilon = 1e-05


def unit_angles(numerators, period):
    phase = (numerators % period).astype(jnp.float32) * (2.0 * math.pi / period)
    return jnp.cos(phase), jnp.sin(phase)


def forward_table():
    coarse = NT // 128
    bins = jnp.arange(NF, dtype=jnp.int32)[None, :]
    cos_a, sin_a = unit_angles(jnp.arange(coarse, dtype=jnp.int32)[:, None] * bins, coarse)
    cos_c, sin_c = unit_angles(jnp.arange(128, dtype=jnp.int32)[:, None] * bins, NT)
    cos_t = cos_a[:, None, :] * cos_c[None] - sin_a[:, None, :] * sin_c[None]
    sin_t = sin_a[:, None, :] * cos_c[None] + cos_a[:, None, :] * sin_c[None]
    table = jnp.concatenate([cos_t, -sin_t], axis=-1).astype(jnp.bfloat16)
    return table.reshape(NT, 2 * NF)


def inverse_factors():
    coarse = NT // 128
    groups = LAGS // 128
    bins = jnp.arange(NF, dtype=jnp.int32)[:, None]
    cos_a, sin_a = unit_angles(bins * (jnp.arange(groups, dtype=jnp.int32)[None, :] - groups // 2), coarse)
    cos_c, sin_c = unit_angles(bins * jnp.arange(128, dtype=jnp.int32)[None, :], NT)
    weight = jnp.where(bins == 0, 1.0, 2.0).astype(jnp.float32)
    return weight * cos_a, weight * sin_a, cos_c, sin_c


def whiten(spectrum):
    power = jnp.mean(spectrum * spectrum, axis=-1, keepdims=True)
    return (spectrum / jnp.sqrt(power + epsilon)).astype(jnp.bfloat16)


def cross_spectrum(source_row, receivers):
    half_width = receivers.shape[-1] // 2
    source_vals = source_row.astype(jnp.float32)
    receiver_vals = receivers.astype(jnp.float32)
    src_re = source_vals[..., :half_width]
    src_im = source_vals[..., half_width:]
    rec_re = receiver_vals[..., :half_width]
    rec_im = receiver_vals[..., half_width:]
    real_part = src_re * rec_re + src_im * rec_im
    imag_part = src_re * rec_im - src_im * rec_re
    return jnp.concatenate([real_part, imag_part], axis=-1).astype(jnp.bfloat16)


PAIR_BLOCK = 512


def coherence_kernel(
    own_ref, stretch_ref, crossed_ref, wcos_ref, wsin_ref, fcos_ref, fsin_ref,
    out_ref,
):
    minutes = crossed_ref.shape[0]
    moves = stretch_ref.shape[0] - 1
    groups = wcos_ref.shape[1]
    fine = fcos_ref.shape[1]

    fine_cos = fcos_ref[...]
    fine_sin = fsin_ref[...]
    pieces = [[] for _ in range(minutes)]
    for pair_group in range(groups // 2):
        columns = []
        for group in (2 * pair_group, 2 * pair_group + 1):
            coarse_cos = wcos_ref[:, group:group + 1]
            coarse_sin = wsin_ref[:, group:group + 1]
            columns.append(
                jnp.concatenate(
                    [
                        coarse_cos * fine_cos - coarse_sin * fine_sin,
                        -(coarse_sin * fine_cos + coarse_cos * fine_sin),
                    ],
                    axis=0,
                ).astype(jnp.bfloat16)
            )
        inverse = jnp.concatenate(columns, axis=1)
        for minute in range(minutes):
            pieces[minute].append(
                jnp.dot(crossed_ref[minute], inverse, preferred_element_type=jnp.float32)
            )
    stacked = None
    current = None
    for minute in range(minutes):
        correlation = jnp.concatenate(pieces[minute], axis=1)
        if stacked is None:
            stacked, current = correlation, correlation
        else:
            stacked = stacked + correlation
    high = stacked.astype(jnp.bfloat16)
    low = (stacked - high.astype(jnp.float32)).astype(jnp.bfloat16)
    rows = stacked.shape[0]
    parts = jnp.concatenate([high, low], axis=0)
    lag_rows = lax.broadcasted_iota(jnp.int32, (LAGS, LAGS), 0)
    moved = []
    for move in range(moves):
        picks = (lag_rows == stretch_ref[move + 1:move + 2, :]).astype(jnp.bfloat16)
        product = jnp.dot(parts, picks, preferred_element_type=jnp.float32)
        moved.append(product[:rows] + product[rows:])
    scale = 1.0 / LAGS
    current_power = jnp.sum(current * current, axis=1, keepdims=True) * scale
    lanes = lax.broadcasted_iota(jnp.int32, out_ref.shape, 1)
    result = jnp.zeros(out_ref.shape, jnp.float32)
    for stretch in range(moves + 1):
        if stretch == 0:
            shifted = stacked
        else:
            shifted = moved[stretch - 1]
        numerator = jnp.sum(current * shifted, axis=1, keepdims=True) * scale
        shifted_power = jnp.sum(shifted * shifted, axis=1, keepdims=True) * scale
        value = numerator / jnp.sqrt((current_power + epsilon) * (shifted_power + epsilon))
        result = jnp.where(lanes == stretch, value, result)
    out_ref[...] = result


def coherence(own_minute, stretch_index, crossed, factors):
    minutes, pair_count, width = crossed.shape
    stretch_count = stretch_index.shape[0]
    own = jnp.reshape(own_minute, (1,)).astype(jnp.int32)
    block = min(PAIR_BLOCK, pair_count)
    out = pl.pallas_call(
        coherence_kernel,
        grid_spec=pltpu.PrefetchScalarGridSpec(
            num_scalar_prefetch=1,
            grid=(pair_count // block,),
            in_specs=[
                pl.BlockSpec(stretch_index.shape, lambda i, own: (0, 0)),
                pl.BlockSpec((minutes, block, width), lambda i, own: (0, i, 0)),
            ] + [pl.BlockSpec(factor.shape, lambda i, own: (0, 0)) for factor in factors],
            out_specs=pl.BlockSpec((block, stretch_count), lambda i, own: (i, 0)),
        ),
        out_shape=jax.ShapeDtypeStruct((pair_count, stretch_count), jnp.float32),
        compiler_params=pltpu.CompilerParams(
            dimension_semantics=("arbitrary",), vmem_limit_bytes=48 << 20
        ),
    )(own, stretch_index, crossed, *factors)
    return out.T


def body(axis_order, record, pairs, stretch_index):
    block_rows = record.shape[1]
    minutes = lax.axis_size("tm")
    blocks = lax.axis_size("chan")
    def linear(t, b):
        return t * blocks + b if axis_order[0] == "tm" else b * minutes + t

    parts = []
    for shift in range(minutes):
        if shift == 0:
            own = record
        else:
            own = lax.ppermute(record, "tm", [(i, (i + shift) % minutes) for i in range(minutes)])
        route = [
            (linear(t, b), linear((t + shift) % minutes, blocks - 1 - b))
            for t in range(minutes)
            for b in range(blocks)
        ]
        mirrored = lax.ppermute(record, axis_order, route)
        parts.append(jnp.concatenate([own, mirrored], axis=1))
    bundle = jnp.concatenate(parts, axis=0)
    from_below = lax.ppermute(bundle, "chan", [(s, s + 1) for s in range(blocks - 1)])
    from_above = lax.ppermute(bundle, "chan", [(s, s - 1) for s in range(1, blocks)])
    forward = forward_table()

    def spectra(rows):
        count = rows.shape[1]
        spectrum = jnp.dot(
            rows.reshape(minutes * count, NT), forward, preferred_element_type=jnp.float32
        )
        return whiten(spectrum).reshape(minutes, count, 2 * NF)

    local = spectra(bundle)
    below_rows = spectra(from_below)
    above_rows = spectra(from_above)
    whitened = jnp.concatenate(
        [
            below_rows[:, :block_rows],
            local[:, :block_rows],
            above_rows[:, :block_rows],
            above_rows[:, block_rows:],
            local[:, block_rows:],
            below_rows[:, block_rows:],
        ],
        axis=1,
    )
    slot_rows = whitened.shape[1]

    position = lax.axis_index("chan")
    column_index = jnp.arange(pairs.shape[1], dtype=jnp.int32)[None, :]
    is_near = column_index < pairs.shape[1] // 2
    near_slot = pairs - (position - 1) * block_rows
    far_slot = pairs - (blocks - 2 - position) * block_rows + 3 * block_rows
    slot_index = jnp.where(is_near, near_slot, far_slot)
    source_count, recv_count = slot_index.shape
    pair_count = source_count * recv_count
    sources = whitened[:, block_rows:2 * block_rows:8]
    selector = (
        slot_index.reshape(pair_count, 1) == jnp.arange(slot_rows, dtype=jnp.int32)[None, :]
    ).astype(jnp.bfloat16)
    receivers = jnp.einsum(
        "pq,mqk->mpk", selector, whitened, preferred_element_type=jnp.float32
    )
    receivers = receivers.reshape(minutes, source_count, recv_count, 2 * NF)
    crossed = cross_spectrum(sources[:, :, None, :], receivers)
    crossed = crossed.reshape(minutes, pair_count, 2 * NF)
    result = coherence(0, stretch_index, crossed, inverse_factors())
    stretch_count = stretch_index.shape[0]
    return result.reshape(1, stretch_count, source_count, recv_count)


def solution(mesh):
    axis_order = tuple(name for name in mesh.axis_names if name in ("tm", "chan"))
    return jax.shard_map(
        functools.partial(body, axis_order),
        mesh=mesh,
        in_specs=(P("tm", "chan", None), P("chan", None), P()),
        out_specs=P("tm", None, "chan", None),
        check_vma=False,
    )
```

```python
import functools
import math

import jax
import jax.numpy as jnp
from jax import lax
from jax.experimental import pallas as pl
from jax.experimental.pallas import tpu as pltpu
from jax.sharding import PartitionSpec as P

NT = 1536
LAGS = 1024
NF = 768

epsilon = 1e-05


def unit_angles(numerators, period):
    phase = (numerators % period).astype(jnp.float32) * (2.0 * math.pi / period)
    return jnp.cos(phase), jnp.sin(phase)


def forward_table():
    coarse = NT // 128
    bins = jnp.arange(NF, dtype=jnp.int32)[None, :]
    cos_a, sin_a = unit_angles(jnp.arange(coarse, dtype=jnp.int32)[:, None] * bins, coarse)
    cos_c, sin_c = unit_angles(jnp.arange(128, dtype=jnp.int32)[:, None] * bins, NT)
    cos_t = cos_a[:, None, :] * cos_c[None] - sin_a[:, None, :] * sin_c[None]
    sin_t = sin_a[:, None, :] * cos_c[None] + cos_a[:, None, :] * sin_c[None]
    table = jnp.concatenate([cos_t, -sin_t], axis=-1).astype(jnp.bfloat16)
    return table.reshape(NT, 2 * NF)


def inverse_factors():
    coarse = NT // 128
    groups = LAGS // 128
    bins = jnp.arange(NF, dtype=jnp.int32)[:, None]
    cos_a, sin_a = unit_angles(bins * (jnp.arange(groups, dtype=jnp.int32)[None, :] - groups // 2), coarse)
    cos_c, sin_c = unit_angles(bins * jnp.arange(128, dtype=jnp.int32)[None, :], NT)
    weight = jnp.where(bins == 0, 1.0, 2.0).astype(jnp.float32)
    return weight * cos_a, weight * sin_a, cos_c, sin_c


def whiten(spectrum):
    power = jnp.mean(spectrum * spectrum, axis=-1, keepdims=True)
    return (spectrum / jnp.sqrt(power + epsilon)).astype(jnp.bfloat16)


def cross_spectrum(source_row, receivers):
    half_width = receivers.shape[-1] // 2
    source_vals = source_row.astype(jnp.float32)
    receiver_vals = receivers.astype(jnp.float32)
    src_re = source_vals[..., :half_width]
    src_im = source_vals[..., half_width:]
    rec_re = receiver_vals[..., :half_width]
    rec_im = receiver_vals[..., half_width:]
    real_part = src_re * rec_re + src_im * rec_im
    imag_part = src_re * rec_im - src_im * rec_re
    return jnp.concatenate([real_part, imag_part], axis=-1).astype(jnp.bfloat16)


PAIR_BLOCK = 512


def coherence_kernel(
    own_ref, stretch_ref, crossed_ref, wcos_ref, wsin_ref, fcos_ref, fsin_ref,
    out_ref,
):
    minutes = crossed_ref.shape[0]
    moves = stretch_ref.shape[0] - 1
    groups = wcos_ref.shape[1]
    fine = fcos_ref.shape[1]

    fine_cos = fcos_ref[...]
    fine_sin = fsin_ref[...]
    pieces = [[] for _ in range(minutes)]
    for pair_group in range(groups // 2):
        columns = []
        for group in (2 * pair_group, 2 * pair_group + 1):
            coarse_cos = wcos_ref[:, group:group + 1]
            coarse_sin = wsin_ref[:, group:group + 1]
            columns.append(
                jnp.concatenate(
                    [
                        coarse_cos * fine_cos - coarse_sin * fine_sin,
                        -(coarse_sin * fine_cos + coarse_cos * fine_sin),
                    ],
                    axis=0,
                ).astype(jnp.bfloat16)
            )
        inverse = jnp.concatenate(columns, axis=1)
        for minute in range(minutes):
            pieces[minute].append(
                jnp.dot(crossed_ref[minute], inverse, preferred_element_type=jnp.float32)
            )
    stacked = None
    current = None
    for minute in range(minutes):
        correlation = jnp.concatenate(pieces[minute], axis=1)
        if stacked is None:
            stacked, current = correlation, correlation
        else:
            stacked = stacked + correlation
    high = stacked.astype(jnp.bfloat16)
    low = (stacked - high.astype(jnp.float32)).astype(jnp.bfloat16)
    rows = stacked.shape[0]
    parts = jnp.concatenate([high, low], axis=0)
    lag_rows = lax.broadcasted_iota(jnp.int32, (LAGS, LAGS), 0)
    moved = []
    for move in range(moves):
        picks = (lag_rows == stretch_ref[move + 1:move + 2, :]).astype(jnp.bfloat16)
        product = jnp.dot(parts, picks, preferred_element_type=jnp.float32)
        moved.append(product[:rows] + product[rows:])
    scale = 1.0 / LAGS
    current_power = jnp.sum(current * current, axis=1, keepdims=True) * scale
    slab = (rows, 128)
    lanes = lax.broadcasted_iota(jnp.int32, slab, 1)
    result = jnp.zeros(slab, jnp.float32)
    for stretch in range(moves + 1):
        if stretch == 0:
            shifted = stacked
        else:
            shifted = moved[stretch - 1]
        numerator = jnp.sum(current * shifted, axis=1, keepdims=True) * scale
        shifted_power = jnp.sum(shifted * shifted, axis=1, keepdims=True) * scale
        value = numerator / jnp.sqrt((current_power + epsilon) * (shifted_power + epsilon))
        result = jnp.where(lanes == stretch, value, result)
    out_ref[...] = result.T[:out_ref.shape[0]]


def coherence(own_minute, stretch_index, crossed, factors):
    minutes, pair_count, width = crossed.shape
    stretch_count = stretch_index.shape[0]
    own = jnp.reshape(own_minute, (1,)).astype(jnp.int32)
    block = min(PAIR_BLOCK, pair_count)
    out = pl.pallas_call(
        coherence_kernel,
        grid_spec=pltpu.PrefetchScalarGridSpec(
            num_scalar_prefetch=1,
            grid=(pair_count // block,),
            in_specs=[
                pl.BlockSpec(stretch_index.shape, lambda i, own: (0, 0)),
                pl.BlockSpec((minutes, block, width), lambda i, own: (0, i, 0)),
            ] + [pl.BlockSpec(factor.shape, lambda i, own: (0, 0)) for factor in factors],
            out_specs=pl.BlockSpec((stretch_count, block), lambda i, own: (0, i)),
        ),
        out_shape=jax.ShapeDtypeStruct((stretch_count, pair_count), jnp.float32),
        compiler_params=pltpu.CompilerParams(
            dimension_semantics=("arbitrary",), vmem_limit_bytes=48 << 20
        ),
    )(own, stretch_index, crossed, *factors)
    return out


def body(axis_order, record, pairs, stretch_index):
    block_rows = record.shape[1]
    minutes = lax.axis_size("tm")
    blocks = lax.axis_size("chan")
    def linear(t, b):
        return t * blocks + b if axis_order[0] == "tm" else b * minutes + t

    parts = []
    for shift in range(minutes):
        if shift == 0:
            own = record
        else:
            own = lax.ppermute(record, "tm", [(i, (i + shift) % minutes) for i in range(minutes)])
        route = [
            (linear(t, b), linear((t + shift) % minutes, blocks - 1 - b))
            for t in range(minutes)
            for b in range(blocks)
        ]
        mirrored = lax.ppermute(record, axis_order, route)
        parts.append(jnp.concatenate([own, mirrored], axis=1))
    bundle = jnp.concatenate(parts, axis=0)
    from_below = lax.ppermute(bundle, "chan", [(s, s + 1) for s in range(blocks - 1)])
    from_above = lax.ppermute(bundle, "chan", [(s, s - 1) for s in range(1, blocks)])
    forward = forward_table()

    def spectra(rows):
        count = rows.shape[1]
        spectrum = jnp.dot(
            rows.reshape(minutes * count, NT), forward, preferred_element_type=jnp.float32
        )
        return whiten(spectrum).reshape(minutes, count, 2 * NF)

    local = spectra(bundle)
    below_rows = spectra(from_below)
    above_rows = spectra(from_above)
    whitened = jnp.concatenate(
        [
            below_rows[:, :block_rows],
            local[:, :block_rows],
            above_rows[:, :block_rows],
            above_rows[:, block_rows:],
            local[:, block_rows:],
            below_rows[:, block_rows:],
        ],
        axis=1,
    )
    slot_rows = whitened.shape[1]

    position = lax.axis_index("chan")
    column_index = jnp.arange(pairs.shape[1], dtype=jnp.int32)[None, :]
    is_near = column_index < pairs.shape[1] // 2
    near_slot = pairs - (position - 1) * block_rows
    far_slot = pairs - (blocks - 2 - position) * block_rows + 3 * block_rows
    slot_index = jnp.where(is_near, near_slot, far_slot)
    source_count, recv_count = slot_index.shape
    pair_count = source_count * recv_count
    sources = whitened[:, block_rows:2 * block_rows:8]
    selector = (
        slot_index.reshape(pair_count, 1) == jnp.arange(slot_rows, dtype=jnp.int32)[None, :]
    ).astype(jnp.bfloat16)
    receivers = jnp.einsum(
        "pq,mqk->mpk", selector, whitened, preferred_element_type=jnp.float32
    )
    receivers = receivers.reshape(minutes, source_count, recv_count, 2 * NF)
    crossed = cross_spectrum(sources[:, :, None, :], receivers)
    crossed = crossed.reshape(minutes, pair_count, 2 * NF)
    result = coherence(0, stretch_index, crossed, inverse_factors())
    stretch_count = stretch_index.shape[0]
    return result.reshape(1, stretch_count, source_count, recv_count)


def solution(mesh):
    axis_order = tuple(name for name in mesh.axis_names if name in ("tm", "chan"))
    return jax.shard_map(
        functools.partial(body, axis_order),
        mesh=mesh,
        in_specs=(P("tm", "chan", None), P("chan", None), P()),
        out_specs=P("tm", None, "chan", None),
        check_vma=False,
    )
```
